32 devices in a mesh: clip: 2 (over y), strip: 4 (over z), tm: 4 (over x, core).
Axes of the slice: x: 2, y: 2, z: 4, core: 2. Of those that a mesh axis runs over, the one named last changes fastest.
Arguments:
- frames: bfloat16 [8, 12, 160, 384], P(('clip', 'tm'), 'strip'), parts along dimension 0, may hold values from -6 to 6
- cache_frames: bfloat16 [4, 12, 160, 384], P('clip', 'strip'), parts along dimension 0, may hold values from -6 to 6
- attn_gain: float32 [384], replicated, may hold values from 0.1 to 1.9
- query_weight: bfloat16 [384, 384], replicated, may hold values from -4 to 4
- key_weight: bfloat16 [384, 384], replicated, may hold values from -2 to 2
- value_weight: bfloat16 [384, 384], replicated, may hold values from -0.3125 to 0.3125
- out_weight: bfloat16 [384, 384], replicated, may hold values from -0.3125 to 0.3125
- conv_gain: float32 [384], replicated, may hold values from 0.1 to 1.9
- conv_weight: bfloat16 [3, 3, 3, 384, 384], replicated, may hold values from -0.0625 to 0.0625
Outputs:
- decoded: bfloat16 [8, 12, 160, 384], P(('clip', 'tm'), 'strip'), parts along dimension 0
The draws below stay inside these ranges and needn't reach their ends.
There are 2 independent parts, one for each index of `clip`. The reference program is written for one: setup_inputs(seed, part) draws one part's arguments, and reference() takes and returns one part's arrays. A program takes and returns all parts, laid end to end along the dimension named above; an argument that names none is the same for every part. Nothing has to cross between parts.
All inputs are finite; a program needn't handle non-finite values.
Results may differ from the reference program's by a relative error of at most 0.009.
Values may be sent and summed in bfloat16 or wider, within the bound.
No kernel may reach another device: no remote copies, remote signals or barrier semaphores. Data moves between devices by JAX's collectives and lax.ppermute only.
A program may use at most 128 MiB of HBM per device.

```python
import jax
import jax.numpy as jnp
from jax import lax

D = 384
COLS = 160
ROWS = 12
FRAMES = 4


def drawn_matrix(key, spread):
    noise = jax.random.truncated_normal(key, -6.0, 6.0, (D, D)) * (spread / jnp.sqrt(jnp.float32(D)))
    return noise.astype(jnp.bfloat16)


def draw_query_weight(key, part):
    return drawn_matrix(jax.random.fold_in(key, 11), 3.0)


def draw_key_weight(key, part):
    return drawn_matrix(jax.random.fold_in(key, 12), 1.0)


def draw_frames(key, part):
    shape = (FRAMES, ROWS, COLS, D)
    first = jax.random.fold_in(jax.random.fold_in(key, 13), 0)
    values = jax.random.truncated_normal(first, -6.0, 6.0, shape)
    return values.astype(jnp.bfloat16)


def block_levels(rng, extent, shards, smallest, largest):
    factor_of, own = 1.0, jax.random.fold_in(rng, 6)
    for position, parts in shards:
        draws = jnp.exp(jax.random.uniform(jax.random.fold_in(own, position), (parts,), jnp.float32, smallest / len(shards), largest / len(shards)))
        factor_of = factor_of * jnp.repeat(draws, extent[position] // parts).reshape([-1 if axis == position else 1 for axis in range(len(extent))])
    return factor_of


def gaussian(key, shape, scale, reach, cuts=(), kind=jnp.bfloat16):
    values = scale * jax.random.normal(key, shape, jnp.float32)
    if cuts:
        values = values * block_levels(key, shape, cuts, -0.22, 0.18)
    return jnp.clip(values, -reach, reach).astype(kind)


def setup_inputs(seed: int = 0, part: int = 0) -> dict:
    arg_keys = jax.random.split(jax.random.key(seed), 10)
    own_keys = jax.random.split(jax.random.fold_in(arg_keys[9], part), 10)
    return {
        "frames": draw_frames(jax.random.fold_in(jax.random.fold_in(arg_keys[9], part), 71), part),
        "cache_frames": gaussian(own_keys[1], (2, ROWS, COLS, D), 1.0, 6.0, ((1, 4),)),
        "attn_gain": jnp.clip(1.0 + 0.18 * jax.random.normal(arg_keys[2], (D,), jnp.float32), 0.1, 1.9),
        "query_weight": draw_query_weight(jax.random.fold_in(arg_keys[9], 71), part),
        "key_weight": draw_key_weight(jax.random.fold_in(arg_keys[9], 71), part),
        "value_weight": gaussian(arg_keys[5], (D, D), D ** -0.5, 0.3125),
        "out_weight": gaussian(arg_keys[6], (D, D), D ** -0.5, 0.3125),
        "conv_gain": jnp.clip(1.0 + 0.18 * jax.random.normal(arg_keys[7], (D,), jnp.float32), 0.1, 1.9),
        "conv_weight": gaussian(arg_keys[8], (3, 3, 3, D, D), (27 * D) ** -0.5, 0.0625),
    }


def rms_scale(values, gain):
    wide = values.astype(jnp.float32)
    return wide * lax.rsqrt(lax.optimization_barrier(jnp.mean(wide * wide, axis=-1, keepdims=True)) + 1e-06) * gain

def one_frame(frame, attn_gain, query_weight, key_weight, value_weight, out_weight):
    width = frame.shape[-1]
    flat = frame.reshape(-1, width)
    normed = rms_scale(flat, attn_gain).astype(jnp.bfloat16)
    query = jnp.dot(normed, query_weight, preferred_element_type=jnp.float32).astype(jnp.bfloat16)
    keys = jnp.dot(normed, key_weight, preferred_element_type=jnp.float32).astype(jnp.bfloat16)
    values = jnp.dot(normed, value_weight, preferred_element_type=jnp.float32).astype(jnp.bfloat16)
    scores = jnp.dot(query, keys.T, preferred_element_type=jnp.float32) / jnp.sqrt(jnp.float32(width))
    peak = lax.optimization_barrier(jnp.max(scores, axis=1, keepdims=True))
    weights = jnp.exp(scores - peak)
    total = lax.optimization_barrier(jnp.sum(weights, axis=1, keepdims=True))
    attended = (jnp.dot(weights.astype(jnp.bfloat16), values, preferred_element_type=jnp.float32) / total).astype(jnp.bfloat16)
    resid = flat.astype(jnp.float32) + jnp.dot(attended, out_weight, preferred_element_type=jnp.float32)
    return resid.astype(jnp.bfloat16).reshape(frame.shape)

def reference(frames, cache_frames, attn_gain, query_weight, key_weight, value_weight, out_weight, conv_gain, conv_weight):
    resid = lax.map(lambda frame: one_frame(frame, attn_gain, query_weight, key_weight, value_weight, out_weight), frames)
    act = jax.nn.silu(rms_scale(resid, conv_gain)).astype(jnp.bfloat16)
    extended = jnp.concatenate([cache_frames, act], axis=0)
    conv = lax.conv_general_dilated(extended.astype(jnp.float32)[None], conv_weight.astype(jnp.float32), (1, 1, 1), ((0, 0), (1, 1), (1, 1)), dimension_numbers=('NDHWC', 'DHWIO', 'NDHWC'), precision=lax.Precision.HIGHEST)[0]
    return (resid.astype(jnp.float32) + conv).astype(jnp.bfloat16)
```

```python
import jax
import jax.numpy as jnp
from jax import lax
from jax.sharding import PartitionSpec as P


def passed_along(x, axis, by):
    size = lax.axis_size(axis)
    pairs = [(i, i + by) for i in range(size) if 0 <= i + by < size]
    return lax.ppermute(x, axis, pairs)


def with_halo(x, sides, width):
    for axis, dim in sides:
        size, length = (lax.axis_size(axis), x.shape[dim])
        up = [(i, (i + 1) % size) for i in range(size - 1)]
        down = [(j, i) for i, j in up]
        last = lax.slice_in_dim(x, length - width, length, axis=dim)
        leading = lax.slice_in_dim(x, 0, width, axis=dim)
        before = lax.ppermute(last, axis, up)
        after = lax.ppermute(leading, axis, down)
        x = jnp.concatenate([before, x, after], axis=dim)
    return x


def strip_gather(x, axis):
    n = lax.axis_size(axis)
    if n == 1:
        return x
    m = x.shape[0]
    up_pairs = [(i, i + 1) for i in range(n - 1)]
    down_pairs = [(i + 1, i) for i in range(n - 1)]
    ups, downs = [], []
    up, down = x, x
    for _ in range(n - 1):
        up = lax.ppermute(up, axis, up_pairs)
        down = lax.ppermute(down, axis, down_pairs)
        ups.append(up)
        downs.append(down)
    stacked = jnp.concatenate(ups[::-1] + [x] + downs, axis=0)
    me = lax.axis_index(axis)
    return lax.dynamic_slice_in_dim(stacked, (n - 1 - me) * m, n * m, axis=0)


def rms_scale(values, gain):
    wide = values.astype(jnp.float32)
    return wide * lax.rsqrt(jnp.mean(wide * wide, axis=-1, keepdims=True) + 1e-06) * gain


def attend(carry, query, keys, values, scale):
    peak, total, summed = carry
    scores = (
        lax.dot_general(query, keys, (((1,), (1,)), ((), ())), preferred_element_type=jnp.float32)
        * scale
    )
    fresh = jnp.maximum(peak, jnp.max(scores, axis=1))
    weights = jnp.exp(scores - fresh[:, None])
    total = jnp.sum(weights, axis=1)
    summed = jnp.dot(weights.astype(jnp.bfloat16), values, preferred_element_type=jnp.float32)
    return (fresh, total, summed)


def shards(
    frames,
    cache_frames,
    attn_gain,
    query_weight,
    key_weight,
    value_weight,
    out_weight,
    conv_gain,
    conv_weight,
):
    rows = frames.shape[1]
    cols = frames.shape[2]
    width = frames.shape[3]
    flat = frames.reshape(-1, width)
    count = flat.shape[0]
    scale = 1.0 / jnp.sqrt(jnp.float32(width))
    whole = strip_gather(flat, "strip")
    normed = rms_scale(flat, attn_gain).astype(jnp.bfloat16)
    normed_all = rms_scale(whole, attn_gain).astype(jnp.bfloat16)
    query = jnp.dot(normed, query_weight, preferred_element_type=jnp.float32).astype(jnp.bfloat16)
    start_carry = (
        jnp.full((count,), -1e30, jnp.float32),
        jnp.zeros((count,), jnp.float32),
        jnp.zeros((count, width), jnp.float32),
    )
    keys = jnp.dot(normed_all, key_weight, preferred_element_type=jnp.float32).astype(jnp.bfloat16)
    values = jnp.dot(normed_all, value_weight, preferred_element_type=jnp.float32).astype(jnp.bfloat16)
    peak, total, summed = attend(
        start_carry,
        query,
        keys,
        values,
        scale,
    )
    attended = (summed / total[:, None]).astype(jnp.bfloat16)
    resid = (
        flat.astype(jnp.float32) + jnp.dot(attended, out_weight, preferred_element_type=jnp.float32)
    ).astype(jnp.bfloat16)
    act = jax.nn.silu(rms_scale(resid, conv_gain)).astype(jnp.bfloat16).reshape(rows, cols, width)
    frame_index = lax.axis_index("tm")
    prior = passed_along(act, "tm", 1)
    prior = jnp.where(frame_index == 0, cache_frames[1], prior)
    older = passed_along(prior, "tm", 1)
    older = jnp.where(frame_index == 0, cache_frames[0], older)
    stacked = jnp.stack([older, prior, act])
    padded = with_halo(stacked, (("strip", 1),), 1)
    padded = jnp.pad(padded, ((0, 0), (0, 0), (1, 1), (0, 0)))
    widened = jnp.concatenate(
        [padded[:, :, 0:cols], padded[:, :, 1 : cols + 1], padded[:, :, 2 : cols + 2]], axis=-1
    )
    kernel = conv_weight.reshape(3, 3, 3 * width, width)
    result = resid.astype(jnp.float32)
    for step_t in range(3):
        for step_r in range(3):
            window = widened[step_t, step_r : step_r + rows].reshape(-1, 3 * width)
            result = result + jnp.dot(
                window, kernel[step_t, step_r], preferred_element_type=jnp.float32
            )
    return result.astype(jnp.bfloat16).reshape(1, rows, cols, width)


def solution(mesh):
    return jax.shard_map(
        shards,
        mesh=mesh,
        in_specs=(
            P(("clip", "tm"), "strip", None, None),
            P("clip", "strip", None, None),
            P(),
            P(),
            P(),
            P(),
            P(),
            P(),
            P(),
        ),
        out_specs=P(("clip", "tm"), "strip", None, None),
        check_vma=False,
    )
```

```python
import jax
import jax.numpy as jnp
from jax import lax
from jax.sharding import PartitionSpec as P


def relay_blocks(x, axis):
    n = lax.axis_size(axis)
    up_pairs = [(i, i + 1) for i in range(n - 1)]
    down_pairs = [(i + 1, i) for i in range(n - 1)]
    ups, downs = [], []
    up, down = x, x
    for _ in range(n - 1):
        up = lax.ppermute(up, axis, up_pairs)
        down = lax.ppermute(down, axis, down_pairs)
        ups.append(up)
        downs.append(down)
    return ups, downs


def with_halo(x, axis, dim):
    size, length = (lax.axis_size(axis), x.shape[dim])
    up = [(i, i + 1) for i in range(size - 1)]
    down = [(j, i) for i, j in up]
    last = lax.slice_in_dim(x, length - 1, length, axis=dim)
    leading = lax.slice_in_dim(x, 0, 1, axis=dim)
    before = lax.ppermute(last, axis, up)
    after = lax.ppermute(leading, axis, down)
    return jnp.concatenate([before, x, after], axis=dim)


def rms_scale(values, gain):
    wide = values.astype(jnp.float32)
    return wide * lax.rsqrt(jnp.mean(wide * wide, axis=-1, keepdims=True) + 1e-06) * gain


def frame_conv(padded, kernel, rows, cols, width):
    padded = jnp.pad(padded, ((0, 0), (1, 1), (0, 0)))
    widened = jnp.concatenate(
        [padded[:, 0:cols], padded[:, 1 : cols + 1], padded[:, 2 : cols + 2]], axis=-1
    )
    total = None
    for step_r in range(3):
        window = widened[step_r : step_r + rows].reshape(-1, 3 * width)
        part = jnp.dot(window, kernel[step_r], preferred_element_type=jnp.float32)
        total = part if total is None else total + part
    return total


def shards(
    frames,
    cache_frames,
    attn_gain,
    query_weight,
    key_weight,
    value_weight,
    out_weight,
    conv_gain,
    conv_weight,
):
    rows = frames.shape[1]
    cols = frames.shape[2]
    width = frames.shape[3]
    flat = frames.reshape(-1, width)
    count = flat.shape[0]
    scale = 1.0 / jnp.sqrt(jnp.float32(width))
    normed = rms_scale(flat, attn_gain).astype(jnp.bfloat16)
    query = jnp.dot(normed, query_weight, preferred_element_type=jnp.float32).astype(jnp.bfloat16)

    def block_parts(block):
        block_normed = rms_scale(block, attn_gain).astype(jnp.bfloat16)
        keys = jnp.dot(block_normed, key_weight, preferred_element_type=jnp.float32).astype(
            jnp.bfloat16
        )
        values = jnp.dot(block_normed, value_weight, preferred_element_type=jnp.float32).astype(
            jnp.bfloat16
        )
        scores_t = (
            lax.dot_general(keys, query, (((1,), (1,)), ((), ())), preferred_element_type=jnp.float32)
            * scale
        )
        return scores_t, values

    n = lax.axis_size("strip")
    ups, downs = relay_blocks(flat, "strip")
    parts = [block_parts(b) for b in ups[::-1] + [flat] + downs]
    scores_all = jnp.concatenate([p[0] for p in parts], axis=0)
    values_all = jnp.concatenate([p[1] for p in parts], axis=0)
    me = lax.axis_index("strip")
    start = (n - 1 - me) * count
    scores_t = lax.dynamic_slice_in_dim(scores_all, start, n * count, axis=0)
    values = lax.dynamic_slice_in_dim(values_all, start, n * count, axis=0)
    peak = jnp.max(scores_t, axis=0)
    weights = jnp.exp(scores_t - peak[None, :])
    total = jnp.sum(weights, axis=0)
    summed = lax.dot_general(
        weights.astype(jnp.bfloat16), values, (((0,), (0,)), ((), ())),
        preferred_element_type=jnp.float32,
    )
    attended = (summed / total[:, None]).astype(jnp.bfloat16)
    resid = (
        flat.astype(jnp.float32) + jnp.dot(attended, out_weight, preferred_element_type=jnp.float32)
    ).astype(jnp.bfloat16)
    act = jax.nn.silu(rms_scale(resid, conv_gain)).astype(jnp.bfloat16).reshape(rows, cols, width)

    cache = lax.optimization_barrier((cache_frames, scores_all))[0]
    cache_padded = with_halo(cache, "strip", 1)
    act_padded = with_halo(act, "strip", 0)

    kernel = conv_weight.reshape(3, 3, 3 * width, width)
    result = resid.astype(jnp.float32) + frame_conv(act_padded, kernel[2], rows, cols, width)

    nt = lax.axis_size("tm")
    frame_index = lax.axis_index("tm")
    prior = lax.ppermute(act_padded, "tm", [(i, i + 1) for i in range(nt - 1)])
    older_even = lax.ppermute(act_padded, "tm", [(i, i + 2) for i in range(0, nt - 2, 2)])
    older_odd = lax.ppermute(prior, "tm", [(i, i + 1) for i in range(2, nt - 1, 2)])
    prior = jnp.where(frame_index == 0, cache_padded[1], prior)
    result = result + frame_conv(prior, kernel[1], rows, cols, width)
    older = jnp.where(frame_index % 2 == 0, older_even, older_odd)
    older = jnp.where(frame_index == 0, cache_padded[0], older)
    older = jnp.where(frame_index == 1, cache_padded[1], older)
    result = result + frame_conv(older, kernel[0], rows, cols, width)
    return result.astype(jnp.bfloat16).reshape(1, rows, cols, width)


def solution(mesh):
    return jax.shard_map(
        shards,
        mesh=mesh,
        in_specs=(
            P(("clip", "tm"), "strip", None, None),
            P("clip", "strip", None, None),
            P(),
            P(),
            P(),
            P(),
            P(),
            P(),
            P(),
        ),
        out_specs=P(("clip", "tm"), "strip", None, None),
        check_vma=False,
    )
```

```python
import functools

import jax
import jax.numpy as jnp
import numpy as np
from jax import lax
from jax.experimental import pallas as pl
from jax.experimental.pallas import tpu as pltpu
from jax.sharding import PartitionSpec as P


def passed_along(x, axis, by):
    size = lax.axis_size(axis)
    pairs = [(i, i + by) for i in range(size) if 0 <= i + by < size]
    return lax.ppermute(x, axis, pairs)


def with_halo(x, sides, width):
    for axis, dim in sides:
        size, length = (lax.axis_size(axis), x.shape[dim])
        up = [(i, (i + 1) % size) for i in range(size - 1)]
        down = [(j, i) for i, j in up]
        last = lax.slice_in_dim(x, length - width, length, axis=dim)
        leading = lax.slice_in_dim(x, 0, width, axis=dim)
        before = lax.ppermute(last, axis, up)
        after = lax.ppermute(leading, axis, down)
        x = jnp.concatenate([before, x, after], axis=dim)
    return x


def strip_gather(x, axis):
    n = lax.axis_size(axis)
    if n == 1:
        return x
    m = x.shape[0]
    up_pairs = [(i, i + 1) for i in range(n - 1)]
    down_pairs = [(i + 1, i) for i in range(n - 1)]
    ups, downs = [], []
    up, down = x, x
    for _ in range(n - 1):
        up = lax.ppermute(up, axis, up_pairs)
        down = lax.ppermute(down, axis, down_pairs)
        ups.append(up)
        downs.append(down)
    stacked = jnp.concatenate(ups[::-1] + [x] + downs, axis=0)
    me = lax.axis_index(axis)
    return lax.dynamic_slice_in_dim(stacked, (n - 1 - me) * m, n * m, axis=0)


def rms_scale(values, gain):
    wide = values.astype(jnp.float32)
    return wide * lax.rsqrt(jnp.mean(wide * wide, axis=-1, keepdims=True) + 1e-06) * gain


def attention_kernel(scale, q_ref, k_ref, v_ref, o_ref):
    scores = (
        lax.dot_general(
            q_ref[...], k_ref[...], (((1,), (1,)), ((), ())), preferred_element_type=jnp.float32
        )
        * scale
    )
    peak = jnp.max(scores, axis=1, keepdims=True)
    weights = jnp.exp(scores - peak)
    total = jnp.sum(weights, axis=1, keepdims=True)
    summed = jnp.dot(weights.astype(jnp.bfloat16), v_ref[...], preferred_element_type=jnp.float32)
    o_ref[...] = (summed / total).astype(o_ref.dtype)


def attend(query, keys, values, scale):
    count, width = query.shape
    total_keys = keys.shape[0]
    block = 160 if count % 160 == 0 else count
    flops = 4 * count * total_keys * width
    return pl.pallas_call(
        functools.partial(attention_kernel, scale),
        out_shape=jax.ShapeDtypeStruct((count, width), jnp.bfloat16),
        grid=(count // block,),
        in_specs=[
            pl.BlockSpec((block, width), lambda i: (i, 0)),
            pl.BlockSpec((total_keys, width), lambda i: (0, 0)),
            pl.BlockSpec((total_keys, width), lambda i: (0, 0)),
        ],
        out_specs=pl.BlockSpec((block, width), lambda i: (i, 0)),
        compiler_params=pltpu.CompilerParams(vmem_limit_bytes=60 * 1024 * 1024),
        cost_estimate=pl.CostEstimate(
            flops=flops,
            transcendentals=count * total_keys,
            bytes_accessed=2 * width * (2 * count + 2 * total_keys),
        ),
    )(query, keys, values)


def shards(
    frames,
    cache_frames,
    attn_gain,
    query_weight,
    key_weight,
    value_weight,
    out_weight,
    conv_gain,
    conv_weight,
):
    rows = frames.shape[1]
    cols = frames.shape[2]
    width = frames.shape[3]
    flat = frames.reshape(-1, width)
    count = flat.shape[0]
    scale = float(np.float32(1.0) / np.sqrt(np.float32(width)))
    whole = strip_gather(flat, "strip")
    normed = rms_scale(flat, attn_gain).astype(jnp.bfloat16)
    normed_all = rms_scale(whole, attn_gain).astype(jnp.bfloat16)
    query = jnp.dot(normed, query_weight, preferred_element_type=jnp.float32).astype(jnp.bfloat16)
    keys = jnp.dot(normed_all, key_weight, preferred_element_type=jnp.float32).astype(jnp.bfloat16)
    values = jnp.dot(normed_all, value_weight, preferred_element_type=jnp.float32).astype(jnp.bfloat16)
    attended = attend(query, keys, values, scale)
    resid = (
        flat.astype(jnp.float32) + jnp.dot(attended, out_weight, preferred_element_type=jnp.float32)
    ).astype(jnp.bfloat16)
    act = jax.nn.silu(rms_scale(resid, conv_gain)).astype(jnp.bfloat16).reshape(rows, cols, width)
    frame_index = lax.axis_index("tm")
    prior = passed_along(act, "tm", 1)
    prior = jnp.where(frame_index == 0, cache_frames[1], prior)
    older = passed_along(prior, "tm", 1)
    older = jnp.where(frame_index == 0, cache_frames[0], older)
    stacked = jnp.stack([older, prior, act])
    padded = with_halo(stacked, (("strip", 1),), 1)
    padded = jnp.pad(padded, ((0, 0), (0, 0), (1, 1), (0, 0)))
    widened = jnp.concatenate(
        [padded[:, :, 0:cols], padded[:, :, 1 : cols + 1], padded[:, :, 2 : cols + 2]], axis=-1
    )
    kernel = conv_weight.reshape(3, 3, 3 * width, width)
    result = resid.astype(jnp.float32)
    for step_t in range(3):
        for step_r in range(3):
            window = widened[step_t, step_r : step_r + rows].reshape(-1, 3 * width)
            result = result + jnp.dot(
                window, kernel[step_t, step_r], preferred_element_type=jnp.float32
            )
    return result.astype(jnp.bfloat16).reshape(1, rows, cols, width)


def solution(mesh):
    return jax.shard_map(
        shards,
        mesh=mesh,
        in_specs=(
            P(("clip", "tm"), "strip", None, None),
            P("clip", "strip", None, None),
            P(),
            P(),
            P(),
            P(),
            P(),
            P(),
            P(),
        ),
        out_specs=P(("clip", "tm"), "strip", None, None),
        check_vma=False,
    )
```

```python
import functools

import jax
import jax.numpy as jnp
import numpy as np
from jax import lax
from jax.experimental import pallas as pl
from jax.experimental.pallas import tpu as pltpu
from jax.sharding import PartitionSpec as P


def passed_along(x, axis, by):
    size = lax.axis_size(axis)
    pairs = [(i, i + by) for i in range(size) if 0 <= i + by < size]
    return lax.ppermute(x, axis, pairs)


def with_halo(x, sides, width):
    for axis, dim in sides:
        size, length = (lax.axis_size(axis), x.shape[dim])
        up = [(i, (i + 1) % size) for i in range(size - 1)]
        down = [(j, i) for i, j in up]
        last = lax.slice_in_dim(x, length - width, length, axis=dim)
        leading = lax.slice_in_dim(x, 0, width, axis=dim)
        before = lax.ppermute(last, axis, up)
        after = lax.ppermute(leading, axis, down)
        x = jnp.concatenate([before, x, after], axis=dim)
    return x


def strip_gather(x, axis, chunks):
    n = lax.axis_size(axis)
    if n == 1:
        return x
    m = x.shape[0]
    up_pairs = [(i, i + 1) for i in range(n - 1)]
    down_pairs = [(i + 1, i) for i in range(n - 1)]
    size = m // chunks
    ups = [[] for _ in range(n - 1)]
    downs = [[] for _ in range(n - 1)]
    for c in range(chunks):
        piece = x[c * size : (c + 1) * size]
        up, down = piece, piece
        for k in range(n - 1):
            up = lax.ppermute(up, axis, up_pairs)
            down = lax.ppermute(down, axis, down_pairs)
            ups[k].append(up)
            downs[k].append(down)
    ups = [jnp.concatenate(p, axis=0) for p in ups]
    downs = [jnp.concatenate(p, axis=0) for p in downs]
    stacked = jnp.concatenate(ups[::-1] + [x] + downs, axis=0)
    me = lax.axis_index(axis)
    return lax.dynamic_slice_in_dim(stacked, (n - 1 - me) * m, n * m, axis=0)


def rms_scale(values, gain):
    wide = values.astype(jnp.float32)
    return wide * lax.rsqrt(jnp.mean(wide * wide, axis=-1, keepdims=True) + 1e-06) * gain


def attention_kernel(scale, q_ref, k_ref, v_ref, o_ref):
    scores = (
        lax.dot_general(
            q_ref[...], k_ref[...], (((1,), (1,)), ((), ())), preferred_element_type=jnp.float32
        )
        * scale
    )
    peak = jnp.max(scores, axis=1, keepdims=True)
    weights = jnp.exp(scores - peak)
    total = jnp.sum(weights, axis=1, keepdims=True)
    summed = jnp.dot(weights.astype(jnp.bfloat16), v_ref[...], preferred_element_type=jnp.float32)
    o_ref[...] = (summed / total).astype(o_ref.dtype)


def attend(query, keys, values, scale):
    count, width = query.shape
    total_keys = keys.shape[0]
    block = 160 if count % 160 == 0 else count
    flops = 4 * count * total_keys * width
    return pl.pallas_call(
        functools.partial(attention_kernel, scale),
        out_shape=jax.ShapeDtypeStruct((count, width), jnp.bfloat16),
        grid=(count // block,),
        in_specs=[
            pl.BlockSpec((block, width), lambda i: (i, 0)),
            pl.BlockSpec((total_keys, width), lambda i: (0, 0)),
            pl.BlockSpec((total_keys, width), lambda i: (0, 0)),
        ],
        out_specs=pl.BlockSpec((block, width), lambda i: (i, 0)),
        compiler_params=pltpu.CompilerParams(vmem_limit_bytes=60 * 1024 * 1024),
        cost_estimate=pl.CostEstimate(
            flops=flops,
            transcendentals=count * total_keys,
            bytes_accessed=2 * width * (2 * count + 2 * total_keys),
        ),
    )(query, keys, values)


def shards(
    frames,
    cache_frames,
    attn_gain,
    query_weight,
    key_weight,
    value_weight,
    out_weight,
    conv_gain,
    conv_weight,
):
    rows = frames.shape[1]
    cols = frames.shape[2]
    width = frames.shape[3]
    flat = frames.reshape(-1, width)
    count = flat.shape[0]
    scale = float(np.float32(1.0) / np.sqrt(np.float32(width)))
    whole = strip_gather(flat, "strip", 2 if count % 16 == 0 else 1)
    normed = rms_scale(flat, attn_gain).astype(jnp.bfloat16)
    normed_all = rms_scale(whole, attn_gain).astype(jnp.bfloat16)
    query = jnp.dot(normed, query_weight, preferred_element_type=jnp.float32).astype(jnp.bfloat16)
    keys = jnp.dot(normed_all, key_weight, preferred_element_type=jnp.float32).astype(jnp.bfloat16)
    values = jnp.dot(normed_all, value_weight, preferred_element_type=jnp.float32).astype(jnp.bfloat16)
    attended = attend(query, keys, values, scale)
    resid = (
        flat.astype(jnp.float32) + jnp.dot(attended, out_weight, preferred_element_type=jnp.float32)
    ).astype(jnp.bfloat16)
    act = jax.nn.silu(rms_scale(resid, conv_gain)).astype(jnp.bfloat16).reshape(rows, cols, width)
    frame_index = lax.axis_index("tm")
    prior = passed_along(act, "tm", 1)
    prior = jnp.where(frame_index == 0, cache_frames[1], prior)
    older = passed_along(prior, "tm", 1)
    older = jnp.where(frame_index == 0, cache_frames[0], older)
    stacked = jnp.stack([older, prior, act])
    padded = with_halo(stacked, (("strip", 1),), 1)
    padded = jnp.pad(padded, ((0, 0), (0, 0), (1, 1), (0, 0)))
    widened = jnp.concatenate(
        [padded[:, :, 0:cols], padded[:, :, 1 : cols + 1], padded[:, :, 2 : cols + 2]], axis=-1
    )
    kernel = conv_weight.reshape(3, 3, 3 * width, width)
    result = resid.astype(jnp.float32)
    for step_t in range(3):
        for step_r in range(3):
            window = widened[step_t, step_r : step_r + rows].reshape(-1, 3 * width)
            result = result + jnp.dot(
                window, kernel[step_t, step_r], preferred_element_type=jnp.float32
            )
    return result.astype(jnp.bfloat16).reshape(1, rows, cols, width)


def solution(mesh):
    return jax.shard_map(
        shards,
        mesh=mesh,
        in_specs=(
            P(("clip", "tm"), "strip", None, None),
            P("clip", "strip", None, None),
            P(),
            P(),
            P(),
            P(),
            P(),
            P(),
            P(),
        ),
        out_specs=P(("clip", "tm"), "strip", None, None),
        check_vma=False,
    )
```

```python
import functools

import jax
import jax.numpy as jnp
import numpy as np
from jax import lax
from jax.experimental import pallas as pl
from jax.experimental.pallas import tpu as pltpu
from jax.sharding import PartitionSpec as P


def with_halo(x, sides, width):
    for axis, dim in sides:
        size, length = (lax.axis_size(axis), x.shape[dim])
        up = [(i, (i + 1) % size) for i in range(size - 1)]
        down = [(j, i) for i, j in up]
        last = lax.slice_in_dim(x, length - width, length, axis=dim)
        leading = lax.slice_in_dim(x, 0, width, axis=dim)
        before = lax.ppermute(last, axis, up)
        after = lax.ppermute(leading, axis, down)
        x = jnp.concatenate([before, x, after], axis=dim)
    return x


def strip_gather(x, axis):
    n = lax.axis_size(axis)
    if n == 1:
        return x
    m = x.shape[0]
    up_pairs = [(i, i + 1) for i in range(n - 1)]
    down_pairs = [(i + 1, i) for i in range(n - 1)]
    ups, downs = [], []
    up, down = x, x
    for _ in range(n - 1):
        up = lax.ppermute(up, axis, up_pairs)
        down = lax.ppermute(down, axis, down_pairs)
        ups.append(up)
        downs.append(down)
    stacked = jnp.concatenate(ups[::-1] + [x] + downs, axis=0)
    me = lax.axis_index(axis)
    return lax.dynamic_slice_in_dim(stacked, (n - 1 - me) * m, n * m, axis=0)


def rms_scale(values, gain):
    wide = values.astype(jnp.float32)
    return wide * lax.rsqrt(jnp.mean(wide * wide, axis=-1, keepdims=True) + 1e-06) * gain


def attention_kernel(scale, q_ref, k_ref, v_ref, o_ref):
    scores = (
        lax.dot_general(
            q_ref[...], k_ref[...], (((1,), (1,)), ((), ())), preferred_element_type=jnp.float32
        )
        * scale
    )
    peak = jnp.max(scores, axis=1, keepdims=True)
    weights = jnp.exp(scores - peak)
    total = jnp.sum(weights, axis=1, keepdims=True)
    summed = jnp.dot(weights.astype(jnp.bfloat16), v_ref[...], preferred_element_type=jnp.float32)
    o_ref[...] = (summed / total).astype(o_ref.dtype)


def attend(query, keys, values, scale):
    count, width = query.shape
    total_keys = keys.shape[0]
    block = 160 if count % 160 == 0 else count
    flops = 4 * count * total_keys * width
    return pl.pallas_call(
        functools.partial(attention_kernel, scale),
        out_shape=jax.ShapeDtypeStruct((count, width), jnp.bfloat16),
        grid=(count // block,),
        in_specs=[
            pl.BlockSpec((block, width), lambda i: (i, 0)),
            pl.BlockSpec((total_keys, width), lambda i: (0, 0)),
            pl.BlockSpec((total_keys, width), lambda i: (0, 0)),
        ],
        out_specs=pl.BlockSpec((block, width), lambda i: (i, 0)),
        compiler_params=pltpu.CompilerParams(vmem_limit_bytes=60 * 1024 * 1024),
        cost_estimate=pl.CostEstimate(
            flops=flops,
            transcendentals=count * total_keys,
            bytes_accessed=2 * width * (2 * count + 2 * total_keys),
        ),
    )(query, keys, values)


def shards(
    frames,
    cache_frames,
    attn_gain,
    query_weight,
    key_weight,
    value_weight,
    out_weight,
    conv_gain,
    conv_weight,
):
    rows = frames.shape[1]
    cols = frames.shape[2]
    width = frames.shape[3]
    flat = frames.reshape(-1, width)
    count = flat.shape[0]
    scale = float(np.float32(1.0) / np.sqrt(np.float32(width)))
    whole = strip_gather(flat, "strip")
    normed = rms_scale(flat, attn_gain).astype(jnp.bfloat16)
    normed_all = rms_scale(whole, attn_gain).astype(jnp.bfloat16)
    query = jnp.dot(normed, query_weight, preferred_element_type=jnp.float32).astype(jnp.bfloat16)
    keys = jnp.dot(normed_all, key_weight, preferred_element_type=jnp.float32).astype(jnp.bfloat16)
    values = jnp.dot(normed_all, value_weight, preferred_element_type=jnp.float32).astype(jnp.bfloat16)
    attended = attend(query, keys, values, scale)
    resid = (
        flat.astype(jnp.float32) + jnp.dot(attended, out_weight, preferred_element_type=jnp.float32)
    ).astype(jnp.bfloat16)
    act = jax.nn.silu(rms_scale(resid, conv_gain)).astype(jnp.bfloat16).reshape(rows, cols, width)
    kernel = conv_weight.reshape(3, 3, 3 * width, width)

    def frame_conv(padded, step_t):
        padded = jnp.pad(padded, ((0, 0), (1, 1), (0, 0)))
        widened = jnp.concatenate(
            [padded[:, 0:cols], padded[:, 1 : cols + 1], padded[:, 2 : cols + 2]], axis=-1
        )
        total = None
        for step_r in range(3):
            window = widened[step_r : step_r + rows].reshape(-1, 3 * width)
            part = jnp.dot(window, kernel[step_t, step_r], preferred_element_type=jnp.float32)
            total = part if total is None else total + part
        return total

    act_padded = with_halo(act, (("strip", 0),), 1)
    nt = lax.axis_size("tm")
    frame_index = lax.axis_index("tm")
    to_next = frame_conv(act_padded, 1).astype(jnp.bfloat16)
    to_after = frame_conv(act_padded, 0).astype(jnp.bfloat16)
    from_prior = lax.ppermute(to_next, "tm", [(i, i + 1) for i in range(nt - 1)])
    from_older = lax.ppermute(to_after, "tm", [(i, i + 2) for i in range(nt - 2)])
    own = frame_conv(act_padded, 2)

    cache = lax.optimization_barrier((cache_frames, keys))[0]
    cache_padded = with_halo(cache, (("strip", 1),), 1)
    cache_part = lax.cond(
        frame_index == 0,
        lambda: frame_conv(cache_padded[1], 1) + frame_conv(cache_padded[0], 0),
        lambda: lax.cond(
            frame_index == 1,
            lambda: frame_conv(cache_padded[1], 0),
            lambda: jnp.zeros((count, width), jnp.float32),
        ),
    )
    result = (
        resid.astype(jnp.float32)
        + own
        + from_prior.astype(jnp.float32)
        + from_older.astype(jnp.float32)
        + cache_part
    )
    return result.astype(jnp.bfloat16).reshape(1, rows, cols, width)


def solution(mesh):
    return jax.shard_map(
        shards,
        mesh=mesh,
        in_specs=(
            P(("clip", "tm"), "strip", None, None),
            P("clip", "strip", None, None),
            P(),
            P(),
            P(),
            P(),
            P(),
            P(),
            P(),
        ),
        out_specs=P(("clip", "tm"), "strip", None, None),
        check_vma=False,
    )
```

```python
import functools

import jax
import jax.numpy as jnp
import numpy as np
from jax import lax
from jax.experimental import pallas as pl
from jax.experimental.pallas import tpu as pltpu
from jax.sharding import PartitionSpec as P


def passed_along(x, axis, by):
    size = lax.axis_size(axis)
    pairs = [(i, i + by) for i in range(size) if 0 <= i + by < size]
    return lax.ppermute(x, axis, pairs)


def with_halo(x, sides, width):
    for axis, dim in sides:
        size, length = (lax.axis_size(axis), x.shape[dim])
        up = [(i, (i + 1) % size) for i in range(size - 1)]
        down = [(j, i) for i, j in up]
        last = lax.slice_in_dim(x, length - width, length, axis=dim)
        leading = lax.slice_in_dim(x, 0, width, axis=dim)
        before = lax.ppermute(last, axis, up)
        after = lax.ppermute(leading, axis, down)
        x = jnp.concatenate([before, x, after], axis=dim)
    return x


def strip_gather(x, axis):
    n = lax.axis_size(axis)
    if n == 1:
        return x
    m = x.shape[0]
    up_pairs = [(i, i + 1) for i in range(n - 1)]
    down_pairs = [(i + 1, i) for i in range(n - 1)]
    ups, downs = [], []
    up, down = x, x
    for _ in range(n - 1):
        up = lax.ppermute(up, axis, up_pairs)
        down = lax.ppermute(down, axis, down_pairs)
        ups.append(up)
        downs.append(down)
    stacked = jnp.concatenate(ups[::-1] + [x] + downs, axis=0)
    me = lax.axis_index(axis)
    return lax.dynamic_slice_in_dim(stacked, (n - 1 - me) * m, n * m, axis=0)


def rms_scale(values, gain):
    wide = values.astype(jnp.float32)
    return wide * lax.rsqrt(jnp.mean(wide * wide, axis=-1, keepdims=True) + 1e-06) * gain


def attention_kernel(scale, q_ref, k_ref, v_ref, o_ref):
    scores = (
        lax.dot_general(
            q_ref[...], k_ref[...], (((1,), (1,)), ((), ())), preferred_element_type=jnp.float32
        )
        * scale
    )
    peak = jnp.max(scores, axis=1, keepdims=True)
    weights = jnp.exp(scores - peak)
    total = jnp.sum(weights, axis=1, keepdims=True)
    summed = jnp.dot(weights.astype(jnp.bfloat16), v_ref[...], preferred_element_type=jnp.float32)
    o_ref[...] = (summed / total).astype(o_ref.dtype)


def attend(query, keys, values, scale):
    count, width = query.shape
    total_keys = keys.shape[0]
    block = 160 if count % 160 == 0 else count
    flops = 4 * count * total_keys * width
    return pl.pallas_call(
        functools.partial(attention_kernel, scale),
        out_shape=jax.ShapeDtypeStruct((count, width), jnp.bfloat16),
        grid=(count // block,),
        in_specs=[
            pl.BlockSpec((block, width), lambda i: (i, 0)),
            pl.BlockSpec((total_keys, width), lambda i: (0, 0)),
            pl.BlockSpec((total_keys, width), lambda i: (0, 0)),
        ],
        out_specs=pl.BlockSpec((block, width), lambda i: (i, 0)),
        compiler_params=pltpu.CompilerParams(vmem_limit_bytes=60 * 1024 * 1024),
        cost_estimate=pl.CostEstimate(
            flops=flops,
            transcendentals=count * total_keys,
            bytes_accessed=2 * width * (2 * count + 2 * total_keys),
        ),
    )(query, keys, values)


def shards(
    frames,
    cache_frames,
    attn_gain,
    query_weight,
    key_weight,
    value_weight,
    out_weight,
    conv_gain,
    conv_weight,
):
    rows = frames.shape[1]
    cols = frames.shape[2]
    width = frames.shape[3]
    flat = frames.reshape(-1, width)
    count = flat.shape[0]
    scale = float(np.float32(1.0) / np.sqrt(np.float32(width)))
    whole = strip_gather(flat, "strip")
    normed = rms_scale(flat, attn_gain).astype(jnp.bfloat16)
    normed_all = rms_scale(whole, attn_gain).astype(jnp.bfloat16)
    query = jnp.dot(normed, query_weight, preferred_element_type=jnp.float32).astype(jnp.bfloat16)
    keys = jnp.dot(normed_all, key_weight, preferred_element_type=jnp.float32).astype(jnp.bfloat16)
    values = jnp.dot(normed_all, value_weight, preferred_element_type=jnp.float32).astype(jnp.bfloat16)
    attended = attend(query, keys, values, scale)
    resid = (
        flat.astype(jnp.float32) + jnp.dot(attended, out_weight, preferred_element_type=jnp.float32)
    ).astype(jnp.bfloat16)
    act = jax.nn.silu(rms_scale(resid, conv_gain)).astype(jnp.bfloat16).reshape(rows, cols, width)
    frame_index = lax.axis_index("tm")
    prior = passed_along(act, "tm", 1)
    older = passed_along(act, "tm", 2)
    prior = jnp.where(frame_index == 0, cache_frames[1], prior)
    older = jnp.where(frame_index == 0, cache_frames[0], older)
    older = jnp.where(frame_index == 1, cache_frames[1], older)
    stacked = jnp.stack([older, prior, act])
    padded = with_halo(stacked, (("strip", 1),), 1)
    padded = jnp.pad(padded, ((0, 0), (0, 0), (1, 1), (0, 0)))
    widened = jnp.concatenate(
        [padded[:, :, 0:cols], padded[:, :, 1 : cols + 1], padded[:, :, 2 : cols + 2]], axis=-1
    )
    kernel = conv_weight.reshape(3, 3, 3 * width, width)
    result = resid.astype(jnp.float32)
    for step_t in range(3):
        for step_r in range(3):
            window = widened[step_t, step_r : step_r + rows].reshape(-1, 3 * width)
            result = result + jnp.dot(
                window, kernel[step_t, step_r], preferred_element_type=jnp.float32
            )
    return result.astype(jnp.bfloat16).reshape(1, rows, cols, width)


def solution(mesh):
    return jax.shard_map(
        shards,
        mesh=mesh,
        in_specs=(
            P(("clip", "tm"), "strip", None, None),
            P("clip", "strip", None, None),
            P(),
            P(),
            P(),
            P(),
            P(),
            P(),
            P(),
        ),
        out_specs=P(("clip", "tm"), "strip", None, None),
        check_vma=False,
    )
```

```python
import functools

import jax
import jax.numpy as jnp
import numpy as np
from jax import lax
from jax.experimental import pallas as pl
from jax.experimental.pallas import tpu as pltpu
from jax.sharding import PartitionSpec as P


def passed_along(x, axis, by):
    size = lax.axis_size(axis)
    pairs = [(i, i + by) for i in range(size) if 0 <= i + by < size]
    return lax.ppermute(x, axis, pairs)


def with_halo(x, sides, width):
    for axis, dim in sides:
        size, length = (lax.axis_size(axis), x.shape[dim])
        up = [(i, (i + 1) % size) for i in range(size - 1)]
        down = [(j, i) for i, j in up]
        last = lax.slice_in_dim(x, length - width, length, axis=dim)
        leading = lax.slice_in_dim(x, 0, width, axis=dim)
        before = lax.ppermute(last, axis, up)
        after = lax.ppermute(leading, axis, down)
        x = jnp.concatenate([before, x, after], axis=dim)
    return x


def strip_gather(x, axis):
    n = lax.axis_size(axis)
    if n == 1:
        return x
    m = x.shape[0]
    up_pairs = [(i, i + 1) for i in range(n - 1)]
    down_pairs = [(i + 1, i) for i in range(n - 1)]
    ups, downs = [], []
    up, down = x, x
    for _ in range(n - 1):
        up = lax.ppermute(up, axis, up_pairs)
        down = lax.ppermute(down, axis, down_pairs)
        ups.append(up)
        downs.append(down)
    stacked = jnp.concatenate(ups[::-1] + [x] + downs, axis=0)
    me = lax.axis_index(axis)
    return lax.dynamic_slice_in_dim(stacked, (n - 1 - me) * m, n * m, axis=0)


def rms_scale(values, gain):
    wide = values.astype(jnp.float32)
    return wide * lax.rsqrt(jnp.mean(wide * wide, axis=-1, keepdims=True) + 1e-06) * gain


def attention_kernel(scale, q_ref, k_ref, v_ref, o_ref):
    scores = (
        lax.dot_general(
            q_ref[...], k_ref[...], (((1,), (1,)), ((), ())), preferred_element_type=jnp.float32
        )
        * scale
    )
    peak = jnp.max(scores, axis=1, keepdims=True)
    weights = jnp.exp(scores - peak)
    total = jnp.sum(weights, axis=1, keepdims=True)
    summed = jnp.dot(weights.astype(jnp.bfloat16), v_ref[...], preferred_element_type=jnp.float32)
    o_ref[...] = (summed / total).astype(o_ref.dtype)


def attend(query, keys, values, scale):
    count, width = query.shape
    total_keys = keys.shape[0]
    block = 160 if count % 160 == 0 else count
    flops = 4 * count * total_keys * width
    return pl.pallas_call(
        functools.partial(attention_kernel, scale),
        out_shape=jax.ShapeDtypeStruct((count, width), jnp.bfloat16),
        grid=(count // block,),
        in_specs=[
            pl.BlockSpec((block, width), lambda i: (i, 0)),
            pl.BlockSpec((total_keys, width), lambda i: (0, 0)),
            pl.BlockSpec((total_keys, width), lambda i: (0, 0)),
        ],
        out_specs=pl.BlockSpec((block, width), lambda i: (i, 0)),
        compiler_params=pltpu.CompilerParams(vmem_limit_bytes=60 * 1024 * 1024),
        cost_estimate=pl.CostEstimate(
            flops=flops,
            transcendentals=count * total_keys,
            bytes_accessed=2 * width * (2 * count + 2 * total_keys),
        ),
    )(query, keys, values)


def shards(
    frames,
    cache_frames,
    attn_gain,
    query_weight,
    key_weight,
    value_weight,
    out_weight,
    conv_gain,
    conv_weight,
):
    rows = frames.shape[1]
    cols = frames.shape[2]
    width = frames.shape[3]
    flat = frames.reshape(-1, width)
    count = flat.shape[0]
    scale = float(np.float32(1.0) / np.sqrt(np.float32(width)))
    whole = lax.all_gather(flat, "strip", axis=0, tiled=True)
    normed = rms_scale(flat, attn_gain).astype(jnp.bfloat16)
    normed_all = rms_scale(whole, attn_gain).astype(jnp.bfloat16)
    query = jnp.dot(normed, query_weight, preferred_element_type=jnp.float32).astype(jnp.bfloat16)
    keys = jnp.dot(normed_all, key_weight, preferred_element_type=jnp.float32).astype(jnp.bfloat16)
    values = jnp.dot(normed_all, value_weight, preferred_element_type=jnp.float32).astype(jnp.bfloat16)
    attended = attend(query, keys, values, scale)
    resid = (
        flat.astype(jnp.float32) + jnp.dot(attended, out_weight, preferred_element_type=jnp.float32)
    ).astype(jnp.bfloat16)
    act = jax.nn.silu(rms_scale(resid, conv_gain)).astype(jnp.bfloat16).reshape(rows, cols, width)
    frame_index = lax.axis_index("tm")
    prior = passed_along(act, "tm", 1)
    prior = jnp.where(frame_index == 0, cache_frames[1], prior)
    older = passed_along(prior, "tm", 1)
    older = jnp.where(frame_index == 0, cache_frames[0], older)
    stacked = jnp.stack([older, prior, act])
    padded = with_halo(stacked, (("strip", 1),), 1)
    padded = jnp.pad(padded, ((0, 0), (0, 0), (1, 1), (0, 0)))
    widened = jnp.concatenate(
        [padded[:, :, 0:cols], padded[:, :, 1 : cols + 1], padded[:, :, 2 : cols + 2]], axis=-1
    )
    kernel = conv_weight.reshape(3, 3, 3 * width, width)
    result = resid.astype(jnp.float32)
    for step_t in range(3):
        for step_r in range(3):
            window = widened[step_t, step_r : step_r + rows].reshape(-1, 3 * width)
            result = result + jnp.dot(
                window, kernel[step_t, step_r], preferred_element_type=jnp.float32
            )
    return result.astype(jnp.bfloat16).reshape(1, rows, cols, width)


def solution(mesh):
    return jax.shard_map(
        shards,
        mesh=mesh,
        in_specs=(
            P(("clip", "tm"), "strip", None, None),
            P("clip", "strip", None, None),
            P(),
            P(),
            P(),
            P(),
            P(),
            P(),
            P(),
        ),
        out_specs=P(("clip", "tm"), "strip", None, None),
        check_vma=False,
    )
```

```python
import functools

import jax
import jax.numpy as jnp
import numpy as np
from jax import lax
from jax.experimental import pallas as pl
from jax.experimental.pallas import tpu as pltpu
from jax.sharding import PartitionSpec as P


def passed_along(x, axis, by):
    size = lax.axis_size(axis)
    pairs = [(i, i + by) for i in range(size) if 0 <= i + by < size]
    return lax.ppermute(x, axis, pairs)


def with_halo(x, sides, width):
    for axis, dim in sides:
        size, length = (lax.axis_size(axis), x.shape[dim])
        up = [(i, (i + 1) % size) for i in range(size - 1)]
        down = [(j, i) for i, j in up]
        last = lax.slice_in_dim(x, length - width, length, axis=dim)
        leading = lax.slice_in_dim(x, 0, width, axis=dim)
        before = lax.ppermute(last, axis, up)
        after = lax.ppermute(leading, axis, down)
        x = jnp.concatenate([before, x, after], axis=dim)
    return x


def strip_gather(x, axis):
    n = lax.axis_size(axis)
    if n == 1:
        return x
    m = x.shape[0]
    up_pairs = [(i, i + 1) for i in range(n - 1)]
    down_pairs = [(i + 1, i) for i in range(n - 1)]
    ups, downs = [], []
    up, down = x, x
    for _ in range(n - 1):
        up = lax.ppermute(up, axis, up_pairs)
        down = lax.ppermute(down, axis, down_pairs)
        ups.append(up)
        downs.append(down)
    stacked = jnp.concatenate(ups[::-1] + [x] + downs, axis=0)
    me = lax.axis_index(axis)
    return lax.dynamic_slice_in_dim(stacked, (n - 1 - me) * m, n * m, axis=0)


def rms_scale(values, gain):
    wide = values.astype(jnp.float32)
    return wide * lax.rsqrt(jnp.mean(wide * wide, axis=-1, keepdims=True) + 1e-06) * gain


def attention_kernel(scale, q_ref, k_ref, v_ref, o_ref):
    scores = (
        lax.dot_general(
            q_ref[...], k_ref[...], (((1,), (1,)), ((), ())), preferred_element_type=jnp.float32
        )
        * scale
    )
    peak = jnp.max(scores, axis=1, keepdims=True)
    weights = jnp.exp(scores - peak)
    total = jnp.sum(weights, axis=1, keepdims=True)
    summed = jnp.dot(weights.astype(jnp.bfloat16), v_ref[...], preferred_element_type=jnp.float32)
    o_ref[...] = (summed / total).astype(o_ref.dtype)


def attend(query, keys, values, scale):
    count, width = query.shape
    total_keys = keys.shape[0]
    block = 160 if count % 160 == 0 else count
    flops = 4 * count * total_keys * width
    return pl.pallas_call(
        functools.partial(attention_kernel, scale),
        out_shape=jax.ShapeDtypeStruct((count, width), jnp.bfloat16),
        grid=(count // block,),
        in_specs=[
            pl.BlockSpec((block, width), lambda i: (i, 0)),
            pl.BlockSpec((total_keys, width), lambda i: (0, 0)),
            pl.BlockSpec((total_keys, width), lambda i: (0, 0)),
        ],
        out_specs=pl.BlockSpec((block, width), lambda i: (i, 0)),
        compiler_params=pltpu.CompilerParams(vmem_limit_bytes=60 * 1024 * 1024),
        cost_estimate=pl.CostEstimate(
            flops=flops,
            transcendentals=count * total_keys,
            bytes_accessed=2 * width * (2 * count + 2 * total_keys),
        ),
    )(query, keys, values)


def shards(
    frames,
    cache_frames,
    attn_gain,
    query_weight,
    key_weight,
    value_weight,
    out_weight,
    conv_gain,
    conv_weight,
):
    rows = frames.shape[1]
    cols = frames.shape[2]
    width = frames.shape[3]
    flat = frames.reshape(-1, width)
    count = flat.shape[0]
    scale = float(np.float32(1.0) / np.sqrt(np.float32(width)))
    whole = strip_gather(flat, "strip")
    normed = rms_scale(flat, attn_gain).astype(jnp.bfloat16)
    normed_all = rms_scale(whole, attn_gain).astype(jnp.bfloat16)
    query = jnp.dot(normed, query_weight, preferred_element_type=jnp.float32).astype(jnp.bfloat16)
    keys = jnp.dot(normed_all, key_weight, preferred_element_type=jnp.float32).astype(jnp.bfloat16)
    values = jnp.dot(normed_all, value_weight, preferred_element_type=jnp.float32).astype(jnp.bfloat16)
    attended = attend(query, keys, values, scale)
    resid = (
        flat.astype(jnp.float32) + jnp.dot(attended, out_weight, preferred_element_type=jnp.float32)
    ).astype(jnp.bfloat16)
    act = jax.nn.silu(rms_scale(resid, conv_gain)).astype(jnp.bfloat16).reshape(rows, cols, width)
    frame_index = lax.axis_index("tm")
    prior = passed_along(act, "tm", 1)
    prior = jnp.where(frame_index == 0, cache_frames[1], prior)
    older = passed_along(prior, "tm", 1)
    older = jnp.where(frame_index == 0, cache_frames[0], older)
    own_padded = with_halo(act[None], (("strip", 1),), 1)
    earlier = with_halo(jnp.stack([older, prior]), (("strip", 1),), 1)
    padded = jnp.concatenate([earlier, own_padded], axis=0)
    padded = jnp.pad(padded, ((0, 0), (0, 0), (1, 1), (0, 0)))
    widened = jnp.concatenate(
        [padded[:, :, 0:cols], padded[:, :, 1 : cols + 1], padded[:, :, 2 : cols + 2]], axis=-1
    )
    kernel = conv_weight.reshape(3, 3, 3 * width, width)
    result = resid.astype(jnp.float32)
    for step_t in range(3):
        for step_r in range(3):
            window = widened[step_t, step_r : step_r + rows].reshape(-1, 3 * width)
            result = result + jnp.dot(
                window, kernel[step_t, step_r], preferred_element_type=jnp.float32
            )
    return result.astype(jnp.bfloat16).reshape(1, rows, cols, width)


def solution(mesh):
    return jax.shard_map(
        shards,
        mesh=mesh,
        in_specs=(
            P(("clip", "tm"), "strip", None, None),
            P("clip", "strip", None, None),
            P(),
            P(),
            P(),
            P(),
            P(),
            P(),
            P(),
        ),
        out_specs=P(("clip", "tm"), "strip", None, None),
        check_vma=False,
    )
```

```python
import functools

import jax
import jax.numpy as jnp
import numpy as np
from jax import lax
from jax.experimental import pallas as pl
from jax.experimental.pallas import tpu as pltpu
from jax.sharding import PartitionSpec as P


def passed_along(x, axis, by):
    size = lax.axis_size(axis)
    pairs = [(i, i + by) for i in range(size) if 0 <= i + by < size]
    return lax.ppermute(x, axis, pairs)


def strip_gather(x, axis):
    n = lax.axis_size(axis)
    if n == 1:
        return x
    m = x.shape[0]
    up_pairs = [(i, i + 1) for i in range(n - 1)]
    down_pairs = [(i + 1, i) for i in range(n - 1)]
    ups, downs = [], []
    up, down = x, x
    for _ in range(n - 1):
        up = lax.ppermute(up, axis, up_pairs)
        down = lax.ppermute(down, axis, down_pairs)
        ups.append(up)
        downs.append(down)
    stacked = jnp.concatenate(ups[::-1] + [x] + downs, axis=0)
    me = lax.axis_index(axis)
    return lax.dynamic_slice_in_dim(stacked, (n - 1 - me) * m, n * m, axis=0)


def rms_scale(values, gain):
    wide = values.astype(jnp.float32)
    return wide * lax.rsqrt(jnp.mean(wide * wide, axis=-1, keepdims=True) + 1e-06) * gain


def attention_kernel(scale, q_ref, k_ref, v_ref, o_ref):
    scores = (
        lax.dot_general(
            q_ref[...], k_ref[...], (((1,), (1,)), ((), ())), preferred_element_type=jnp.float32
        )
        * scale
    )
    peak = jnp.max(scores, axis=1, keepdims=True)
    weights = jnp.exp(scores - peak)
    total = jnp.sum(weights, axis=1, keepdims=True)
    summed = jnp.dot(weights.astype(jnp.bfloat16), v_ref[...], preferred_element_type=jnp.float32)
    o_ref[...] = (summed / total).astype(o_ref.dtype)


def attend(query, keys, values, scale):
    count, width = query.shape
    total_keys = keys.shape[0]
    block = 160 if count % 160 == 0 else count
    flops = 4 * count * total_keys * width
    return pl.pallas_call(
        functools.partial(attention_kernel, scale),
        out_shape=jax.ShapeDtypeStruct((count, width), jnp.bfloat16),
        grid=(count // block,),
        in_specs=[
            pl.BlockSpec((block, width), lambda i: (i, 0)),
            pl.BlockSpec((total_keys, width), lambda i: (0, 0)),
            pl.BlockSpec((total_keys, width), lambda i: (0, 0)),
        ],
        out_specs=pl.BlockSpec((block, width), lambda i: (i, 0)),
        compiler_params=pltpu.CompilerParams(vmem_limit_bytes=60 * 1024 * 1024),
        cost_estimate=pl.CostEstimate(
            flops=flops,
            transcendentals=count * total_keys,
            bytes_accessed=2 * width * (2 * count + 2 * total_keys),
        ),
    )(query, keys, values)


def shards(
    frames,
    cache_frames,
    attn_gain,
    query_weight,
    key_weight,
    value_weight,
    out_weight,
    conv_gain,
    conv_weight,
):
    rows = frames.shape[1]
    cols = frames.shape[2]
    width = frames.shape[3]
    flat = frames.reshape(-1, width)
    count = flat.shape[0]
    scale = float(np.float32(1.0) / np.sqrt(np.float32(width)))
    whole = strip_gather(flat, "strip")
    normed = rms_scale(flat, attn_gain).astype(jnp.bfloat16)
    normed_all = rms_scale(whole, attn_gain).astype(jnp.bfloat16)
    query = jnp.dot(normed, query_weight, preferred_element_type=jnp.float32).astype(jnp.bfloat16)
    keys = jnp.dot(normed_all, key_weight, preferred_element_type=jnp.float32).astype(jnp.bfloat16)
    values = jnp.dot(normed_all, value_weight, preferred_element_type=jnp.float32).astype(jnp.bfloat16)
    attended = attend(query, keys, values, scale)
    resid = (
        flat.astype(jnp.float32) + jnp.dot(attended, out_weight, preferred_element_type=jnp.float32)
    ).astype(jnp.bfloat16)
    act = jax.nn.silu(rms_scale(resid, conv_gain)).astype(jnp.bfloat16).reshape(rows, cols, width)
    frame_index = lax.axis_index("tm")
    prior = passed_along(act, "tm", 1)
    prior = jnp.where(frame_index == 0, cache_frames[1], prior)
    older = passed_along(prior, "tm", 1)
    older = jnp.where(frame_index == 0, cache_frames[0], older)
    stacked = jnp.stack([older, prior, act])
    padded = jnp.pad(stacked, ((0, 0), (1, 1), (1, 1), (0, 0)))
    widened = jnp.concatenate(
        [padded[:, :, 0:cols], padded[:, :, 1 : cols + 1], padded[:, :, 2 : cols + 2]], axis=-1
    )
    kernel = conv_weight.reshape(3, 3, 3 * width, width)
    to_prev = None
    to_next = None
    for step_t in range(3):
        first = jnp.dot(widened[step_t, 1], kernel[step_t, 2], preferred_element_type=jnp.float32)
        last = jnp.dot(widened[step_t, rows], kernel[step_t, 0], preferred_element_type=jnp.float32)
        to_prev = first if to_prev is None else to_prev + first
        to_next = last if to_next is None else to_next + last
    n = lax.axis_size("strip")
    from_next = lax.ppermute(
        to_prev.astype(jnp.bfloat16), "strip", [(i + 1, i) for i in range(n - 1)]
    )
    from_prev = lax.ppermute(
        to_next.astype(jnp.bfloat16), "strip", [(i, i + 1) for i in range(n - 1)]
    )
    result = resid.astype(jnp.float32)
    for step_t in range(3):
        for step_r in range(3):
            window = widened[step_t, step_r : step_r + rows].reshape(-1, 3 * width)
            result = result + jnp.dot(
                window, kernel[step_t, step_r], preferred_element_type=jnp.float32
            )
    edges = jnp.concatenate(
        [
            from_prev[None].astype(jnp.float32),
            jnp.zeros((rows - 2, cols, width), jnp.float32),
            from_next[None].astype(jnp.float32),
        ],
        axis=0,
    )
    result = result + edges.reshape(-1, width)
    return result.astype(jnp.bfloat16).reshape(1, rows, cols, width)


def solution(mesh):
    return jax.shard_map(
        shards,
        mesh=mesh,
        in_specs=(
            P(("clip", "tm"), "strip", None, None),
            P("clip", "strip", None, None),
            P(),
            P(),
            P(),
            P(),
            P(),
            P(),
            P(),
        ),
        out_specs=P(("clip", "tm"), "strip", None, None),
        check_vma=False,
    )
```

```python
import functools

import jax
import jax.numpy as jnp
import numpy as np
from jax import lax
from jax.experimental import pallas as pl
from jax.experimental.pallas import tpu as pltpu
from jax.sharding import PartitionSpec as P


def passed_along(x, axis, by):
    size = lax.axis_size(axis)
    pairs = [(i, i + by) for i in range(size) if 0 <= i + by < size]
    return lax.ppermute(x, axis, pairs)


def strip_gather(x, axis):
    n = lax.axis_size(axis)
    if n == 1:
        return x
    m = x.shape[0]
    up_pairs = [(i, i + 1) for i in range(n - 1)]
    down_pairs = [(i + 1, i) for i in range(n - 1)]
    ups, downs = [], []
    up, down = x, x
    for _ in range(n - 1):
        up = lax.ppermute(up, axis, up_pairs)
        down = lax.ppermute(down, axis, down_pairs)
        ups.append(up)
        downs.append(down)
    stacked = jnp.concatenate(ups[::-1] + [x] + downs, axis=0)
    me = lax.axis_index(axis)
    return lax.dynamic_slice_in_dim(stacked, (n - 1 - me) * m, n * m, axis=0)


def rms_scale(values, gain):
    wide = values.astype(jnp.float32)
    return wide * lax.rsqrt(jnp.mean(wide * wide, axis=-1, keepdims=True) + 1e-06) * gain


def scaled(x, gain):
    wide = x.astype(jnp.float32)
    return wide * lax.rsqrt(jnp.mean(wide * wide, axis=-1, keepdims=True) + 1e-06) * gain


def attention_kernel(
    scale, whole_ref, flat_ref, query_ref, again_ref, wk_ref, wv_ref, wo_ref, cgain_ref,
    resid_ref, act_ref, keys_ref, values_ref,
):
    @pl.when(pl.program_id(0) == 0)
    def _():
        normed_all = scaled(whole_ref[...], again_ref[...]).astype(jnp.bfloat16)
        keys_ref[...] = jnp.dot(
            normed_all, wk_ref[...], preferred_element_type=jnp.float32
        ).astype(jnp.bfloat16)
        values_ref[...] = jnp.dot(
            normed_all, wv_ref[...], preferred_element_type=jnp.float32
        ).astype(jnp.bfloat16)

    scores = (
        lax.dot_general(
            query_ref[...], keys_ref[...], (((1,), (1,)), ((), ())),
            preferred_element_type=jnp.float32,
        )
        * scale
    )
    peak = jnp.max(scores, axis=1, keepdims=True)
    weights = jnp.exp(scores - peak)
    total = jnp.sum(weights, axis=1, keepdims=True)
    summed = jnp.dot(
        weights.astype(jnp.bfloat16), values_ref[...], preferred_element_type=jnp.float32
    )
    attended = (summed / total).astype(jnp.bfloat16)
    resid = (
        flat_ref[...].astype(jnp.float32)
        + jnp.dot(attended, wo_ref[...], preferred_element_type=jnp.float32)
    ).astype(jnp.bfloat16)
    resid_ref[...] = resid
    shown = scaled(resid, cgain_ref[...])
    act_ref[...] = (shown / (1.0 + jnp.exp(-shown))).astype(jnp.bfloat16)


def attend(whole, flat, query, attn_gain, key_weight, value_weight, out_weight, conv_gain, scale):
    count, width = query.shape
    total_keys = whole.shape[0]
    block = 160 if count % 160 == 0 else count
    full = lambda shape: pl.BlockSpec(shape, lambda i: (0, 0))
    rows_of = pl.BlockSpec((block, width), lambda i: (i, 0))
    flops = 4 * count * total_keys * width + 4 * total_keys * width * width
    flops += 2 * count * width * width
    return pl.pallas_call(
        functools.partial(attention_kernel, scale),
        out_shape=(
            jax.ShapeDtypeStruct((count, width), jnp.bfloat16),
            jax.ShapeDtypeStruct((count, width), jnp.bfloat16),
        ),
        grid=(count // block,),
        in_specs=[
            full((total_keys, width)),
            rows_of,
            rows_of,
            full((1, width)),
            full((width, width)),
            full((width, width)),
            full((width, width)),
            full((1, width)),
        ],
        out_specs=(rows_of, rows_of),
        scratch_shapes=[
            pltpu.VMEM((total_keys, width), jnp.bfloat16),
            pltpu.VMEM((total_keys, width), jnp.bfloat16),
        ],
        compiler_params=pltpu.CompilerParams(vmem_limit_bytes=60 * 1024 * 1024),
        cost_estimate=pl.CostEstimate(
            flops=flops,
            transcendentals=count * total_keys + count * width,
            bytes_accessed=2 * width * (total_keys + 4 * count + 3 * width),
        ),
    )(
        whole, flat, query, attn_gain.reshape(1, width), key_weight, value_weight, out_weight,
        conv_gain.reshape(1, width),
    )


def shards(
    frames,
    cache_frames,
    attn_gain,
    query_weight,
    key_weight,
    value_weight,
    out_weight,
    conv_gain,
    conv_weight,
):
    rows = frames.shape[1]
    cols = frames.shape[2]
    width = frames.shape[3]
    flat = frames.reshape(-1, width)
    count = flat.shape[0]
    scale = float(np.float32(1.0) / np.sqrt(np.float32(width)))
    whole = strip_gather(flat, "strip")
    normed = rms_scale(flat, attn_gain).astype(jnp.bfloat16)
    query = jnp.dot(normed, query_weight, preferred_element_type=jnp.float32).astype(jnp.bfloat16)
    resid, act = attend(
        whole, flat, query, attn_gain, key_weight, value_weight, out_weight, conv_gain, scale
    )
    act = act.reshape(rows, cols, width)
    frame_index = lax.axis_index("tm")
    prior = passed_along(act, "tm", 1)
    prior = jnp.where(frame_index == 0, cache_frames[1], prior)
    older = passed_along(prior, "tm", 1)
    older = jnp.where(frame_index == 0, cache_frames[0], older)
    stacked = jnp.stack([older, prior, act])
    padded = jnp.pad(stacked, ((0, 0), (1, 1), (1, 1), (0, 0)))
    widened = jnp.concatenate(
        [padded[:, :, 0:cols], padded[:, :, 1 : cols + 1], padded[:, :, 2 : cols + 2]], axis=-1
    )
    kernel = conv_weight.reshape(3, 3, 3 * width, width)
    to_prev = None
    to_next = None
    for step_t in range(3):
        first = jnp.dot(widened[step_t, 1], kernel[step_t, 2], preferred_element_type=jnp.float32)
        last = jnp.dot(widened[step_t, rows], kernel[step_t, 0], preferred_element_type=jnp.float32)
        to_prev = first if to_prev is None else to_prev + first
        to_next = last if to_next is None else to_next + last
    n = lax.axis_size("strip")
    from_next = lax.ppermute(
        to_prev.astype(jnp.bfloat16), "strip", [(i + 1, i) for i in range(n - 1)]
    )
    from_prev = lax.ppermute(
        to_next.astype(jnp.bfloat16), "strip", [(i, i + 1) for i in range(n - 1)]
    )
    result = resid.astype(jnp.float32)
    for step_t in range(3):
        for step_r in range(3):
            window = widened[step_t, step_r : step_r + rows].reshape(-1, 3 * width)
            result = result + jnp.dot(
                window, kernel[step_t, step_r], preferred_element_type=jnp.float32
            )
    edges = jnp.concatenate(
        [
            from_prev[None].astype(jnp.float32),
            jnp.zeros((rows - 2, cols, width), jnp.float32),
            from_next[None].astype(jnp.float32),
        ],
        axis=0,
    )
    result = result + edges.reshape(-1, width)
    return result.astype(jnp.bfloat16).reshape(1, rows, cols, width)


def solution(mesh):
    return jax.shard_map(
        shards,
        mesh=mesh,
        in_specs=(
            P(("clip", "tm"), "strip", None, None),
            P("clip", "strip", None, None),
            P(),
            P(),
            P(),
            P(),
            P(),
            P(),
            P(),
        ),
        out_specs=P(("clip", "tm"), "strip", None, None),
        check_vma=False,
    )
```

```python
import functools

import jax
import jax.numpy as jnp
import numpy as np
from jax import lax
from jax.experimental import pallas as pl
from jax.experimental.pallas import tpu as pltpu
from jax.sharding import PartitionSpec as P


def passed_along(x, axis, by):
    size = lax.axis_size(axis)
    pairs = [(i, i + by) for i in range(size) if 0 <= i + by < size]
    return lax.ppermute(x, axis, pairs)


def strip_gather(x, axis):
    n = lax.axis_size(axis)
    if n == 1:
        return x
    m = x.shape[0]
    up_pairs = [(i, i + 1) for i in range(n - 1)]
    down_pairs = [(i + 1, i) for i in range(n - 1)]
    ups, downs = [], []
    up, down = x, x
    for _ in range(n - 1):
        up = lax.ppermute(up, axis, up_pairs)
        down = lax.ppermute(down, axis, down_pairs)
        ups.append(up)
        downs.append(down)
    stacked = jnp.concatenate(ups[::-1] + [x] + downs, axis=0)
    me = lax.axis_index(axis)
    return lax.dynamic_slice_in_dim(stacked, (n - 1 - me) * m, n * m, axis=0)


def rms_scale(values, gain):
    wide = values.astype(jnp.float32)
    return wide * lax.rsqrt(jnp.mean(wide * wide, axis=-1, keepdims=True) + 1e-06) * gain


def scaled(x, gain):
    wide = x.astype(jnp.float32)
    return wide * lax.rsqrt(jnp.mean(wide * wide, axis=-1, keepdims=True) + 1e-06) * gain


def attention_kernel(
    scale, whole_ref, flat_ref, query_ref, again_ref, wk_ref, wv_ref, wo_ref, cgain_ref,
    resid_ref, act_ref, keys_ref, values_ref,
):
    @pl.when(pl.program_id(0) == 0)
    def _():
        normed_all = scaled(whole_ref[...], again_ref[...]).astype(jnp.bfloat16)
        keys_ref[...] = jnp.dot(
            normed_all, wk_ref[...], preferred_element_type=jnp.float32
        ).astype(jnp.bfloat16)
        values_ref[...] = jnp.dot(
            normed_all, wv_ref[...], preferred_element_type=jnp.float32
        ).astype(jnp.bfloat16)

    scores = (
        lax.dot_general(
            query_ref[...], keys_ref[...], (((1,), (1,)), ((), ())),
            preferred_element_type=jnp.float32,
        )
        * scale
    )
    peak = jnp.max(scores, axis=1, keepdims=True)
    weights = jnp.exp(scores - peak)
    total = jnp.sum(weights, axis=1, keepdims=True)
    summed = jnp.dot(
        weights.astype(jnp.bfloat16), values_ref[...], preferred_element_type=jnp.float32
    )
    attended = (summed / total).astype(jnp.bfloat16)
    resid = (
        flat_ref[...].astype(jnp.float32)
        + jnp.dot(attended, wo_ref[...], preferred_element_type=jnp.float32)
    ).astype(jnp.bfloat16)
    resid_ref[...] = resid
    shown = scaled(resid, cgain_ref[...])
    act_ref[...] = (shown / (1.0 + jnp.exp(-shown))).astype(jnp.bfloat16)


def attend(whole, flat, query, attn_gain, key_weight, value_weight, out_weight, conv_gain, scale):
    count, width = query.shape
    total_keys = whole.shape[0]
    block = 160 if count % 160 == 0 else count
    full = lambda shape: pl.BlockSpec(shape, lambda i: (0, 0))
    rows_of = pl.BlockSpec((block, width), lambda i: (i, 0))
    flops = 4 * count * total_keys * width + 4 * total_keys * width * width
    flops += 2 * count * width * width
    return pl.pallas_call(
        functools.partial(attention_kernel, scale),
        out_shape=(
            jax.ShapeDtypeStruct((count, width), jnp.bfloat16),
            jax.ShapeDtypeStruct((count, width), jnp.bfloat16),
        ),
        grid=(count // block,),
        in_specs=[
            full((total_keys, width)),
            rows_of,
            rows_of,
            full((1, width)),
            full((width, width)),
            full((width, width)),
            full((width, width)),
            full((1, width)),
        ],
        out_specs=(rows_of, rows_of),
        scratch_shapes=[
            pltpu.VMEM((total_keys, width), jnp.bfloat16),
            pltpu.VMEM((total_keys, width), jnp.bfloat16),
        ],
        compiler_params=pltpu.CompilerParams(vmem_limit_bytes=60 * 1024 * 1024),
        cost_estimate=pl.CostEstimate(
            flops=flops,
            transcendentals=count * total_keys + count * width,
            bytes_accessed=2 * width * (total_keys + 4 * count + 3 * width),
        ),
    )(
        whole, flat, query, attn_gain.reshape(1, width), key_weight, value_weight, out_weight,
        conv_gain.reshape(1, width),
    )


def shards(
    frames,
    cache_frames,
    attn_gain,
    query_weight,
    key_weight,
    value_weight,
    out_weight,
    conv_gain,
    conv_weight,
):
    rows = frames.shape[1]
    cols = frames.shape[2]
    width = frames.shape[3]
    flat = frames.reshape(-1, width)
    count = flat.shape[0]
    scale = float(np.float32(1.0) / np.sqrt(np.float32(width)))
    whole = strip_gather(flat, "strip")
    normed = rms_scale(flat, attn_gain).astype(jnp.bfloat16)
    query = jnp.dot(normed, query_weight, preferred_element_type=jnp.float32).astype(jnp.bfloat16)
    resid, act = attend(
        whole, flat, query, attn_gain, key_weight, value_weight, out_weight, conv_gain, scale
    )
    act = act.reshape(rows, cols, width)
    frame_index = lax.axis_index("tm")
    prior = passed_along(act, "tm", 1)
    prior = jnp.where(frame_index == 0, cache_frames[1], prior)
    older = passed_along(prior, "tm", 1)
    older = jnp.where(frame_index == 0, cache_frames[0], older)
    kernel = conv_weight.reshape(3, 3, 3 * width, width)

    def widen(frame):
        padded = jnp.pad(frame, ((1, 1), (1, 1), (0, 0)))
        return jnp.concatenate(
            [padded[:, 0:cols], padded[:, 1 : cols + 1], padded[:, 2 : cols + 2]], axis=-1
        )

    def frame_terms(wide, step_t):
        main = None
        for step_r in range(3):
            window = wide[step_r : step_r + rows].reshape(-1, 3 * width)
            part = jnp.dot(window, kernel[step_t, step_r], preferred_element_type=jnp.float32)
            main = part if main is None else main + part
        first = jnp.dot(wide[1], kernel[step_t, 2], preferred_element_type=jnp.float32)
        last = jnp.dot(wide[rows], kernel[step_t, 0], preferred_element_type=jnp.float32)
        return main, first, last

    own_main, own_first, own_last = frame_terms(widen(act), 2)
    prior_main, prior_first, prior_last = frame_terms(widen(prior), 1)
    older_main, older_first, older_last = frame_terms(widen(older), 0)
    to_prev = own_first + prior_first + older_first
    to_next = own_last + prior_last + older_last
    n = lax.axis_size("strip")
    from_next = lax.ppermute(
        to_prev.astype(jnp.bfloat16), "strip", [(i + 1, i) for i in range(n - 1)]
    )
    from_prev = lax.ppermute(
        to_next.astype(jnp.bfloat16), "strip", [(i, i + 1) for i in range(n - 1)]
    )
    result = resid.astype(jnp.float32) + own_main + prior_main + older_main
    edges = jnp.concatenate(
        [
            from_prev[None].astype(jnp.float32),
            jnp.zeros((rows - 2, cols, width), jnp.float32),
            from_next[None].astype(jnp.float32),
        ],
        axis=0,
    )
    result = result + edges.reshape(-1, width)
    return result.astype(jnp.bfloat16).reshape(1, rows, cols, width)


def solution(mesh):
    return jax.shard_map(
        shards,
        mesh=mesh,
        in_specs=(
            P(("clip", "tm"), "strip", None, None),
            P("clip", "strip", None, None),
            P(),
            P(),
            P(),
            P(),
            P(),
            P(),
            P(),
        ),
        out_specs=P(("clip", "tm"), "strip", None, None),
        check_vma=False,
    )
```

```python
import functools

import jax
import jax.numpy as jnp
import numpy as np
from jax import lax
from jax.experimental import pallas as pl
from jax.experimental.pallas import tpu as pltpu
from jax.sharding import PartitionSpec as P


def passed_along(x, axis, by):
    size = lax.axis_size(axis)
    pairs = [(i, i + by) for i in range(size) if 0 <= i + by < size]
    return lax.ppermute(x, axis, pairs)


def strip_gather(x, axis):
    n = lax.axis_size(axis)
    m = x.shape[0]
    if n == 1:
        return x, jnp.zeros((1,), jnp.int32)
    up_pairs = [(i, i + 1) for i in range(n - 1)]
    down_pairs = [(i + 1, i) for i in range(n - 1)]
    ups, downs = [], []
    up, down = x, x
    for _ in range(n - 1):
        up = lax.ppermute(up, axis, up_pairs)
        down = lax.ppermute(down, axis, down_pairs)
        ups.append(up)
        downs.append(down)
    stacked = jnp.concatenate(ups[::-1] + [x] + downs, axis=0)
    me = lax.axis_index(axis)
    return stacked, ((n - 1 - me) * m).astype(jnp.int32).reshape(1)


def rms_scale(values, gain):
    wide = values.astype(jnp.float32)
    return wide * lax.rsqrt(jnp.mean(wide * wide, axis=-1, keepdims=True) + 1e-06) * gain


def scaled(x, gain):
    wide = x.astype(jnp.float32)
    return wide * lax.rsqrt(jnp.mean(wide * wide, axis=-1, keepdims=True) + 1e-06) * gain


def attention_kernel(
    scale, start_ref, stacked_ref, flat_ref, query_ref, again_ref, wk_ref, wv_ref, wo_ref,
    cgain_ref, resid_ref, act_ref, whole_ref, keys_ref, values_ref,
):
    @pl.when(pl.program_id(0) == 0)
    def _():
        first = pl.multiple_of(start_ref[0], 16)
        pltpu.sync_copy(stacked_ref.at[pl.ds(first, whole_ref.shape[0])], whole_ref)
        normed_all = scaled(whole_ref[...], again_ref[...]).astype(jnp.bfloat16)
        keys_ref[...] = jnp.dot(
            normed_all, wk_ref[...], preferred_element_type=jnp.float32
        ).astype(jnp.bfloat16)
        values_ref[...] = jnp.dot(
            normed_all, wv_ref[...], preferred_element_type=jnp.float32
        ).astype(jnp.bfloat16)

    scores = (
        lax.dot_general(
            query_ref[...], keys_ref[...], (((1,), (1,)), ((), ())),
            preferred_element_type=jnp.float32,
        )
        * scale
    )
    peak = jnp.max(scores, axis=1, keepdims=True)
    weights = jnp.exp(scores - peak)
    total = jnp.sum(weights, axis=1, keepdims=True)
    summed = jnp.dot(
        weights.astype(jnp.bfloat16), values_ref[...], preferred_element_type=jnp.float32
    )
    attended = (summed / total).astype(jnp.bfloat16)
    resid = (
        flat_ref[...].astype(jnp.float32)
        + jnp.dot(attended, wo_ref[...], preferred_element_type=jnp.float32)
    ).astype(jnp.bfloat16)
    resid_ref[...] = resid
    shown = scaled(resid, cgain_ref[...])
    act_ref[...] = (shown / (1.0 + jnp.exp(-shown))).astype(jnp.bfloat16)


def attend(
    stacked, start, parts, flat, query, attn_gain, key_weight, value_weight, out_weight, conv_gain,
    scale,
):
    count, width = query.shape
    total_keys = parts * count
    block = 160 if count % 160 == 0 else count
    full = lambda shape: pl.BlockSpec(shape, lambda i, start: (0, 0))
    rows_of = pl.BlockSpec((block, width), lambda i, start: (i, 0))
    flops = 4 * count * total_keys * width + 4 * total_keys * width * width
    flops += 2 * count * width * width
    return pl.pallas_call(
        functools.partial(attention_kernel, scale),
        out_shape=(
            jax.ShapeDtypeStruct((count, width), jnp.bfloat16),
            jax.ShapeDtypeStruct((count, width), jnp.bfloat16),
        ),
        grid_spec=pltpu.PrefetchScalarGridSpec(
            num_scalar_prefetch=1,
            grid=(count // block,),
            in_specs=[
            pl.BlockSpec(memory_space=pl.ANY),
            rows_of,
            rows_of,
            full((1, width)),
            full((width, width)),
            full((width, width)),
            full((width, width)),
            full((1, width)),
            ],
            out_specs=(rows_of, rows_of),
            scratch_shapes=[
                pltpu.VMEM((total_keys, width), jnp.bfloat16),
                pltpu.VMEM((total_keys, width), jnp.bfloat16),
                pltpu.VMEM((total_keys, width), jnp.bfloat16),
            ],
        ),
        compiler_params=pltpu.CompilerParams(vmem_limit_bytes=60 * 1024 * 1024),
        cost_estimate=pl.CostEstimate(
            flops=flops,
            transcendentals=count * total_keys + count * width,
            bytes_accessed=2 * width * (total_keys + 4 * count + 3 * width),
        ),
    )(
        start, stacked, flat, query, attn_gain.reshape(1, width), key_weight, value_weight,
        out_weight, conv_gain.reshape(1, width),
    )


def shards(
    frames,
    cache_frames,
    attn_gain,
    query_weight,
    key_weight,
    value_weight,
    out_weight,
    conv_gain,
    conv_weight,
):
    rows = frames.shape[1]
    cols = frames.shape[2]
    width = frames.shape[3]
    flat = frames.reshape(-1, width)
    count = flat.shape[0]
    scale = float(np.float32(1.0) / np.sqrt(np.float32(width)))
    stacked, start = strip_gather(flat, "strip")
    normed = rms_scale(flat, attn_gain).astype(jnp.bfloat16)
    query = jnp.dot(normed, query_weight, preferred_element_type=jnp.float32).astype(jnp.bfloat16)
    resid, act = attend(
        stacked, start, lax.axis_size("strip"), flat, query, attn_gain, key_weight, value_weight,
        out_weight, conv_gain, scale,
    )
    act = act.reshape(rows, cols, width)
    frame_index = lax.axis_index("tm")
    prior = passed_along(act, "tm", 1)
    prior = jnp.where(frame_index == 0, cache_frames[1], prior)
    older = lax.ppermute(prior, "tm", [(i, i + 1) for i in range(1, lax.axis_size("tm") - 1)])
    older = jnp.where(frame_index == 0, cache_frames[0], older)
    older = jnp.where(frame_index == 1, cache_frames[1], older)
    kernel = conv_weight.reshape(3, 3, 3 * width, width)

    def widen(frame):
        padded = jnp.pad(frame, ((1, 1), (1, 1), (0, 0)))
        return jnp.concatenate(
            [padded[:, 0:cols], padded[:, 1 : cols + 1], padded[:, 2 : cols + 2]], axis=-1
        )

    def frame_terms(wide, step_t):
        main = None
        for step_r in range(3):
            window = wide[step_r : step_r + rows].reshape(-1, 3 * width)
            part = jnp.dot(window, kernel[step_t, step_r], preferred_element_type=jnp.float32)
            main = part if main is None else main + part
        first = jnp.dot(wide[1], kernel[step_t, 2], preferred_element_type=jnp.float32)
        last = jnp.dot(wide[rows], kernel[step_t, 0], preferred_element_type=jnp.float32)
        return main, first, last

    own_main, own_first, own_last = frame_terms(widen(act), 2)
    prior_main, prior_first, prior_last = frame_terms(widen(prior), 1)
    older_main, older_first, older_last = frame_terms(widen(older), 0)
    to_prev = own_first + prior_first + older_first
    to_next = own_last + prior_last + older_last
    n = lax.axis_size("strip")
    from_next = lax.ppermute(
        to_prev.astype(jnp.bfloat16), "strip", [(i + 1, i) for i in range(n - 1)]
    )
    from_prev = lax.ppermute(
        to_next.astype(jnp.bfloat16), "strip", [(i, i + 1) for i in range(n - 1)]
    )
    result = resid.astype(jnp.float32) + own_main + prior_main + older_main
    edges = jnp.concatenate(
        [
            from_prev[None].astype(jnp.float32),
            jnp.zeros((rows - 2, cols, width), jnp.float32),
            from_next[None].astype(jnp.float32),
        ],
        axis=0,
    )
    result = result + edges.reshape(-1, width)
    return result.astype(jnp.bfloat16).reshape(1, rows, cols, width)


def solution(mesh):
    return jax.shard_map(
        shards,
        mesh=mesh,
        in_specs=(
            P(("clip", "tm"), "strip", None, None),
            P("clip", "strip", None, None),
            P(),
            P(),
            P(),
            P(),
            P(),
            P(),
            P(),
        ),
        out_specs=P(("clip", "tm"), "strip", None, None),
        check_vma=False,
    )
```

```python
import functools

import jax
import jax.numpy as jnp
import numpy as np
from jax import lax
from jax.experimental import pallas as pl
from jax.experimental.pallas import tpu as pltpu
from jax.sharding import PartitionSpec as P


def passed_along(x, axis, by):
    size = lax.axis_size(axis)
    pairs = [(i, i + by) for i in range(size) if 0 <= i + by < size]
    return lax.ppermute(x, axis, pairs)


def strip_gather(x, axis):
    n = lax.axis_size(axis)
    if n == 1:
        return x
    m = x.shape[0]
    up_pairs = [(i, i + 1) for i in range(n - 1)]
    down_pairs = [(i + 1, i) for i in range(n - 1)]
    ups, downs = [], []
    up, down = x, x
    for _ in range(n - 1):
        up = lax.ppermute(up, axis, up_pairs)
        down = lax.ppermute(down, axis, down_pairs)
        ups.append(up)
        downs.append(down)
    stacked = jnp.concatenate(ups[::-1] + [x] + downs, axis=0)
    me = lax.axis_index(axis)
    return lax.dynamic_slice_in_dim(stacked, (n - 1 - me) * m, n * m, axis=0)


def rms_scale(values, gain):
    wide = values.astype(jnp.float32)
    return wide * lax.rsqrt(jnp.mean(wide * wide, axis=-1, keepdims=True) + 1e-06) * gain


def scaled(x, gain):
    wide = x.astype(jnp.float32)
    return wide * lax.rsqrt(jnp.mean(wide * wide, axis=-1, keepdims=True) + 1e-06) * gain


def attention_kernel(
    scale, whole_ref, flat_ref, query_ref, again_ref, wk_ref, wv_ref, wo_ref, cgain_ref,
    resid_ref, act_ref, keys_ref, values_ref,
):
    @pl.when(pl.program_id(0) == 0)
    def _():
        normed_all = scaled(whole_ref[...], again_ref[...]).astype(jnp.bfloat16)
        keys_ref[...] = jnp.dot(
            normed_all, wk_ref[...], preferred_element_type=jnp.float32
        ).astype(jnp.bfloat16)
        values_ref[...] = jnp.dot(
            normed_all, wv_ref[...], preferred_element_type=jnp.float32
        ).astype(jnp.bfloat16)

    scores = (
        lax.dot_general(
            query_ref[...], keys_ref[...], (((1,), (1,)), ((), ())),
            preferred_element_type=jnp.float32,
        )
        * scale
    )
    peak = jnp.max(scores, axis=1, keepdims=True)
    weights = jnp.exp(scores - peak)
    total = jnp.sum(weights, axis=1, keepdims=True)
    summed = jnp.dot(
        weights.astype(jnp.bfloat16), values_ref[...], preferred_element_type=jnp.float32
    )
    attended = (summed / total).astype(jnp.bfloat16)
    resid = (
        flat_ref[...].astype(jnp.float32)
        + jnp.dot(attended, wo_ref[...], preferred_element_type=jnp.float32)
    ).astype(jnp.bfloat16)
    resid_ref[...] = resid
    shown = scaled(resid, cgain_ref[...])
    act_ref[...] = (shown / (1.0 + jnp.exp(-shown))).astype(jnp.bfloat16)


def attend(whole, flat, query, attn_gain, key_weight, value_weight, out_weight, conv_gain, scale):
    count, width = query.shape
    total_keys = whole.shape[0]
    block = 160 if count % 160 == 0 else count
    full = lambda shape: pl.BlockSpec(shape, lambda i: (0, 0))
    rows_of = pl.BlockSpec((block, width), lambda i: (i, 0))
    flops = 4 * count * total_keys * width + 4 * total_keys * width * width
    flops += 2 * count * width * width
    return pl.pallas_call(
        functools.partial(attention_kernel, scale),
        out_shape=(
            jax.ShapeDtypeStruct((count, width), jnp.bfloat16),
            jax.ShapeDtypeStruct((count, width), jnp.bfloat16),
        ),
        grid=(count // block,),
        in_specs=[
            full((total_keys, width)),
            rows_of,
            rows_of,
            full((1, width)),
            full((width, width)),
            full((width, width)),
            full((width, width)),
            full((1, width)),
        ],
        out_specs=(rows_of, rows_of),
        scratch_shapes=[
            pltpu.VMEM((total_keys, width), jnp.bfloat16),
            pltpu.VMEM((total_keys, width), jnp.bfloat16),
        ],
        compiler_params=pltpu.CompilerParams(vmem_limit_bytes=60 * 1024 * 1024),
        cost_estimate=pl.CostEstimate(
            flops=flops,
            transcendentals=count * total_keys + count * width,
            bytes_accessed=2 * width * (total_keys + 4 * count + 3 * width),
        ),
    )(
        whole, flat, query, attn_gain.reshape(1, width), key_weight, value_weight, out_weight,
        conv_gain.reshape(1, width),
    )


def shards(
    frames,
    cache_frames,
    attn_gain,
    query_weight,
    key_weight,
    value_weight,
    out_weight,
    conv_gain,
    conv_weight,
):
    rows = frames.shape[1]
    cols = frames.shape[2]
    width = frames.shape[3]
    flat = frames.reshape(-1, width)
    count = flat.shape[0]
    scale = float(np.float32(1.0) / np.sqrt(np.float32(width)))
    whole = strip_gather(flat, "strip")
    normed = rms_scale(flat, attn_gain).astype(jnp.bfloat16)
    query = jnp.dot(normed, query_weight, preferred_element_type=jnp.float32).astype(jnp.bfloat16)
    resid, act = attend(
        whole, flat, query, attn_gain, key_weight, value_weight, out_weight, conv_gain, scale
    )
    act = act.reshape(rows, cols, width)
    frame_index = lax.axis_index("tm")
    prior = passed_along(act, "tm", 1)
    prior = jnp.where(frame_index == 0, cache_frames[1], prior)
    nt = lax.axis_size("tm")
    older_even = lax.ppermute(act, "tm", [(i, i + 2) for i in range(0, nt - 2, 2)])
    older_odd = lax.ppermute(prior, "tm", [(i, i + 1) for i in range(2, nt - 1, 2)])
    older = jnp.where(frame_index % 2 == 0, older_even, older_odd)
    older = jnp.where(frame_index == 0, cache_frames[0], older)
    older = jnp.where(frame_index == 1, cache_frames[1], older)
    kernel = conv_weight.reshape(3, 3, 3 * width, width)

    def widen(frame):
        padded = jnp.pad(frame, ((1, 1), (1, 1), (0, 0)))
        return jnp.concatenate(
            [padded[:, 0:cols], padded[:, 1 : cols + 1], padded[:, 2 : cols + 2]], axis=-1
        )

    def frame_terms(wide, step_t):
        main = None
        for step_r in range(3):
            window = wide[step_r : step_r + rows].reshape(-1, 3 * width)
            part = jnp.dot(window, kernel[step_t, step_r], preferred_element_type=jnp.float32)
            main = part if main is None else main + part
        first = jnp.dot(wide[1], kernel[step_t, 2], preferred_element_type=jnp.float32)
        last = jnp.dot(wide[rows], kernel[step_t, 0], preferred_element_type=jnp.float32)
        return main, first, last

    own_main, own_first, own_last = frame_terms(widen(act), 2)
    prior_main, prior_first, prior_last = frame_terms(widen(prior), 1)
    older_main, older_first, older_last = frame_terms(widen(older), 0)
    to_prev = own_first + prior_first + older_first
    to_next = own_last + prior_last + older_last
    n = lax.axis_size("strip")
    from_next = lax.ppermute(
        to_prev.astype(jnp.bfloat16), "strip", [(i + 1, i) for i in range(n - 1)]
    )
    from_prev = lax.ppermute(
        to_next.astype(jnp.bfloat16), "strip", [(i, i + 1) for i in range(n - 1)]
    )
    result = resid.astype(jnp.float32) + own_main + prior_main + older_main
    edges = jnp.concatenate(
        [
            from_prev[None].astype(jnp.float32),
            jnp.zeros((rows - 2, cols, width), jnp.float32),
            from_next[None].astype(jnp.float32),
        ],
        axis=0,
    )
    result = result + edges.reshape(-1, width)
    return result.astype(jnp.bfloat16).reshape(1, rows, cols, width)


def solution(mesh):
    return jax.shard_map(
        shards,
        mesh=mesh,
        in_specs=(
            P(("clip", "tm"), "strip", None, None),
            P("clip", "strip", None, None),
            P(),
            P(),
            P(),
            P(),
            P(),
            P(),
            P(),
        ),
        out_specs=P(("clip", "tm"), "strip", None, None),
        check_vma=False,
    )
```

```python
import functools

import jax
import jax.numpy as jnp
import numpy as np
from jax import lax
from jax.experimental import pallas as pl
from jax.experimental.pallas import tpu as pltpu
from jax.sharding import PartitionSpec as P


def passed_along(x, axis, by):
    size = lax.axis_size(axis)
    pairs = [(i, i + by) for i in range(size) if 0 <= i + by < size]
    return lax.ppermute(x, axis, pairs)


def strip_gather(x, axis):
    n = lax.axis_size(axis)
    if n == 1:
        return x
    m = x.shape[0]
    up_pairs = [(i, i + 1) for i in range(n - 1)]
    down_pairs = [(i + 1, i) for i in range(n - 1)]
    ups, downs = [], []
    up, down = x, x
    for _ in range(n - 1):
        up = lax.ppermute(up, axis, up_pairs)
        down = lax.ppermute(down, axis, down_pairs)
        ups.append(up)
        downs.append(down)
    stacked = jnp.concatenate(ups[::-1] + [x] + downs, axis=0)
    me = lax.axis_index(axis)
    return lax.dynamic_slice_in_dim(stacked, (n - 1 - me) * m, n * m, axis=0)


def rms_scale(values, gain):
    wide = values.astype(jnp.float32)
    return wide * lax.rsqrt(jnp.mean(wide * wide, axis=-1, keepdims=True) + 1e-06) * gain


def scaled(x, gain):
    wide = x.astype(jnp.float32)
    return wide * lax.rsqrt(jnp.mean(wide * wide, axis=-1, keepdims=True) + 1e-06) * gain


def attention_kernel(
    scale, whole_ref, flat_ref, query_ref, again_ref, wk_ref, wv_ref, wo_ref, cgain_ref,
    resid_ref, act_ref, keys_ref, values_ref,
):
    @pl.when(pl.program_id(0) == 0)
    def _():
        normed_all = scaled(whole_ref[...], again_ref[...]).astype(jnp.bfloat16)
        keys_ref[...] = jnp.dot(
            normed_all, wk_ref[...], preferred_element_type=jnp.float32
        ).astype(jnp.bfloat16)
        values_ref[...] = jnp.dot(
            normed_all, wv_ref[...], preferred_element_type=jnp.float32
        ).astype(jnp.bfloat16)

    scores = (
        lax.dot_general(
            query_ref[...], keys_ref[...], (((1,), (1,)), ((), ())),
            preferred_element_type=jnp.float32,
        )
        * scale
    )
    peak = jnp.max(scores, axis=1, keepdims=True)
    weights = jnp.exp(scores - peak)
    total = jnp.sum(weights, axis=1, keepdims=True)
    summed = jnp.dot(
        weights.astype(jnp.bfloat16), values_ref[...], preferred_element_type=jnp.float32
    )
    attended = (summed / total).astype(jnp.bfloat16)
    resid = (
        flat_ref[...].astype(jnp.float32)
        + jnp.dot(attended, wo_ref[...], preferred_element_type=jnp.float32)
    ).astype(jnp.bfloat16)
    resid_ref[...] = resid
    shown = scaled(resid, cgain_ref[...])
    act_ref[...] = (shown / (1.0 + jnp.exp(-shown))).astype(jnp.bfloat16)


def attend(whole, flat, query, attn_gain, key_weight, value_weight, out_weight, conv_gain, scale):
    count, width = query.shape
    total_keys = whole.shape[0]
    block = 160 if count % 160 == 0 and count * total_keys > 2 ** 21 else count
    full = lambda shape: pl.BlockSpec(shape, lambda i: (0, 0))
    rows_of = pl.BlockSpec((block, width), lambda i: (i, 0))
    flops = 4 * count * total_keys * width + 4 * total_keys * width * width
    flops += 2 * count * width * width
    return pl.pallas_call(
        functools.partial(attention_kernel, scale),
        out_shape=(
            jax.ShapeDtypeStruct((count, width), jnp.bfloat16),
            jax.ShapeDtypeStruct((count, width), jnp.bfloat16),
        ),
        grid=(count // block,),
        in_specs=[
            full((total_keys, width)),
            rows_of,
            rows_of,
            full((1, width)),
            full((width, width)),
            full((width, width)),
            full((width, width)),
            full((1, width)),
        ],
        out_specs=(rows_of, rows_of),
        scratch_shapes=[
            pltpu.VMEM((total_keys, width), jnp.bfloat16),
            pltpu.VMEM((total_keys, width), jnp.bfloat16),
        ],
        compiler_params=pltpu.CompilerParams(vmem_limit_bytes=60 * 1024 * 1024),
        cost_estimate=pl.CostEstimate(
            flops=flops,
            transcendentals=count * total_keys + count * width,
            bytes_accessed=2 * width * (total_keys + 4 * count + 3 * width),
        ),
    )(
        whole, flat, query, attn_gain.reshape(1, width), key_weight, value_weight, out_weight,
        conv_gain.reshape(1, width),
    )


def shards(
    frames,
    cache_frames,
    attn_gain,
    query_weight,
    key_weight,
    value_weight,
    out_weight,
    conv_gain,
    conv_weight,
):
    rows = frames.shape[1]
    cols = frames.shape[2]
    width = frames.shape[3]
    flat = frames.reshape(-1, width)
    count = flat.shape[0]
    scale = float(np.float32(1.0) / np.sqrt(np.float32(width)))
    whole = strip_gather(flat, "strip")
    normed = rms_scale(flat, attn_gain).astype(jnp.bfloat16)
    query = jnp.dot(normed, query_weight, preferred_element_type=jnp.float32).astype(jnp.bfloat16)
    resid, act = attend(
        whole, flat, query, attn_gain, key_weight, value_weight, out_weight, conv_gain, scale
    )
    act = act.reshape(rows, cols, width)
    frame_index = lax.axis_index("tm")
    prior = passed_along(act, "tm", 1)
    prior = jnp.where(frame_index == 0, cache_frames[1], prior)
    older = passed_along(prior, "tm", 1)
    older = jnp.where(frame_index == 0, cache_frames[0], older)
    kernel = conv_weight.reshape(3, 3, 3 * width, width)

    def widen(frame):
        padded = jnp.pad(frame, ((1, 1), (1, 1), (0, 0)))
        return jnp.concatenate(
            [padded[:, 0:cols], padded[:, 1 : cols + 1], padded[:, 2 : cols + 2]], axis=-1
        )

    def frame_terms(wide, step_t):
        main = None
        for step_r in range(3):
            window = wide[step_r : step_r + rows].reshape(-1, 3 * width)
            part = jnp.dot(window, kernel[step_t, step_r], preferred_element_type=jnp.float32)
            main = part if main is None else main + part
        first = jnp.dot(wide[1], kernel[step_t, 2], preferred_element_type=jnp.float32)
        last = jnp.dot(wide[rows], kernel[step_t, 0], preferred_element_type=jnp.float32)
        return main, first, last

    own_main, own_first, own_last = frame_terms(widen(act), 2)
    prior_main, prior_first, prior_last = frame_terms(widen(prior), 1)
    older_main, older_first, older_last = frame_terms(widen(older), 0)
    to_prev = own_first + prior_first + older_first
    to_next = own_last + prior_last + older_last
    n = lax.axis_size("strip")
    from_next = lax.ppermute(
        to_prev.astype(jnp.bfloat16), "strip", [(i + 1, i) for i in range(n - 1)]
    )
    from_prev = lax.ppermute(
        to_next.astype(jnp.bfloat16), "strip", [(i, i + 1) for i in range(n - 1)]
    )
    result = resid.astype(jnp.float32) + own_main + prior_main + older_main
    edges = jnp.concatenate(
        [
            from_prev[None].astype(jnp.float32),
            jnp.zeros((rows - 2, cols, width), jnp.float32),
            from_next[None].astype(jnp.float32),
        ],
        axis=0,
    )
    result = result + edges.reshape(-1, width)
    return result.astype(jnp.bfloat16).reshape(1, rows, cols, width)


def solution(mesh):
    return jax.shard_map(
        shards,
        mesh=mesh,
        in_specs=(
            P(("clip", "tm"), "strip", None, None),
            P("clip", "strip", None, None),
            P(),
            P(),
            P(),
            P(),
            P(),
            P(),
            P(),
        ),
        out_specs=P(("clip", "tm"), "strip", None, None),
        check_vma=False,
    )
```

```python
import functools

import jax
import jax.numpy as jnp
import numpy as np
from jax import lax
from jax.experimental import pallas as pl
from jax.experimental.pallas import tpu as pltpu
from jax.sharding import PartitionSpec as P


def passed_along(x, axis, by):
    size = lax.axis_size(axis)
    pairs = [(i, i + by) for i in range(size) if 0 <= i + by < size]
    return lax.ppermute(x, axis, pairs)


def strip_gather(x, axis):
    n = lax.axis_size(axis)
    if n == 1:
        return x
    m = x.shape[0]
    ups, downs = [], []
    up, down = x, x
    for step in range(1, n):
        up = lax.ppermute(up, axis, [(i, i + 1) for i in range(step - 1, n - 1)])
        down = lax.ppermute(down, axis, [(i + 1, i) for i in range(0, n - step)])
        ups.append(up)
        downs.append(down)
    stacked = jnp.concatenate(ups[::-1] + [x] + downs, axis=0)
    me = lax.axis_index(axis)
    return lax.dynamic_slice_in_dim(stacked, (n - 1 - me) * m, n * m, axis=0)


def rms_scale(values, gain):
    wide = values.astype(jnp.float32)
    return wide * lax.rsqrt(jnp.mean(wide * wide, axis=-1, keepdims=True) + 1e-06) * gain


def scaled(x, gain):
    wide = x.astype(jnp.float32)
    return wide * lax.rsqrt(jnp.mean(wide * wide, axis=-1, keepdims=True) + 1e-06) * gain


def attention_kernel(
    scale, whole_ref, flat_ref, query_ref, again_ref, wkv_ref, wo_ref, cgain_ref,
    resid_ref, act_ref, keys_ref, values_ref,
):
    @pl.when(pl.program_id(0) == 0)
    def _():
        normed_all = scaled(whole_ref[...], again_ref[...]).astype(jnp.bfloat16)
        both = jnp.dot(
            normed_all, wkv_ref[...], preferred_element_type=jnp.float32
        ).astype(jnp.bfloat16)
        width = keys_ref.shape[1]
        keys_ref[...] = both[:, :width]
        values_ref[...] = both[:, width:]

    scores = (
        lax.dot_general(
            query_ref[...], keys_ref[...], (((1,), (1,)), ((), ())),
            preferred_element_type=jnp.float32,
        )
        * scale
    )
    peak = jnp.max(scores, axis=1, keepdims=True)
    weights = jnp.exp(scores - peak)
    total = jnp.sum(weights, axis=1, keepdims=True)
    summed = jnp.dot(
        weights.astype(jnp.bfloat16), values_ref[...], preferred_element_type=jnp.float32
    )
    attended = (summed / total).astype(jnp.bfloat16)
    resid = (
        flat_ref[...].astype(jnp.float32)
        + jnp.dot(attended, wo_ref[...], preferred_element_type=jnp.float32)
    ).astype(jnp.bfloat16)
    resid_ref[...] = resid
    shown = scaled(resid, cgain_ref[...])
    act_ref[...] = (shown / (1.0 + jnp.exp(-shown))).astype(jnp.bfloat16)


def attend(whole, flat, query, attn_gain, key_weight, value_weight, out_weight, conv_gain, scale):
    count, width = query.shape
    total_keys = whole.shape[0]
    block = 160 if count % 160 == 0 and count * total_keys > 2 ** 21 else count
    full = lambda shape: pl.BlockSpec(shape, lambda i: (0, 0))
    rows_of = pl.BlockSpec((block, width), lambda i: (i, 0))
    flops = 4 * count * total_keys * width + 4 * total_keys * width * width
    flops += 2 * count * width * width
    return pl.pallas_call(
        functools.partial(attention_kernel, scale),
        out_shape=(
            jax.ShapeDtypeStruct((count, width), jnp.bfloat16),
            jax.ShapeDtypeStruct((count, width), jnp.bfloat16),
        ),
        grid=(count // block,),
        in_specs=[
            full((total_keys, width)),
            rows_of,
            rows_of,
            full((1, width)),
            full((width, 2 * width)),
            full((width, width)),
            full((1, width)),
        ],
        out_specs=(rows_of, rows_of),
        scratch_shapes=[
            pltpu.VMEM((total_keys, width), jnp.bfloat16),
            pltpu.VMEM((total_keys, width), jnp.bfloat16),
        ],
        compiler_params=pltpu.CompilerParams(vmem_limit_bytes=60 * 1024 * 1024),
        cost_estimate=pl.CostEstimate(
            flops=flops,
            transcendentals=count * total_keys + count * width,
            bytes_accessed=2 * width * (total_keys + 4 * count + 3 * width),
        ),
    )(
        whole, flat, query, attn_gain.reshape(1, width),
        jnp.concatenate([key_weight, value_weight], axis=1), out_weight,
        conv_gain.reshape(1, width),
    )


def shards(
    frames,
    cache_frames,
    attn_gain,
    query_weight,
    key_weight,
    value_weight,
    out_weight,
    conv_gain,
    conv_weight,
):
    rows = frames.shape[1]
    cols = frames.shape[2]
    width = frames.shape[3]
    flat = frames.reshape(-1, width)
    count = flat.shape[0]
    scale = float(np.float32(1.0) / np.sqrt(np.float32(width)))
    whole = strip_gather(flat, "strip")
    normed = rms_scale(flat, attn_gain).astype(jnp.bfloat16)
    query = jnp.dot(normed, query_weight, preferred_element_type=jnp.float32).astype(jnp.bfloat16)
    resid, act = attend(
        whole, flat, query, attn_gain, key_weight, value_weight, out_weight, conv_gain, scale
    )
    act = act.reshape(rows, cols, width)
    frame_index = lax.axis_index("tm")
    prior = passed_along(act, "tm", 1)
    prior = jnp.where(frame_index == 0, cache_frames[1], prior)
    older = passed_along(prior, "tm", 1)
    older = jnp.where(frame_index == 0, cache_frames[0], older)
    kernel = conv_weight.reshape(3, 3, 3 * width, width)

    def widen(frame):
        padded = jnp.pad(frame, ((1, 1), (1, 1), (0, 0)))
        return jnp.concatenate(
            [padded[:, 0:cols], padded[:, 1 : cols + 1], padded[:, 2 : cols + 2]], axis=-1
        )

    def frame_terms(wide, step_t):
        main = None
        for step_r in range(3):
            window = wide[step_r : step_r + rows].reshape(-1, 3 * width)
            part = jnp.dot(window, kernel[step_t, step_r], preferred_element_type=jnp.float32)
            main = part if main is None else main + part
        first = jnp.dot(wide[1], kernel[step_t, 2], preferred_element_type=jnp.float32)
        last = jnp.dot(wide[rows], kernel[step_t, 0], preferred_element_type=jnp.float32)
        return main, first, last

    own_main, own_first, own_last = frame_terms(widen(act), 2)
    prior_main, prior_first, prior_last = frame_terms(widen(prior), 1)
    older_main, older_first, older_last = frame_terms(widen(older), 0)
    to_prev = own_first + prior_first + older_first
    to_next = own_last + prior_last + older_last
    n = lax.axis_size("strip")
    from_next = lax.ppermute(
        to_prev.astype(jnp.bfloat16), "strip", [(i + 1, i) for i in range(n - 1)]
    )
    from_prev = lax.ppermute(
        to_next.astype(jnp.bfloat16), "strip", [(i, i + 1) for i in range(n - 1)]
    )
    result = resid.astype(jnp.float32) + own_main + prior_main + older_main
    edges = jnp.concatenate(
        [
            from_prev[None].astype(jnp.float32),
            jnp.zeros((rows - 2, cols, width), jnp.float32),
            from_next[None].astype(jnp.float32),
        ],
        axis=0,
    )
    result = result + edges.reshape(-1, width)
    return result.astype(jnp.bfloat16).reshape(1, rows, cols, width)


def solution(mesh):
    return jax.shard_map(
        shards,
        mesh=mesh,
        in_specs=(
            P(("clip", "tm"), "strip", None, None),
            P("clip", "strip", None, None),
            P(),
            P(),
            P(),
            P(),
            P(),
            P(),
            P(),
        ),
        out_specs=P(("clip", "tm"), "strip", None, None),
        check_vma=False,
    )
```

```python
import functools

import jax
import jax.numpy as jnp
import numpy as np
from jax import lax
from jax.experimental import pallas as pl
from jax.experimental.pallas import tpu as pltpu
from jax.sharding import PartitionSpec as P


def passed_along(x, axis, by):
    size = lax.axis_size(axis)
    pairs = [(i, i + by) for i in range(size) if 0 <= i + by < size]
    return lax.ppermute(x, axis, pairs)


def relay(x, axis):
    n = lax.axis_size(axis)
    ups, downs = [], []
    up, down = x, x
    for step in range(1, n):
        up = lax.ppermute(up, axis, [(i, i + 1) for i in range(step - 1, n - 1)])
        down = lax.ppermute(down, axis, [(i + 1, i) for i in range(0, n - step)])
        ups.append(up)
        downs.append(down)
    return ups, downs


def strip_gather(x, axis):
    n = lax.axis_size(axis)
    if n == 1:
        return x
    m = x.shape[0]
    ups, downs = [], []
    up, down = x, x
    for step in range(1, n):
        up = lax.ppermute(up, axis, [(i, i + 1) for i in range(step - 1, n - 1)])
        down = lax.ppermute(down, axis, [(i + 1, i) for i in range(0, n - step)])
        ups.append(up)
        downs.append(down)
    stacked = jnp.concatenate(ups[::-1] + [x] + downs, axis=0)
    me = lax.axis_index(axis)
    return lax.dynamic_slice_in_dim(stacked, (n - 1 - me) * m, n * m, axis=0)


def rms_scale(values, gain):
    wide = values.astype(jnp.float32)
    return wide * lax.rsqrt(jnp.mean(wide * wide, axis=-1, keepdims=True) + 1e-06) * gain


def scaled(x, gain):
    wide = x.astype(jnp.float32)
    return wide * lax.rsqrt(jnp.mean(wide * wide, axis=-1, keepdims=True) + 1e-06) * gain


def attention_kernel(
    scale, whole_ref, flat_ref, query_ref, again_ref, wkv_ref, wo_ref, cgain_ref,
    resid_ref, act_ref, keys_ref, values_ref,
):
    @pl.when(pl.program_id(0) == 0)
    def _():
        normed_all = scaled(whole_ref[...], again_ref[...]).astype(jnp.bfloat16)
        both = jnp.dot(
            normed_all, wkv_ref[...], preferred_element_type=jnp.float32
        ).astype(jnp.bfloat16)
        width = keys_ref.shape[1]
        keys_ref[...] = both[:, :width]
        values_ref[...] = both[:, width:]

    scores = (
        lax.dot_general(
            query_ref[...], keys_ref[...], (((1,), (1,)), ((), ())),
            preferred_element_type=jnp.float32,
        )
        * scale
    )
    peak = jnp.max(scores, axis=1, keepdims=True)
    weights = jnp.exp(scores - peak)
    total = jnp.sum(weights, axis=1, keepdims=True)
    summed = jnp.dot(
        weights.astype(jnp.bfloat16), values_ref[...], preferred_element_type=jnp.float32
    )
    attended = (summed / total).astype(jnp.bfloat16)
    resid = (
        flat_ref[...].astype(jnp.float32)
        + jnp.dot(attended, wo_ref[...], preferred_element_type=jnp.float32)
    ).astype(jnp.bfloat16)
    resid_ref[...] = resid
    shown = scaled(resid, cgain_ref[...])
    act_ref[...] = (shown / (1.0 + jnp.exp(-shown))).astype(jnp.bfloat16)


def attend(whole, flat, query, attn_gain, key_weight, value_weight, out_weight, conv_gain, scale):
    count, width = query.shape
    total_keys = whole.shape[0]
    block = 160 if count % 160 == 0 and count * total_keys > 2 ** 21 else count
    full = lambda shape: pl.BlockSpec(shape, lambda i: (0, 0))
    rows_of = pl.BlockSpec((block, width), lambda i: (i, 0))
    flops = 4 * count * total_keys * width + 4 * total_keys * width * width
    flops += 2 * count * width * width
    return pl.pallas_call(
        functools.partial(attention_kernel, scale),
        out_shape=(
            jax.ShapeDtypeStruct((count, width), jnp.bfloat16),
            jax.ShapeDtypeStruct((count, width), jnp.bfloat16),
        ),
        grid=(count // block,),
        in_specs=[
            full((total_keys, width)),
            rows_of,
            rows_of,
            full((1, width)),
            full((width, 2 * width)),
            full((width, width)),
            full((1, width)),
        ],
        out_specs=(rows_of, rows_of),
        scratch_shapes=[
            pltpu.VMEM((total_keys, width), jnp.bfloat16),
            pltpu.VMEM((total_keys, width), jnp.bfloat16),
        ],
        compiler_params=pltpu.CompilerParams(vmem_limit_bytes=60 * 1024 * 1024),
        cost_estimate=pl.CostEstimate(
            flops=flops,
            transcendentals=count * total_keys + count * width,
            bytes_accessed=2 * width * (total_keys + 4 * count + 3 * width),
        ),
    )(
        whole, flat, query, attn_gain.reshape(1, width),
        jnp.concatenate([key_weight, value_weight], axis=1), out_weight,
        conv_gain.reshape(1, width),
    )


def split_kernels_a(scale, blocks_ref, query_ref, again_ref, wkv_ref, bias_ref, m_ref, l_ref, o_ref):
    width = query_ref.shape[1]
    normed = scaled(blocks_ref[...], again_ref[...]).astype(jnp.bfloat16)
    both = jnp.dot(normed, wkv_ref[...], preferred_element_type=jnp.float32).astype(jnp.bfloat16)
    scores = (
        lax.dot_general(
            query_ref[...], both[:, :width], (((1,), (1,)), ((), ())),
            preferred_element_type=jnp.float32,
        )
        * scale
        + bias_ref[...]
    )
    peak = jnp.max(scores, axis=1, keepdims=True)
    weights = jnp.exp(scores - peak)
    m_ref[...] = peak
    l_ref[...] = jnp.sum(weights, axis=1, keepdims=True)
    o_ref[...] = jnp.dot(
        weights.astype(jnp.bfloat16), both[:, width:], preferred_element_type=jnp.float32
    )


def split_kernels_b(
    scale, blocks_ref, query_ref, again_ref, wkv_ref, bias_ref, m_ref, l_ref, o_ref, flat_ref,
    wo_ref, cgain_ref, resid_ref, act_ref,
):
    width = query_ref.shape[1]
    normed = scaled(blocks_ref[...], again_ref[...]).astype(jnp.bfloat16)
    both = jnp.dot(normed, wkv_ref[...], preferred_element_type=jnp.float32).astype(jnp.bfloat16)
    scores = (
        lax.dot_general(
            query_ref[...], both[:, :width], (((1,), (1,)), ((), ())),
            preferred_element_type=jnp.float32,
        )
        * scale
        + bias_ref[...]
    )
    earlier = m_ref[...]
    peak = jnp.maximum(jnp.max(scores, axis=1, keepdims=True), earlier)
    alpha = jnp.exp(earlier - peak)
    weights = jnp.exp(scores - peak)
    total = l_ref[...] * alpha + jnp.sum(weights, axis=1, keepdims=True)
    summed = o_ref[...] * alpha + jnp.dot(
        weights.astype(jnp.bfloat16), both[:, width:], preferred_element_type=jnp.float32
    )
    attended = (summed / total).astype(jnp.bfloat16)
    resid = (
        flat_ref[...].astype(jnp.float32)
        + jnp.dot(attended, wo_ref[...], preferred_element_type=jnp.float32)
    ).astype(jnp.bfloat16)
    resid_ref[...] = resid
    shown = scaled(resid, cgain_ref[...])
    act_ref[...] = (shown / (1.0 + jnp.exp(-shown))).astype(jnp.bfloat16)


def whole_call(kernel, inputs, outputs, flops, transcendentals):
    return pl.pallas_call(
        kernel,
        out_shape=outputs,
        grid=(1,),
        in_specs=[pl.BlockSpec(x.shape, lambda i: (0, 0)) for x in inputs],
        out_specs=tuple(pl.BlockSpec(o.shape, lambda i: (0, 0)) for o in outputs),
        compiler_params=pltpu.CompilerParams(vmem_limit_bytes=60 * 1024 * 1024),
        cost_estimate=pl.CostEstimate(
            flops=flops,
            transcendentals=transcendentals,
            bytes_accessed=sum(x.size * x.dtype.itemsize for x in inputs),
        ),
    )(*inputs)


def split_attend(
    blocks_a, bias_a, blocks_b, bias_b, flat, query, attn_gain, key_weight, value_weight,
    out_weight, conv_gain, scale,
):
    count, width = query.shape
    wkv = jnp.concatenate([key_weight, value_weight], axis=1)
    again = attn_gain.reshape(1, width)
    f32 = jnp.float32
    keys_a, keys_b = blocks_a.shape[0], blocks_b.shape[0]
    m_a, l_a, o_a = whole_call(
        functools.partial(split_kernels_a, scale),
        [blocks_a, query, again, wkv, bias_a],
        (
            jax.ShapeDtypeStruct((count, 1), f32),
            jax.ShapeDtypeStruct((count, 1), f32),
            jax.ShapeDtypeStruct((count, width), f32),
        ),
        4 * keys_a * width * width + 4 * count * keys_a * width,
        count * keys_a,
    )
    return whole_call(
        functools.partial(split_kernels_b, scale),
        [blocks_b, query, again, wkv, bias_b, m_a, l_a, o_a, flat, out_weight,
         conv_gain.reshape(1, width)],
        (
            jax.ShapeDtypeStruct((count, width), jnp.bfloat16),
            jax.ShapeDtypeStruct((count, width), jnp.bfloat16),
        ),
        4 * keys_b * width * width + 4 * count * keys_b * width + 2 * count * width * width,
        count * keys_b + count * width,
    )


def shards(
    frames,
    cache_frames,
    attn_gain,
    query_weight,
    key_weight,
    value_weight,
    out_weight,
    conv_gain,
    conv_weight,
):
    rows = frames.shape[1]
    cols = frames.shape[2]
    width = frames.shape[3]
    flat = frames.reshape(-1, width)
    count = flat.shape[0]
    scale = float(np.float32(1.0) / np.sqrt(np.float32(width)))
    n = lax.axis_size("strip")
    split_path = 3 <= n <= 4
    if not split_path:
        whole = strip_gather(flat, "strip")
    normed = rms_scale(flat, attn_gain).astype(jnp.bfloat16)
    query = jnp.dot(normed, query_weight, preferred_element_type=jnp.float32).astype(jnp.bfloat16)
    if split_path:
        me = lax.axis_index("strip")
        ups, downs = relay(flat, "strip")
        early = range(1, n - 1)
        blocks_a = [ups[k - 1] for k in early[::-1]] + [flat] + [downs[k - 1] for k in early]
        valid_a = [me >= k for k in early[::-1]] + [me >= 0] + [me <= n - 1 - k for k in early]
        blocks_b = [ups[n - 2], downs[n - 2]]
        valid_b = [me >= n - 1, me <= 0]

        def bias(valid):
            rows_of = [jnp.broadcast_to(jnp.where(v, 0.0, -1e30), (count,)) for v in valid]
            return jnp.concatenate(rows_of).astype(jnp.float32).reshape(1, -1)

        resid, act = split_attend(
            jnp.concatenate(blocks_a, axis=0), bias(valid_a), jnp.concatenate(blocks_b, axis=0),
            bias(valid_b), flat, query, attn_gain, key_weight, value_weight, out_weight,
            conv_gain, scale,
        )
    else:
        resid, act = attend(
            whole, flat, query, attn_gain, key_weight, value_weight, out_weight, conv_gain, scale
        )
    act = act.reshape(rows, cols, width)
    frame_index = lax.axis_index("tm")
    prior = passed_along(act, "tm", 1)
    prior = jnp.where(frame_index == 0, cache_frames[1], prior)
    older = passed_along(prior, "tm", 1)
    older = jnp.where(frame_index == 0, cache_frames[0], older)
    kernel = conv_weight.reshape(3, 3, 3 * width, width)

    def widen(frame):
        padded = jnp.pad(frame, ((1, 1), (1, 1), (0, 0)))
        return jnp.concatenate(
            [padded[:, 0:cols], padded[:, 1 : cols + 1], padded[:, 2 : cols + 2]], axis=-1
        )

    def frame_terms(wide, step_t):
        main = None
        for step_r in range(3):
            window = wide[step_r : step_r + rows].reshape(-1, 3 * width)
            part = jnp.dot(window, kernel[step_t, step_r], preferred_element_type=jnp.float32)
            main = part if main is None else main + part
        first = jnp.dot(wide[1], kernel[step_t, 2], preferred_element_type=jnp.float32)
        last = jnp.dot(wide[rows], kernel[step_t, 0], preferred_element_type=jnp.float32)
        return main, first, last

    own_main, own_first, own_last = frame_terms(widen(act), 2)
    prior_main, prior_first, prior_last = frame_terms(widen(prior), 1)
    older_main, older_first, older_last = frame_terms(widen(older), 0)
    to_prev = own_first + prior_first + older_first
    to_next = own_last + prior_last + older_last
    n = lax.axis_size("strip")
    from_next = lax.ppermute(
        to_prev.astype(jnp.bfloat16), "strip", [(i + 1, i) for i in range(n - 1)]
    )
    from_prev = lax.ppermute(
        to_next.astype(jnp.bfloat16), "strip", [(i, i + 1) for i in range(n - 1)]
    )
    result = resid.astype(jnp.float32) + own_main + prior_main + older_main
    edges = jnp.concatenate(
        [
            from_prev[None].astype(jnp.float32),
            jnp.zeros((rows - 2, cols, width), jnp.float32),
            from_next[None].astype(jnp.float32),
        ],
        axis=0,
    )
    result = result + edges.reshape(-1, width)
    return result.astype(jnp.bfloat16).reshape(1, rows, cols, width)


def solution(mesh):
    return jax.shard_map(
        shards,
        mesh=mesh,
        in_specs=(
            P(("clip", "tm"), "strip", None, None),
            P("clip", "strip", None, None),
            P(),
            P(),
            P(),
            P(),
            P(),
            P(),
            P(),
        ),
        out_specs=P(("clip", "tm"), "strip", None, None),
        check_vma=False,
    )
```

```python
import functools

import jax
import jax.numpy as jnp
import numpy as np
from jax import lax
from jax.experimental import pallas as pl
from jax.experimental.pallas import tpu as pltpu
from jax.sharding import PartitionSpec as P


def passed_along(x, axis, by):
    size = lax.axis_size(axis)
    pairs = [(i, i + by) for i in range(size) if 0 <= i + by < size]
    return lax.ppermute(x, axis, pairs)


def relay(x, axis):
    n = lax.axis_size(axis)
    ups, downs = [], []
    up, down = x, x
    for step in range(1, n):
        up = lax.ppermute(up, axis, [(i, i + 1) for i in range(step - 1, n - 1)])
        down = lax.ppermute(down, axis, [(i + 1, i) for i in range(0, n - step)])
        ups.append(up)
        downs.append(down)
    return ups, downs


def strip_gather(x, axis):
    n = lax.axis_size(axis)
    if n == 1:
        return x
    m = x.shape[0]
    ups, downs = [], []
    up, down = x, x
    for step in range(1, n):
        up = lax.ppermute(up, axis, [(i, i + 1) for i in range(step - 1, n - 1)])
        down = lax.ppermute(down, axis, [(i + 1, i) for i in range(0, n - step)])
        ups.append(up)
        downs.append(down)
    stacked = jnp.concatenate(ups[::-1] + [x] + downs, axis=0)
    me = lax.axis_index(axis)
    return lax.dynamic_slice_in_dim(stacked, (n - 1 - me) * m, n * m, axis=0)


def rms_scale(values, gain):
    wide = values.astype(jnp.float32)
    return wide * lax.rsqrt(jnp.mean(wide * wide, axis=-1, keepdims=True) + 1e-06) * gain


def scaled(x, gain):
    wide = x.astype(jnp.float32)
    return wide * lax.rsqrt(jnp.mean(wide * wide, axis=-1, keepdims=True) + 1e-06) * gain


def attention_kernel(
    scale, whole_ref, flat_ref, query_ref, again_ref, wkv_ref, wo_ref, cgain_ref,
    resid_ref, act_ref, keys_ref, values_ref,
):
    @pl.when(pl.program_id(0) == 0)
    def _():
        normed_all = scaled(whole_ref[...], again_ref[...]).astype(jnp.bfloat16)
        both = jnp.dot(
            normed_all, wkv_ref[...], preferred_element_type=jnp.float32
        ).astype(jnp.bfloat16)
        width = keys_ref.shape[1]
        keys_ref[...] = both[:, :width]
        values_ref[...] = both[:, width:]

    scores = (
        lax.dot_general(
            query_ref[...], keys_ref[...], (((1,), (1,)), ((), ())),
            preferred_element_type=jnp.float32,
        )
        * scale
    )
    peak = jnp.max(scores, axis=1, keepdims=True)
    weights = jnp.exp(scores - peak)
    total = jnp.sum(weights, axis=1, keepdims=True)
    summed = jnp.dot(
        weights.astype(jnp.bfloat16), values_ref[...], preferred_element_type=jnp.float32
    )
    attended = (summed / total).astype(jnp.bfloat16)
    resid = (
        flat_ref[...].astype(jnp.float32)
        + jnp.dot(attended, wo_ref[...], preferred_element_type=jnp.float32)
    ).astype(jnp.bfloat16)
    resid_ref[...] = resid
    shown = scaled(resid, cgain_ref[...])
    act_ref[...] = (shown / (1.0 + jnp.exp(-shown))).astype(jnp.bfloat16)


def attend(whole, flat, query, attn_gain, key_weight, value_weight, out_weight, conv_gain, scale):
    count, width = query.shape
    total_keys = whole.shape[0]
    block = 160 if count % 160 == 0 and count * total_keys > 2 ** 21 else count
    full = lambda shape: pl.BlockSpec(shape, lambda i: (0, 0))
    rows_of = pl.BlockSpec((block, width), lambda i: (i, 0))
    flops = 4 * count * total_keys * width + 4 * total_keys * width * width
    flops += 2 * count * width * width
    return pl.pallas_call(
        functools.partial(attention_kernel, scale),
        out_shape=(
            jax.ShapeDtypeStruct((count, width), jnp.bfloat16),
            jax.ShapeDtypeStruct((count, width), jnp.bfloat16),
        ),
        grid=(count // block,),
        in_specs=[
            full((total_keys, width)),
            rows_of,
            rows_of,
            full((1, width)),
            full((width, 2 * width)),
            full((width, width)),
            full((1, width)),
        ],
        out_specs=(rows_of, rows_of),
        scratch_shapes=[
            pltpu.VMEM((total_keys, width), jnp.bfloat16),
            pltpu.VMEM((total_keys, width), jnp.bfloat16),
        ],
        compiler_params=pltpu.CompilerParams(vmem_limit_bytes=60 * 1024 * 1024),
        cost_estimate=pl.CostEstimate(
            flops=flops,
            transcendentals=count * total_keys + count * width,
            bytes_accessed=2 * width * (total_keys + 4 * count + 3 * width),
        ),
    )(
        whole, flat, query, attn_gain.reshape(1, width),
        jnp.concatenate([key_weight, value_weight], axis=1), out_weight,
        conv_gain.reshape(1, width),
    )


def split_kernels_a(scale, count, *refs):
    blocks = refs[:count]
    query_ref, again_ref, wkv_ref, bias_ref, m_ref, l_ref, o_ref, kv_ref = refs[count:]
    width = query_ref.shape[1]
    rows = blocks[0].shape[0]
    for index, block_ref in enumerate(blocks):
        normed = scaled(block_ref[...], again_ref[...]).astype(jnp.bfloat16)
        kv_ref[index * rows : (index + 1) * rows, :] = jnp.dot(
            normed, wkv_ref[...], preferred_element_type=jnp.float32
        ).astype(jnp.bfloat16)
    both = kv_ref[...]
    scores = (
        lax.dot_general(
            query_ref[...], both[:, :width], (((1,), (1,)), ((), ())),
            preferred_element_type=jnp.float32,
        )
        * scale
        + bias_ref[...]
    )
    peak = jnp.max(scores, axis=1, keepdims=True)
    weights = jnp.exp(scores - peak)
    m_ref[...] = peak
    l_ref[...] = jnp.sum(weights, axis=1, keepdims=True)
    o_ref[...] = jnp.dot(
        weights.astype(jnp.bfloat16), both[:, width:], preferred_element_type=jnp.float32
    )


def split_kernels_b(
    scale, blocks_ref, query_ref, again_ref, wkv_ref, bias_ref, m_ref, l_ref, o_ref, flat_ref,
    wo_ref, cgain_ref, resid_ref, act_ref,
):
    width = query_ref.shape[1]
    normed = scaled(blocks_ref[...], again_ref[...]).astype(jnp.bfloat16)
    both = jnp.dot(normed, wkv_ref[...], preferred_element_type=jnp.float32).astype(jnp.bfloat16)
    scores = (
        lax.dot_general(
            query_ref[...], both[:, :width], (((1,), (1,)), ((), ())),
            preferred_element_type=jnp.float32,
        )
        * scale
        + bias_ref[...]
    )
    earlier = m_ref[...]
    peak = jnp.maximum(jnp.max(scores, axis=1, keepdims=True), earlier)
    alpha = jnp.exp(earlier - peak)
    weights = jnp.exp(scores - peak)
    total = l_ref[...] * alpha + jnp.sum(weights, axis=1, keepdims=True)
    summed = o_ref[...] * alpha + jnp.dot(
        weights.astype(jnp.bfloat16), both[:, width:], preferred_element_type=jnp.float32
    )
    attended = (summed / total).astype(jnp.bfloat16)
    resid = (
        flat_ref[...].astype(jnp.float32)
        + jnp.dot(attended, wo_ref[...], preferred_element_type=jnp.float32)
    ).astype(jnp.bfloat16)
    resid_ref[...] = resid
    shown = scaled(resid, cgain_ref[...])
    act_ref[...] = (shown / (1.0 + jnp.exp(-shown))).astype(jnp.bfloat16)


def whole_call(kernel, inputs, outputs, flops, transcendentals, scratch=()):
    return pl.pallas_call(
        kernel,
        out_shape=outputs,
        grid=(1,),
        in_specs=[pl.BlockSpec(x.shape, lambda i: (0, 0)) for x in inputs],
        out_specs=tuple(pl.BlockSpec(o.shape, lambda i: (0, 0)) for o in outputs),
        scratch_shapes=list(scratch),
        compiler_params=pltpu.CompilerParams(vmem_limit_bytes=60 * 1024 * 1024),
        cost_estimate=pl.CostEstimate(
            flops=flops,
            transcendentals=transcendentals,
            bytes_accessed=sum(x.size * x.dtype.itemsize for x in inputs),
        ),
    )(*inputs)


def split_attend(
    blocks_a, bias_a, blocks_b, bias_b, flat, query, attn_gain, key_weight, value_weight,
    out_weight, conv_gain, scale,
):
    count, width = query.shape
    wkv = jnp.concatenate([key_weight, value_weight], axis=1)
    again = attn_gain.reshape(1, width)
    f32 = jnp.float32
    keys_a, keys_b = count * len(blocks_a), blocks_b.shape[0]
    m_a, l_a, o_a = whole_call(
        functools.partial(split_kernels_a, scale, len(blocks_a)),
        list(blocks_a) + [query, again, wkv, bias_a],
        (
            jax.ShapeDtypeStruct((count, 1), f32),
            jax.ShapeDtypeStruct((count, 1), f32),
            jax.ShapeDtypeStruct((count, width), f32),
        ),
        4 * keys_a * width * width + 4 * count * keys_a * width,
        count * keys_a,
        [pltpu.VMEM((keys_a, 2 * width), jnp.bfloat16)],
    )
    return whole_call(
        functools.partial(split_kernels_b, scale),
        [blocks_b, query, again, wkv, bias_b, m_a, l_a, o_a, flat, out_weight,
         conv_gain.reshape(1, width)],
        (
            jax.ShapeDtypeStruct((count, width), jnp.bfloat16),
            jax.ShapeDtypeStruct((count, width), jnp.bfloat16),
        ),
        4 * keys_b * width * width + 4 * count * keys_b * width + 2 * count * width * width,
        count * keys_b + count * width,
    )


def shards(
    frames,
    cache_frames,
    attn_gain,
    query_weight,
    key_weight,
    value_weight,
    out_weight,
    conv_gain,
    conv_weight,
):
    rows = frames.shape[1]
    cols = frames.shape[2]
    width = frames.shape[3]
    flat = frames.reshape(-1, width)
    count = flat.shape[0]
    scale = float(np.float32(1.0) / np.sqrt(np.float32(width)))
    n = lax.axis_size("strip")
    split_path = n == 4
    if not split_path:
        whole = strip_gather(flat, "strip")
    normed = rms_scale(flat, attn_gain).astype(jnp.bfloat16)
    query = jnp.dot(normed, query_weight, preferred_element_type=jnp.float32).astype(jnp.bfloat16)
    if split_path:
        me = lax.axis_index("strip")
        ups, downs = relay(flat, "strip")
        far = jnp.where(me <= 1, downs[1], ups[1])
        blocks_a = [flat, ups[0], downs[0], far]
        valid_a = [me >= 0, me >= 1, me <= n - 2, me >= 0]
        blocks_b = jnp.where(me == n - 1, ups[n - 2], downs[n - 2])
        valid_b = [(me == 0) | (me == n - 1)]

        def bias(valid):
            rows_of = [jnp.broadcast_to(jnp.where(v, 0.0, -1e30), (count,)) for v in valid]
            return jnp.concatenate(rows_of).astype(jnp.float32).reshape(1, -1)

        resid, act = split_attend(
            blocks_a, bias(valid_a), blocks_b,
            bias(valid_b), flat, query, attn_gain, key_weight, value_weight, out_weight,
            conv_gain, scale,
        )
    else:
        resid, act = attend(
            whole, flat, query, attn_gain, key_weight, value_weight, out_weight, conv_gain, scale
        )
    act = act.reshape(rows, cols, width)
    frame_index = lax.axis_index("tm")
    prior = passed_along(act, "tm", 1)
    prior = jnp.where(frame_index == 0, cache_frames[1], prior)
    older = passed_along(prior, "tm", 1)
    older = jnp.where(frame_index == 0, cache_frames[0], older)
    kernel = conv_weight.reshape(3, 3, 3 * width, width)

    def widen(frame):
        padded = jnp.pad(frame, ((1, 1), (1, 1), (0, 0)))
        return jnp.concatenate(
            [padded[:, 0:cols], padded[:, 1 : cols + 1], padded[:, 2 : cols + 2]], axis=-1
        )

    def frame_terms(wide, step_t):
        main = None
        for step_r in range(3):
            window = wide[step_r : step_r + rows].reshape(-1, 3 * width)
            part = jnp.dot(window, kernel[step_t, step_r], preferred_element_type=jnp.float32)
            main = part if main is None else main + part
        first = jnp.dot(wide[1], kernel[step_t, 2], preferred_element_type=jnp.float32)
        last = jnp.dot(wide[rows], kernel[step_t, 0], preferred_element_type=jnp.float32)
        return main, first, last

    own_main, own_first, own_last = frame_terms(widen(act), 2)
    prior_main, prior_first, prior_last = frame_terms(widen(prior), 1)
    older_main, older_first, older_last = frame_terms(widen(older), 0)
    to_prev = own_first + prior_first + older_first
    to_next = own_last + prior_last + older_last
    n = lax.axis_size("strip")
    from_next = lax.ppermute(
        to_prev.astype(jnp.bfloat16), "strip", [(i + 1, i) for i in range(n - 1)]
    )
    from_prev = lax.ppermute(
        to_next.astype(jnp.bfloat16), "strip", [(i, i + 1) for i in range(n - 1)]
    )
    result = resid.astype(jnp.float32) + own_main + prior_main + older_main
    edges = jnp.concatenate(
        [
            from_prev[None].astype(jnp.float32),
            jnp.zeros((rows - 2, cols, width), jnp.float32),
            from_next[None].astype(jnp.float32),
        ],
        axis=0,
    )
    result = result + edges.reshape(-1, width)
    return result.astype(jnp.bfloat16).reshape(1, rows, cols, width)


def solution(mesh):
    return jax.shard_map(
        shards,
        mesh=mesh,
        in_specs=(
            P(("clip", "tm"), "strip", None, None),
            P("clip", "strip", None, None),
            P(),
            P(),
            P(),
            P(),
            P(),
            P(),
            P(),
        ),
        out_specs=P(("clip", "tm"), "strip", None, None),
        check_vma=False,
    )
```

```python
import functools

import jax
import jax.numpy as jnp
import numpy as np
from jax import lax
from jax.experimental import pallas as pl
from jax.experimental.pallas import tpu as pltpu
from jax.sharding import PartitionSpec as P


def passed_along(x, axis, by):
    size = lax.axis_size(axis)
    pairs = [(i, i + by) for i in range(size) if 0 <= i + by < size]
    return lax.ppermute(x, axis, pairs)


def relay(x, axis):
    n = lax.axis_size(axis)
    ups, downs = [], []
    up, down = x, x
    for step in range(1, n):
        up = lax.ppermute(up, axis, [(i, i + 1) for i in range(step - 1, n - 1)])
        down = lax.ppermute(down, axis, [(i + 1, i) for i in range(0, n - step)])
        ups.append(up)
        downs.append(down)
    return ups, downs


def strip_gather(x, axis):
    n = lax.axis_size(axis)
    if n == 1:
        return x
    m = x.shape[0]
    ups, downs = [], []
    up, down = x, x
    for step in range(1, n):
        up = lax.ppermute(up, axis, [(i, i + 1) for i in range(step - 1, n - 1)])
        down = lax.ppermute(down, axis, [(i + 1, i) for i in range(0, n - step)])
        ups.append(up)
        downs.append(down)
    stacked = jnp.concatenate(ups[::-1] + [x] + downs, axis=0)
    me = lax.axis_index(axis)
    return lax.dynamic_slice_in_dim(stacked, (n - 1 - me) * m, n * m, axis=0)


def rms_scale(values, gain):
    wide = values.astype(jnp.float32)
    return wide * lax.rsqrt(jnp.mean(wide * wide, axis=-1, keepdims=True) + 1e-06) * gain


def scaled(x, gain):
    wide = x.astype(jnp.float32)
    return wide * lax.rsqrt(jnp.mean(wide * wide, axis=-1, keepdims=True) + 1e-06) * gain


def attention_kernel(
    scale, whole_ref, flat_ref, query_ref, again_ref, wkv_ref, wo_ref, cgain_ref,
    resid_ref, act_ref, keys_ref, values_ref,
):
    @pl.when(pl.program_id(0) == 0)
    def _():
        normed_all = scaled(whole_ref[...], again_ref[...]).astype(jnp.bfloat16)
        both = jnp.dot(
            normed_all, wkv_ref[...], preferred_element_type=jnp.float32
        ).astype(jnp.bfloat16)
        width = keys_ref.shape[1]
        keys_ref[...] = both[:, :width]
        values_ref[...] = both[:, width:]

    scores = (
        lax.dot_general(
            query_ref[...], keys_ref[...], (((1,), (1,)), ((), ())),
            preferred_element_type=jnp.float32,
        )
        * scale
    )
    peak = jnp.max(scores, axis=1, keepdims=True)
    weights = jnp.exp(scores - peak)
    total = jnp.sum(weights, axis=1, keepdims=True)
    summed = jnp.dot(
        weights.astype(jnp.bfloat16), values_ref[...], preferred_element_type=jnp.float32
    )
    attended = (summed / total).astype(jnp.bfloat16)
    resid = (
        flat_ref[...].astype(jnp.float32)
        + jnp.dot(attended, wo_ref[...], preferred_element_type=jnp.float32)
    ).astype(jnp.bfloat16)
    resid_ref[...] = resid
    shown = scaled(resid, cgain_ref[...])
    act_ref[...] = (shown / (1.0 + jnp.exp(-shown))).astype(jnp.bfloat16)


def attend(whole, flat, query, attn_gain, key_weight, value_weight, out_weight, conv_gain, scale):
    count, width = query.shape
    total_keys = whole.shape[0]
    block = 160 if count % 160 == 0 and count * total_keys > 2 ** 21 else count
    full = lambda shape: pl.BlockSpec(shape, lambda i: (0, 0))
    rows_of = pl.BlockSpec((block, width), lambda i: (i, 0))
    flops = 4 * count * total_keys * width + 4 * total_keys * width * width
    flops += 2 * count * width * width
    return pl.pallas_call(
        functools.partial(attention_kernel, scale),
        out_shape=(
            jax.ShapeDtypeStruct((count, width), jnp.bfloat16),
            jax.ShapeDtypeStruct((count, width), jnp.bfloat16),
        ),
        grid=(count // block,),
        in_specs=[
            full((total_keys, width)),
            rows_of,
            rows_of,
            full((1, width)),
            full((width, 2 * width)),
            full((width, width)),
            full((1, width)),
        ],
        out_specs=(rows_of, rows_of),
        scratch_shapes=[
            pltpu.VMEM((total_keys, width), jnp.bfloat16),
            pltpu.VMEM((total_keys, width), jnp.bfloat16),
        ],
        compiler_params=pltpu.CompilerParams(vmem_limit_bytes=60 * 1024 * 1024),
        cost_estimate=pl.CostEstimate(
            flops=flops,
            transcendentals=count * total_keys + count * width,
            bytes_accessed=2 * width * (total_keys + 4 * count + 3 * width),
        ),
    )(
        whole, flat, query, attn_gain.reshape(1, width),
        jnp.concatenate([key_weight, value_weight], axis=1), out_weight,
        conv_gain.reshape(1, width),
    )


def split_kernels_a(scale, count, parts, me_ref, *refs):
    blocks = refs[:count]
    query_ref, again_ref, wkv_ref, m_ref, l_ref, o_ref, kv_ref = refs[count:]
    width = query_ref.shape[1]
    rows = blocks[0].shape[0]
    for index, block_ref in enumerate(blocks):
        normed = scaled(block_ref[...], again_ref[...]).astype(jnp.bfloat16)
        kv_ref[index * rows : (index + 1) * rows, :] = jnp.dot(
            normed, wkv_ref[...], preferred_element_type=jnp.float32
        ).astype(jnp.bfloat16)
    both = kv_ref[...]
    scores = (
        lax.dot_general(
            query_ref[...], both[:, :width], (((1,), (1,)), ((), ())),
            preferred_element_type=jnp.float32,
        )
        * scale
    )
    me = me_ref[0]
    column = lax.broadcasted_iota(jnp.int32, scores.shape, 1)
    second = (column >= rows) & (column < 2 * rows)
    third = (column >= 2 * rows) & (column < 3 * rows)
    hidden = (second & (me < 1)) | (third & (me > parts - 2))
    scores = jnp.where(hidden, -1e30, scores)
    peak = jnp.max(scores, axis=1, keepdims=True)
    weights = jnp.exp(scores - peak)
    m_ref[...] = peak
    l_ref[...] = jnp.sum(weights, axis=1, keepdims=True)
    o_ref[...] = jnp.dot(
        weights.astype(jnp.bfloat16), both[:, width:], preferred_element_type=jnp.float32
    )


def split_kernels_b(
    scale, parts, me_ref, up_ref, down_ref, query_ref, again_ref, wkv_ref, m_ref, l_ref, o_ref,
    flat_ref, wo_ref, cgain_ref, resid_ref, act_ref,
):
    width = query_ref.shape[1]
    me = me_ref[0]
    block = jnp.where(me == parts - 1, up_ref[...], down_ref[...])
    normed = scaled(block, again_ref[...]).astype(jnp.bfloat16)
    both = jnp.dot(normed, wkv_ref[...], preferred_element_type=jnp.float32).astype(jnp.bfloat16)
    scores = (
        lax.dot_general(
            query_ref[...], both[:, :width], (((1,), (1,)), ((), ())),
            preferred_element_type=jnp.float32,
        )
        * scale
    )
    scores = jnp.where((me == 0) | (me == parts - 1), scores, -1e30)
    earlier = m_ref[...]
    peak = jnp.maximum(jnp.max(scores, axis=1, keepdims=True), earlier)
    alpha = jnp.exp(earlier - peak)
    weights = jnp.exp(scores - peak)
    total = l_ref[...] * alpha + jnp.sum(weights, axis=1, keepdims=True)
    summed = o_ref[...] * alpha + jnp.dot(
        weights.astype(jnp.bfloat16), both[:, width:], preferred_element_type=jnp.float32
    )
    attended = (summed / total).astype(jnp.bfloat16)
    resid = (
        flat_ref[...].astype(jnp.float32)
        + jnp.dot(attended, wo_ref[...], preferred_element_type=jnp.float32)
    ).astype(jnp.bfloat16)
    resid_ref[...] = resid
    shown = scaled(resid, cgain_ref[...])
    act_ref[...] = (shown / (1.0 + jnp.exp(-shown))).astype(jnp.bfloat16)


def whole_call(kernel, me, inputs, outputs, flops, transcendentals, scratch=()):
    return pl.pallas_call(
        kernel,
        out_shape=outputs,
        grid_spec=pltpu.PrefetchScalarGridSpec(
            num_scalar_prefetch=1,
            grid=(1,),
            in_specs=[pl.BlockSpec(x.shape, lambda i, me: (0, 0)) for x in inputs],
            out_specs=tuple(pl.BlockSpec(o.shape, lambda i, me: (0, 0)) for o in outputs),
            scratch_shapes=list(scratch),
        ),
        compiler_params=pltpu.CompilerParams(vmem_limit_bytes=60 * 1024 * 1024),
        cost_estimate=pl.CostEstimate(
            flops=flops,
            transcendentals=transcendentals,
            bytes_accessed=sum(x.size * x.dtype.itemsize for x in inputs),
        ),
    )(me, *inputs)


def split_attend(
    me, parts, blocks_a, up_b, down_b, flat, query, attn_gain, key_weight, value_weight,
    out_weight, conv_gain, scale,
):
    count, width = query.shape
    wkv = jnp.concatenate([key_weight, value_weight], axis=1)
    again = attn_gain.reshape(1, width)
    f32 = jnp.float32
    keys_a, keys_b = count * len(blocks_a), count
    m_a, l_a, o_a = whole_call(
        functools.partial(split_kernels_a, scale, len(blocks_a), parts),
        me,
        list(blocks_a) + [query, again, wkv],
        (
            jax.ShapeDtypeStruct((count, 1), f32),
            jax.ShapeDtypeStruct((count, 1), f32),
            jax.ShapeDtypeStruct((count, width), f32),
        ),
        4 * keys_a * width * width + 4 * count * keys_a * width,
        count * keys_a,
        [pltpu.VMEM((keys_a, 2 * width), jnp.bfloat16)],
    )
    return whole_call(
        functools.partial(split_kernels_b, scale, parts),
        me,
        [up_b, down_b, query, again, wkv, m_a, l_a, o_a, flat, out_weight,
         conv_gain.reshape(1, width)],
        (
            jax.ShapeDtypeStruct((count, width), jnp.bfloat16),
            jax.ShapeDtypeStruct((count, width), jnp.bfloat16),
        ),
        4 * keys_b * width * width + 4 * count * keys_b * width + 2 * count * width * width,
        count * keys_b + count * width,
    )


def shards(
    frames,
    cache_frames,
    attn_gain,
    query_weight,
    key_weight,
    value_weight,
    out_weight,
    conv_gain,
    conv_weight,
):
    rows = frames.shape[1]
    cols = frames.shape[2]
    width = frames.shape[3]
    flat = frames.reshape(-1, width)
    count = flat.shape[0]
    scale = float(np.float32(1.0) / np.sqrt(np.float32(width)))
    n = lax.axis_size("strip")
    split_path = n == 4
    if not split_path:
        whole = strip_gather(flat, "strip")
    normed = rms_scale(flat, attn_gain).astype(jnp.bfloat16)
    query = jnp.dot(normed, query_weight, preferred_element_type=jnp.float32).astype(jnp.bfloat16)
    if split_path:
        me = lax.axis_index("strip")
        ups, downs = relay(flat, "strip")
        far = jnp.where(me <= 1, downs[1], ups[1])
        resid, act = split_attend(
            me.astype(jnp.int32).reshape(1), n, [flat, ups[0], downs[0], far], ups[n - 2],
            downs[n - 2], flat, query, attn_gain, key_weight, value_weight, out_weight,
            conv_gain, scale,
        )
    else:
        resid, act = attend(
            whole, flat, query, attn_gain, key_weight, value_weight, out_weight, conv_gain, scale
        )
    act = act.reshape(rows, cols, width)
    frame_index = lax.axis_index("tm")
    prior = passed_along(act, "tm", 1)
    prior = jnp.where(frame_index == 0, cache_frames[1], prior)
    older = passed_along(prior, "tm", 1)
    older = jnp.where(frame_index == 0, cache_frames[0], older)
    kernel = conv_weight.reshape(3, 3, 3 * width, width)

    def widen(frame):
        padded = jnp.pad(frame, ((1, 1), (1, 1), (0, 0)))
        return jnp.concatenate(
            [padded[:, 0:cols], padded[:, 1 : cols + 1], padded[:, 2 : cols + 2]], axis=-1
        )

    def frame_terms(wide, step_t):
        main = None
        for step_r in range(3):
            window = wide[step_r : step_r + rows].reshape(-1, 3 * width)
            part = jnp.dot(window, kernel[step_t, step_r], preferred_element_type=jnp.float32)
            main = part if main is None else main + part
        first = jnp.dot(wide[1], kernel[step_t, 2], preferred_element_type=jnp.float32)
        last = jnp.dot(wide[rows], kernel[step_t, 0], preferred_element_type=jnp.float32)
        return main, first, last

    own_main, own_first, own_last = frame_terms(widen(act), 2)
    prior_main, prior_first, prior_last = frame_terms(widen(prior), 1)
    older_main, older_first, older_last = frame_terms(widen(older), 0)
    to_prev = own_first + prior_first + older_first
    to_next = own_last + prior_last + older_last
    n = lax.axis_size("strip")
    from_next = lax.ppermute(
        to_prev.astype(jnp.bfloat16), "strip", [(i + 1, i) for i in range(n - 1)]
    )
    from_prev = lax.ppermute(
        to_next.astype(jnp.bfloat16), "strip", [(i, i + 1) for i in range(n - 1)]
    )
    result = resid.astype(jnp.float32) + own_main + prior_main + older_main
    edges = jnp.concatenate(
        [
            from_prev[None].astype(jnp.float32),
            jnp.zeros((rows - 2, cols, width), jnp.float32),
            from_next[None].astype(jnp.float32),
        ],
        axis=0,
    )
    result = result + edges.reshape(-1, width)
    return result.astype(jnp.bfloat16).reshape(1, rows, cols, width)


def solution(mesh):
    return jax.shard_map(
        shards,
        mesh=mesh,
        in_specs=(
            P(("clip", "tm"), "strip", None, None),
            P("clip", "strip", None, None),
            P(),
            P(),
            P(),
            P(),
            P(),
            P(),
            P(),
        ),
        out_specs=P(("clip", "tm"), "strip", None, None),
        check_vma=False,
    )
```

```python
import functools

import jax
import jax.numpy as jnp
import numpy as np
from jax import lax
from jax.experimental import pallas as pl
from jax.experimental.pallas import tpu as pltpu
from jax.sharding import PartitionSpec as P


def passed_along(x, axis, by):
    size = lax.axis_size(axis)
    pairs = [(i, i + by) for i in range(size) if 0 <= i + by < size]
    return lax.ppermute(x, axis, pairs)


def relay(x, axis):
    n = lax.axis_size(axis)
    ups, downs = [], []
    up, down = x, x
    for step in range(1, n):
        up = lax.ppermute(up, axis, [(i, i + 1) for i in range(step - 1, n - 1)])
        down = lax.ppermute(down, axis, [(i + 1, i) for i in range(0, n - step)])
        ups.append(up)
        downs.append(down)
    return ups, downs


def strip_gather(x, axis):
    n = lax.axis_size(axis)
    if n == 1:
        return x
    m = x.shape[0]
    ups, downs = [], []
    up, down = x, x
    for step in range(1, n):
        up = lax.ppermute(up, axis, [(i, i + 1) for i in range(step - 1, n - 1)])
        down = lax.ppermute(down, axis, [(i + 1, i) for i in range(0, n - step)])
        ups.append(up)
        downs.append(down)
    stacked = jnp.concatenate(ups[::-1] + [x] + downs, axis=0)
    me = lax.axis_index(axis)
    return lax.dynamic_slice_in_dim(stacked, (n - 1 - me) * m, n * m, axis=0)


def rms_scale(values, gain):
    wide = values.astype(jnp.float32)
    return wide * lax.rsqrt(jnp.mean(wide * wide, axis=-1, keepdims=True) + 1e-06) * gain


def scaled(x, gain):
    wide = x.astype(jnp.float32)
    return wide * lax.rsqrt(jnp.mean(wide * wide, axis=-1, keepdims=True) + 1e-06) * gain


def attention_kernel(
    scale, whole_ref, flat_ref, query_ref, again_ref, wkv_ref, wo_ref, cgain_ref,
    resid_ref, act_ref, keys_ref, values_ref,
):
    @pl.when(pl.program_id(0) == 0)
    def _():
        normed_all = scaled(whole_ref[...], again_ref[...]).astype(jnp.bfloat16)
        both = jnp.dot(
            normed_all, wkv_ref[...], preferred_element_type=jnp.float32
        ).astype(jnp.bfloat16)
        width = keys_ref.shape[1]
        keys_ref[...] = both[:, :width]
        values_ref[...] = both[:, width:]

    scores = (
        lax.dot_general(
            query_ref[...], keys_ref[...], (((1,), (1,)), ((), ())),
            preferred_element_type=jnp.float32,
        )
        * scale
    )
    peak = jnp.max(scores, axis=1, keepdims=True)
    weights = jnp.exp(scores - peak)
    total = jnp.sum(weights, axis=1, keepdims=True)
    summed = jnp.dot(
        weights.astype(jnp.bfloat16), values_ref[...], preferred_element_type=jnp.float32
    )
    attended = (summed / total).astype(jnp.bfloat16)
    resid = (
        flat_ref[...].astype(jnp.float32)
        + jnp.dot(attended, wo_ref[...], preferred_element_type=jnp.float32)
    ).astype(jnp.bfloat16)
    resid_ref[...] = resid
    shown = scaled(resid, cgain_ref[...])
    act_ref[...] = (shown / (1.0 + jnp.exp(-shown))).astype(jnp.bfloat16)


def attend(whole, flat, query, attn_gain, key_weight, value_weight, out_weight, conv_gain, scale):
    count, width = query.shape
    total_keys = whole.shape[0]
    block = 160 if count % 160 == 0 and count * total_keys > 2 ** 21 else count
    full = lambda shape: pl.BlockSpec(shape, lambda i: (0, 0))
    rows_of = pl.BlockSpec((block, width), lambda i: (i, 0))
    flops = 4 * count * total_keys * width + 4 * total_keys * width * width
    flops += 2 * count * width * width
    return pl.pallas_call(
        functools.partial(attention_kernel, scale),
        out_shape=(
            jax.ShapeDtypeStruct((count, width), jnp.bfloat16),
            jax.ShapeDtypeStruct((count, width), jnp.bfloat16),
        ),
        grid=(count // block,),
        in_specs=[
            full((total_keys, width)),
            rows_of,
            rows_of,
            full((1, width)),
            full((width, 2 * width)),
            full((width, width)),
            full((1, width)),
        ],
        out_specs=(rows_of, rows_of),
        scratch_shapes=[
            pltpu.VMEM((total_keys, width), jnp.bfloat16),
            pltpu.VMEM((total_keys, width), jnp.bfloat16),
        ],
        compiler_params=pltpu.CompilerParams(vmem_limit_bytes=60 * 1024 * 1024),
        cost_estimate=pl.CostEstimate(
            flops=flops,
            transcendentals=count * total_keys + count * width,
            bytes_accessed=2 * width * (total_keys + 4 * count + 3 * width),
        ),
    )(
        whole, flat, query, attn_gain.reshape(1, width),
        jnp.concatenate([key_weight, value_weight], axis=1), out_weight,
        conv_gain.reshape(1, width),
    )


def split_kernels_a(scale, count, parts, me_ref, *refs):
    blocks = refs[:count]
    query_ref, again_ref, wkv_ref, m_ref, l_ref, o_ref, kv_ref = refs[count:]
    width = query_ref.shape[1]
    rows = blocks[0].shape[0]
    for index, block_ref in enumerate(blocks):
        normed = scaled(block_ref[...], again_ref[...]).astype(jnp.bfloat16)
        kv_ref[index * rows : (index + 1) * rows, :] = jnp.dot(
            normed, wkv_ref[...], preferred_element_type=jnp.float32
        ).astype(jnp.bfloat16)
    both = kv_ref[...]
    scores = (
        lax.dot_general(
            query_ref[...], both[:, :width], (((1,), (1,)), ((), ())),
            preferred_element_type=jnp.float32,
        )
        * scale
    )
    me = me_ref[0]
    column = lax.broadcasted_iota(jnp.int32, scores.shape, 1)
    second = (column >= rows) & (column < 2 * rows)
    third = (column >= 2 * rows) & (column < 3 * rows)
    hidden = (second & (me < 1)) | (third & (me > parts - 2))
    scores = jnp.where(hidden, -1e30, scores)
    peak = jnp.max(scores, axis=1, keepdims=True)
    weights = jnp.exp(scores - peak)
    m_ref[...] = peak
    l_ref[...] = jnp.sum(weights, axis=1, keepdims=True)
    o_ref[...] = jnp.dot(
        weights.astype(jnp.bfloat16), both[:, width:], preferred_element_type=jnp.float32
    )


def split_kernels_b(
    scale, parts, me_ref, up_ref, down_ref, query_ref, again_ref, wkv_ref, m_ref, l_ref, o_ref,
    flat_ref, wo_ref, cgain_ref, resid_ref, act_ref,
):
    width = query_ref.shape[1]
    me = me_ref[0]
    block = jnp.where(me == parts - 1, up_ref[...], down_ref[...])
    normed = scaled(block, again_ref[...]).astype(jnp.bfloat16)
    both = jnp.dot(normed, wkv_ref[...], preferred_element_type=jnp.float32).astype(jnp.bfloat16)
    scores = (
        lax.dot_general(
            query_ref[...], both[:, :width], (((1,), (1,)), ((), ())),
            preferred_element_type=jnp.float32,
        )
        * scale
    )
    scores = jnp.where((me == 0) | (me == parts - 1), scores, -1e30)
    earlier = m_ref[...]
    peak = jnp.maximum(jnp.max(scores, axis=1, keepdims=True), earlier)
    alpha = jnp.exp(earlier - peak)
    weights = jnp.exp(scores - peak)
    total = l_ref[...] * alpha + jnp.sum(weights, axis=1, keepdims=True)
    summed = o_ref[...] * alpha + jnp.dot(
        weights.astype(jnp.bfloat16), both[:, width:], preferred_element_type=jnp.float32
    )
    attended = (summed / total).astype(jnp.bfloat16)
    resid = (
        flat_ref[...].astype(jnp.float32)
        + jnp.dot(attended, wo_ref[...], preferred_element_type=jnp.float32)
    ).astype(jnp.bfloat16)
    resid_ref[...] = resid
    shown = scaled(resid, cgain_ref[...])
    act_ref[...] = (shown / (1.0 + jnp.exp(-shown))).astype(jnp.bfloat16)


def whole_call(kernel, me, inputs, outputs, flops, transcendentals, scratch=()):
    return pl.pallas_call(
        kernel,
        out_shape=outputs,
        grid_spec=pltpu.PrefetchScalarGridSpec(
            num_scalar_prefetch=1,
            grid=(1,),
            in_specs=[pl.BlockSpec(x.shape, lambda i, me: (0, 0)) for x in inputs],
            out_specs=tuple(pl.BlockSpec(o.shape, lambda i, me: (0, 0)) for o in outputs),
            scratch_shapes=list(scratch),
        ),
        compiler_params=pltpu.CompilerParams(vmem_limit_bytes=24 * 1024 * 1024),
        cost_estimate=pl.CostEstimate(
            flops=flops,
            transcendentals=transcendentals,
            bytes_accessed=sum(x.size * x.dtype.itemsize for x in inputs),
        ),
    )(me, *inputs)


def split_attend(
    me, parts, blocks_a, up_b, down_b, flat, query, attn_gain, key_weight, value_weight,
    out_weight, conv_gain, scale,
):
    count, width = query.shape
    wkv = jnp.concatenate([key_weight, value_weight], axis=1)
    again = attn_gain.reshape(1, width)
    f32 = jnp.float32
    keys_a, keys_b = count * len(blocks_a), count
    m_a, l_a, o_a = whole_call(
        functools.partial(split_kernels_a, scale, len(blocks_a), parts),
        me,
        list(blocks_a) + [query, again, wkv],
        (
            jax.ShapeDtypeStruct((count, 1), f32),
            jax.ShapeDtypeStruct((count, 1), f32),
            jax.ShapeDtypeStruct((count, width), f32),
        ),
        4 * keys_a * width * width + 4 * count * keys_a * width,
        count * keys_a,
        [pltpu.VMEM((keys_a, 2 * width), jnp.bfloat16)],
    )
    return whole_call(
        functools.partial(split_kernels_b, scale, parts),
        me,
        [up_b, down_b, query, again, wkv, m_a, l_a, o_a, flat, out_weight,
         conv_gain.reshape(1, width)],
        (
            jax.ShapeDtypeStruct((count, width), jnp.bfloat16),
            jax.ShapeDtypeStruct((count, width), jnp.bfloat16),
        ),
        4 * keys_b * width * width + 4 * count * keys_b * width + 2 * count * width * width,
        count * keys_b + count * width,
    )


def shards(
    frames,
    cache_frames,
    attn_gain,
    query_weight,
    key_weight,
    value_weight,
    out_weight,
    conv_gain,
    conv_weight,
):
    rows = frames.shape[1]
    cols = frames.shape[2]
    width = frames.shape[3]
    flat = frames.reshape(-1, width)
    count = flat.shape[0]
    scale = float(np.float32(1.0) / np.sqrt(np.float32(width)))
    n = lax.axis_size("strip")
    split_path = n == 4
    if not split_path:
        whole = strip_gather(flat, "strip")
    normed = rms_scale(flat, attn_gain).astype(jnp.bfloat16)
    query = jnp.dot(normed, query_weight, preferred_element_type=jnp.float32).astype(jnp.bfloat16)
    if split_path:
        me = lax.axis_index("strip")
        ups, downs = relay(flat, "strip")
        far = jnp.where(me <= 1, downs[1], ups[1])
        resid, act = split_attend(
            me.astype(jnp.int32).reshape(1), n, [flat, ups[0], downs[0], far], ups[n - 2],
            downs[n - 2], flat, query, attn_gain, key_weight, value_weight, out_weight,
            conv_gain, scale,
        )
    else:
        resid, act = attend(
            whole, flat, query, attn_gain, key_weight, value_weight, out_weight, conv_gain, scale
        )
    act = act.reshape(rows, cols, width)
    frame_index = lax.axis_index("tm")
    prior = passed_along(act, "tm", 1)
    prior = jnp.where(frame_index == 0, cache_frames[1], prior)
    older = passed_along(prior, "tm", 1)
    older = jnp.where(frame_index == 0, cache_frames[0], older)
    kernel = conv_weight.reshape(3, 3, 3 * width, width)

    def widen(frame):
        padded = jnp.pad(frame, ((1, 1), (1, 1), (0, 0)))
        return jnp.concatenate(
            [padded[:, 0:cols], padded[:, 1 : cols + 1], padded[:, 2 : cols + 2]], axis=-1
        )

    def frame_terms(wide, step_t):
        main = None
        for step_r in range(3):
            window = wide[step_r : step_r + rows].reshape(-1, 3 * width)
            part = jnp.dot(window, kernel[step_t, step_r], preferred_element_type=jnp.float32)
            main = part if main is None else main + part
        first = jnp.dot(wide[1], kernel[step_t, 2], preferred_element_type=jnp.float32)
        last = jnp.dot(wide[rows], kernel[step_t, 0], preferred_element_type=jnp.float32)
        return main, first, last

    own_main, own_first, own_last = frame_terms(widen(act), 2)
    prior_main, prior_first, prior_last = frame_terms(widen(prior), 1)
    older_main, older_first, older_last = frame_terms(widen(older), 0)
    to_prev = own_first + prior_first + older_first
    to_next = own_last + prior_last + older_last
    n = lax.axis_size("strip")
    from_next = lax.ppermute(
        to_prev.astype(jnp.bfloat16), "strip", [(i + 1, i) for i in range(n - 1)]
    )
    from_prev = lax.ppermute(
        to_next.astype(jnp.bfloat16), "strip", [(i, i + 1) for i in range(n - 1)]
    )
    result = resid.astype(jnp.float32) + own_main + prior_main + older_main
    edges = jnp.concatenate(
        [
            from_prev[None].astype(jnp.float32),
            jnp.zeros((rows - 2, cols, width), jnp.float32),
            from_next[None].astype(jnp.float32),
        ],
        axis=0,
    )
    result = result + edges.reshape(-1, width)
    return result.astype(jnp.bfloat16).reshape(1, rows, cols, width)


def solution(mesh):
    return jax.shard_map(
        shards,
        mesh=mesh,
        in_specs=(
            P(("clip", "tm"), "strip", None, None),
            P("clip", "strip", None, None),
            P(),
            P(),
            P(),
            P(),
            P(),
            P(),
            P(),
        ),
        out_specs=P(("clip", "tm"), "strip", None, None),
        check_vma=False,
    )
```

```python
import functools

import jax
import jax.numpy as jnp
import numpy as np
from jax import lax
from jax.experimental import pallas as pl
from jax.experimental.pallas import tpu as pltpu
from jax.sharding import PartitionSpec as P


def passed_along(x, axis, by):
    size = lax.axis_size(axis)
    pairs = [(i, i + by) for i in range(size) if 0 <= i + by < size]
    return lax.ppermute(x, axis, pairs)


def relay(x, axis):
    n = lax.axis_size(axis)
    ups, downs = [], []
    up, down = x, x
    for step in range(1, n):
        up = lax.ppermute(up, axis, [(i, i + 1) for i in range(step - 1, n - 1)])
        down = lax.ppermute(down, axis, [(i + 1, i) for i in range(0, n - step)])
        ups.append(up)
        downs.append(down)
    return ups, downs


def strip_gather(x, axis):
    n = lax.axis_size(axis)
    if n == 1:
        return x
    m = x.shape[0]
    ups, downs = [], []
    up, down = x, x
    for step in range(1, n):
        up = lax.ppermute(up, axis, [(i, i + 1) for i in range(step - 1, n - 1)])
        down = lax.ppermute(down, axis, [(i + 1, i) for i in range(0, n - step)])
        ups.append(up)
        downs.append(down)
    stacked = jnp.concatenate(ups[::-1] + [x] + downs, axis=0)
    me = lax.axis_index(axis)
    return lax.dynamic_slice_in_dim(stacked, (n - 1 - me) * m, n * m, axis=0)


def rms_scale(values, gain):
    wide = values.astype(jnp.float32)
    return wide * lax.rsqrt(jnp.mean(wide * wide, axis=-1, keepdims=True) + 1e-06) * gain


def scaled(x, gain):
    wide = x.astype(jnp.float32)
    return wide * lax.rsqrt(jnp.mean(wide * wide, axis=-1, keepdims=True) + 1e-06) * gain


def attention_kernel(
    scale, whole_ref, flat_ref, query_ref, again_ref, wkv_ref, wo_ref, cgain_ref,
    resid_ref, act_ref, keys_ref, values_ref,
):
    @pl.when(pl.program_id(0) == 0)
    def _():
        normed_all = scaled(whole_ref[...], again_ref[...]).astype(jnp.bfloat16)
        both = jnp.dot(
            normed_all, wkv_ref[...], preferred_element_type=jnp.float32
        ).astype(jnp.bfloat16)
        width = keys_ref.shape[1]
        keys_ref[...] = both[:, :width]
        values_ref[...] = both[:, width:]

    scores = (
        lax.dot_general(
            query_ref[...], keys_ref[...], (((1,), (1,)), ((), ())),
            preferred_element_type=jnp.float32,
        )
        * scale
    )
    peak = jnp.max(scores, axis=1, keepdims=True)
    weights = jnp.exp(scores - peak)
    total = jnp.sum(weights, axis=1, keepdims=True)
    summed = jnp.dot(
        weights.astype(jnp.bfloat16), values_ref[...], preferred_element_type=jnp.float32
    )
    attended = (summed / total).astype(jnp.bfloat16)
    resid = (
        flat_ref[...].astype(jnp.float32)
        + jnp.dot(attended, wo_ref[...], preferred_element_type=jnp.float32)
    ).astype(jnp.bfloat16)
    resid_ref[...] = resid
    shown = scaled(resid, cgain_ref[...])
    act_ref[...] = (shown / (1.0 + jnp.exp(-shown))).astype(jnp.bfloat16)


def attend(whole, flat, query, attn_gain, key_weight, value_weight, out_weight, conv_gain, scale):
    count, width = query.shape
    total_keys = whole.shape[0]
    block = 160 if count % 160 == 0 and count * total_keys > 2 ** 21 else count
    full = lambda shape: pl.BlockSpec(shape, lambda i: (0, 0))
    rows_of = pl.BlockSpec((block, width), lambda i: (i, 0))
    flops = 4 * count * total_keys * width + 4 * total_keys * width * width
    flops += 2 * count * width * width
    return pl.pallas_call(
        functools.partial(attention_kernel, scale),
        out_shape=(
            jax.ShapeDtypeStruct((count, width), jnp.bfloat16),
            jax.ShapeDtypeStruct((count, width), jnp.bfloat16),
        ),
        grid=(count // block,),
        in_specs=[
            full((total_keys, width)),
            rows_of,
            rows_of,
            full((1, width)),
            full((width, 2 * width)),
            full((width, width)),
            full((1, width)),
        ],
        out_specs=(rows_of, rows_of),
        scratch_shapes=[
            pltpu.VMEM((total_keys, width), jnp.bfloat16),
            pltpu.VMEM((total_keys, width), jnp.bfloat16),
        ],
        compiler_params=pltpu.CompilerParams(vmem_limit_bytes=60 * 1024 * 1024),
        cost_estimate=pl.CostEstimate(
            flops=flops,
            transcendentals=count * total_keys + count * width,
            bytes_accessed=2 * width * (total_keys + 4 * count + 3 * width),
        ),
    )(
        whole, flat, query, attn_gain.reshape(1, width),
        jnp.concatenate([key_weight, value_weight], axis=1), out_weight,
        conv_gain.reshape(1, width),
    )


def split_kernels_a(scale, count, parts, me_ref, *refs):
    blocks = refs[:count]
    query_ref, again_ref, wkv_ref, m_ref, l_ref, o_ref, kv_ref = refs[count:]
    width = query_ref.shape[1]
    rows = blocks[0].shape[0]
    for index, block_ref in enumerate(blocks):
        normed = scaled(block_ref[...], again_ref[...]).astype(jnp.bfloat16)
        kv_ref[index * rows : (index + 1) * rows, :] = jnp.dot(
            normed, wkv_ref[...], preferred_element_type=jnp.float32
        ).astype(jnp.bfloat16)
    both = kv_ref[...]
    scores = (
        lax.dot_general(
            query_ref[...], both[:, :width], (((1,), (1,)), ((), ())),
            preferred_element_type=jnp.float32,
        )
        * scale
    )
    me = me_ref[0]
    column = lax.broadcasted_iota(jnp.int32, scores.shape, 1)
    second = (column >= rows) & (column < 2 * rows)
    third = (column >= 2 * rows) & (column < 3 * rows)
    hidden = (second & (me < 1)) | (third & (me > parts - 2))
    scores = jnp.where(hidden, -1e30, scores)
    peak = jnp.max(scores, axis=1, keepdims=True)
    weights = jnp.exp(scores - peak)
    m_ref[...] = peak
    l_ref[...] = jnp.sum(weights, axis=1, keepdims=True)
    o_ref[...] = jnp.dot(
        weights.astype(jnp.bfloat16), both[:, width:], preferred_element_type=jnp.float32
    )


def split_kernels_b(
    scale, parts, me_ref, up_ref, down_ref, query_ref, again_ref, wkv_ref, m_ref, l_ref, o_ref,
    flat_ref, wo_ref, cgain_ref, resid_ref, act_ref,
):
    width = query_ref.shape[1]
    me = me_ref[0]
    block = jnp.where(me == parts - 1, up_ref[...], down_ref[...])
    normed = scaled(block, again_ref[...]).astype(jnp.bfloat16)
    both = jnp.dot(normed, wkv_ref[...], preferred_element_type=jnp.float32).astype(jnp.bfloat16)
    scores = (
        lax.dot_general(
            query_ref[...], both[:, :width], (((1,), (1,)), ((), ())),
            preferred_element_type=jnp.float32,
        )
        * scale
    )
    scores = jnp.where((me == 0) | (me == parts - 1), scores, -1e30)
    earlier = m_ref[...]
    peak = jnp.maximum(jnp.max(scores, axis=1, keepdims=True), earlier)
    alpha = jnp.exp(earlier - peak)
    weights = jnp.exp(scores - peak)
    total = l_ref[...] * alpha + jnp.sum(weights, axis=1, keepdims=True)
    summed = o_ref[...] * alpha + jnp.dot(
        weights.astype(jnp.bfloat16), both[:, width:], preferred_element_type=jnp.float32
    )
    attended = (summed / total).astype(jnp.bfloat16)
    resid = (
        flat_ref[...].astype(jnp.float32)
        + jnp.dot(attended, wo_ref[...], preferred_element_type=jnp.float32)
    ).astype(jnp.bfloat16)
    resid_ref[...] = resid
    shown = scaled(resid, cgain_ref[...])
    act_ref[...] = (shown / (1.0 + jnp.exp(-shown))).astype(jnp.bfloat16)


def whole_call(kernel, me, inputs, outputs, flops, transcendentals, scratch=()):
    return pl.pallas_call(
        kernel,
        out_shape=outputs,
        grid_spec=pltpu.PrefetchScalarGridSpec(
            num_scalar_prefetch=1,
            grid=(1,),
            in_specs=[pl.BlockSpec(x.shape, lambda i, me: (0, 0)) for x in inputs],
            out_specs=tuple(pl.BlockSpec(o.shape, lambda i, me: (0, 0)) for o in outputs),
            scratch_shapes=list(scratch),
        ),
        compiler_params=pltpu.CompilerParams(vmem_limit_bytes=16 * 1024 * 1024),
        cost_estimate=pl.CostEstimate(
            flops=flops,
            transcendentals=transcendentals,
            bytes_accessed=sum(x.size * x.dtype.itemsize for x in inputs),
        ),
    )(me, *inputs)


def split_attend(
    me, parts, blocks_a, up_b, down_b, flat, query, attn_gain, key_weight, value_weight,
    out_weight, conv_gain, scale,
):
    count, width = query.shape
    wkv = jnp.concatenate([key_weight, value_weight], axis=1)
    again = attn_gain.reshape(1, width)
    f32 = jnp.float32
    keys_a, keys_b = count * len(blocks_a), count
    m_a, l_a, o_a = whole_call(
        functools.partial(split_kernels_a, scale, len(blocks_a), parts),
        me,
        list(blocks_a) + [query, again, wkv],
        (
            jax.ShapeDtypeStruct((count, 1), f32),
            jax.ShapeDtypeStruct((count, 1), f32),
            jax.ShapeDtypeStruct((count, width), f32),
        ),
        4 * keys_a * width * width + 4 * count * keys_a * width,
        count * keys_a,
        [pltpu.VMEM((keys_a, 2 * width), jnp.bfloat16)],
    )
    return whole_call(
        functools.partial(split_kernels_b, scale, parts),
        me,
        [up_b, down_b, query, again, wkv, m_a, l_a, o_a, flat, out_weight,
         conv_gain.reshape(1, width)],
        (
            jax.ShapeDtypeStruct((count, width), jnp.bfloat16),
            jax.ShapeDtypeStruct((count, width), jnp.bfloat16),
        ),
        4 * keys_b * width * width + 4 * count * keys_b * width + 2 * count * width * width,
        count * keys_b + count * width,
    )


def shards(
    frames,
    cache_frames,
    attn_gain,
    query_weight,
    key_weight,
    value_weight,
    out_weight,
    conv_gain,
    conv_weight,
):
    rows = frames.shape[1]
    cols = frames.shape[2]
    width = frames.shape[3]
    flat = frames.reshape(-1, width)
    count = flat.shape[0]
    scale = float(np.float32(1.0) / np.sqrt(np.float32(width)))
    n = lax.axis_size("strip")
    split_path = n == 4
    if not split_path:
        whole = strip_gather(flat, "strip")
    normed = rms_scale(flat, attn_gain).astype(jnp.bfloat16)
    query = jnp.dot(normed, query_weight, preferred_element_type=jnp.float32).astype(jnp.bfloat16)
    if split_path:
        me = lax.axis_index("strip")
        ups, downs = relay(flat, "strip")
        far = jnp.where(me <= 1, downs[1], ups[1])
        resid, act = split_attend(
            me.astype(jnp.int32).reshape(1), n, [flat, ups[0], downs[0], far], ups[n - 2],
            downs[n - 2], flat, query, attn_gain, key_weight, value_weight, out_weight,
            conv_gain, scale,
        )
    else:
        resid, act = attend(
            whole, flat, query, attn_gain, key_weight, value_weight, out_weight, conv_gain, scale
        )
    act = act.reshape(rows, cols, width)
    frame_index = lax.axis_index("tm")
    prior = passed_along(act, "tm", 1)
    prior = jnp.where(frame_index == 0, cache_frames[1], prior)
    older = passed_along(prior, "tm", 1)
    older = jnp.where(frame_index == 0, cache_frames[0], older)
    kernel = conv_weight.reshape(3, 3, 3 * width, width)

    def widen(frame):
        padded = jnp.pad(frame, ((1, 1), (1, 1), (0, 0)))
        return jnp.concatenate(
            [padded[:, 0:cols], padded[:, 1 : cols + 1], padded[:, 2 : cols + 2]], axis=-1
        )

    def frame_terms(wide, step_t):
        main = None
        for step_r in range(3):
            window = wide[step_r : step_r + rows].reshape(-1, 3 * width)
            part = jnp.dot(window, kernel[step_t, step_r], preferred_element_type=jnp.float32)
            main = part if main is None else main + part
        first = jnp.dot(wide[1], kernel[step_t, 2], preferred_element_type=jnp.float32)
        last = jnp.dot(wide[rows], kernel[step_t, 0], preferred_element_type=jnp.float32)
        return main, first, last

    own_main, own_first, own_last = frame_terms(widen(act), 2)
    prior_main, prior_first, prior_last = frame_terms(widen(prior), 1)
    older_main, older_first, older_last = frame_terms(widen(older), 0)
    to_prev = own_first + prior_first + older_first
    to_next = own_last + prior_last + older_last
    n = lax.axis_size("strip")
    from_next = lax.ppermute(
        to_prev.astype(jnp.bfloat16), "strip", [(i + 1, i) for i in range(n - 1)]
    )
    from_prev = lax.ppermute(
        to_next.astype(jnp.bfloat16), "strip", [(i, i + 1) for i in range(n - 1)]
    )
    result = resid.astype(jnp.float32) + own_main + prior_main + older_main
    edges = jnp.concatenate(
        [
            from_prev[None].astype(jnp.float32),
            jnp.zeros((rows - 2, cols, width), jnp.float32),
            from_next[None].astype(jnp.float32),
        ],
        axis=0,
    )
    result = result + edges.reshape(-1, width)
    return result.astype(jnp.bfloat16).reshape(1, rows, cols, width)


def solution(mesh):
    return jax.shard_map(
        shards,
        mesh=mesh,
        in_specs=(
            P(("clip", "tm"), "strip", None, None),
            P("clip", "strip", None, None),
            P(),
            P(),
            P(),
            P(),
            P(),
            P(),
            P(),
        ),
        out_specs=P(("clip", "tm"), "strip", None, None),
        check_vma=False,
    )
```

```python
import functools

import jax
import jax.numpy as jnp
import numpy as np
from jax import lax
from jax.experimental import pallas as pl
from jax.experimental.pallas import tpu as pltpu
from jax.sharding import PartitionSpec as P


def passed_along(x, axis, by):
    size = lax.axis_size(axis)
    pairs = [(i, i + by) for i in range(size) if 0 <= i + by < size]
    return lax.ppermute(x, axis, pairs)


def relay(x, axis):
    n = lax.axis_size(axis)
    ups, downs = [], []
    up, down = x, x
    for step in range(1, n):
        up = lax.ppermute(up, axis, [(i, i + 1) for i in range(step - 1, n - 1)])
        down = lax.ppermute(down, axis, [(i + 1, i) for i in range(0, n - step)])
        ups.append(up)
        downs.append(down)
    return ups, downs


def strip_gather(x, axis):
    n = lax.axis_size(axis)
    if n == 1:
        return x
    m = x.shape[0]
    ups, downs = [], []
    up, down = x, x
    for step in range(1, n):
        up = lax.ppermute(up, axis, [(i, i + 1) for i in range(step - 1, n - 1)])
        down = lax.ppermute(down, axis, [(i + 1, i) for i in range(0, n - step)])
        ups.append(up)
        downs.append(down)
    stacked = jnp.concatenate(ups[::-1] + [x] + downs, axis=0)
    me = lax.axis_index(axis)
    return lax.dynamic_slice_in_dim(stacked, (n - 1 - me) * m, n * m, axis=0)


def rms_scale(values, gain):
    wide = values.astype(jnp.float32)
    return wide * lax.rsqrt(jnp.mean(wide * wide, axis=-1, keepdims=True) + 1e-06) * gain


def scaled(x, gain):
    wide = x.astype(jnp.float32)
    return wide * lax.rsqrt(jnp.mean(wide * wide, axis=-1, keepdims=True) + 1e-06) * gain


def attention_kernel(
    scale, whole_ref, flat_ref, query_ref, again_ref, wkv_ref, wo_ref, cgain_ref,
    resid_ref, act_ref, keys_ref, values_ref,
):
    @pl.when(pl.program_id(0) == 0)
    def _():
        normed_all = scaled(whole_ref[...], again_ref[...]).astype(jnp.bfloat16)
        both = jnp.dot(
            normed_all, wkv_ref[...], preferred_element_type=jnp.float32
        ).astype(jnp.bfloat16)
        width = keys_ref.shape[1]
        keys_ref[...] = both[:, :width]
        values_ref[...] = both[:, width:]

    scores = (
        lax.dot_general(
            query_ref[...], keys_ref[...], (((1,), (1,)), ((), ())),
            preferred_element_type=jnp.float32,
        )
        * scale
    )
    peak = jnp.max(scores, axis=1, keepdims=True)
    weights = jnp.exp(scores - peak)
    total = jnp.sum(weights, axis=1, keepdims=True)
    summed = jnp.dot(
        weights.astype(jnp.bfloat16), values_ref[...], preferred_element_type=jnp.float32
    )
    attended = (summed / total).astype(jnp.bfloat16)
    resid = (
        flat_ref[...].astype(jnp.float32)
        + jnp.dot(attended, wo_ref[...], preferred_element_type=jnp.float32)
    ).astype(jnp.bfloat16)
    resid_ref[...] = resid
    shown = scaled(resid, cgain_ref[...])
    act_ref[...] = (shown / (1.0 + jnp.exp(-shown))).astype(jnp.bfloat16)


def attend(whole, flat, query, attn_gain, key_weight, value_weight, out_weight, conv_gain, scale):
    count, width = query.shape
    total_keys = whole.shape[0]
    block = 160 if count % 160 == 0 and count * total_keys > 2 ** 21 else count
    full = lambda shape: pl.BlockSpec(shape, lambda i: (0, 0))
    rows_of = pl.BlockSpec((block, width), lambda i: (i, 0))
    flops = 4 * count * total_keys * width + 4 * total_keys * width * width
    flops += 2 * count * width * width
    return pl.pallas_call(
        functools.partial(attention_kernel, scale),
        out_shape=(
            jax.ShapeDtypeStruct((count, width), jnp.bfloat16),
            jax.ShapeDtypeStruct((count, width), jnp.bfloat16),
        ),
        grid=(count // block,),
        in_specs=[
            full((total_keys, width)),
            rows_of,
            rows_of,
            full((1, width)),
            full((width, 2 * width)),
            full((width, width)),
            full((1, width)),
        ],
        out_specs=(rows_of, rows_of),
        scratch_shapes=[
            pltpu.VMEM((total_keys, width), jnp.bfloat16),
            pltpu.VMEM((total_keys, width), jnp.bfloat16),
        ],
        compiler_params=pltpu.CompilerParams(vmem_limit_bytes=60 * 1024 * 1024),
        cost_estimate=pl.CostEstimate(
            flops=flops,
            transcendentals=count * total_keys + count * width,
            bytes_accessed=2 * width * (total_keys + 4 * count + 3 * width),
        ),
    )(
        whole, flat, query, attn_gain.reshape(1, width),
        jnp.concatenate([key_weight, value_weight], axis=1), out_weight,
        conv_gain.reshape(1, width),
    )


def split_kernels_a(scale, count, parts, me_ref, *refs):
    blocks = refs[:count]
    query_ref, again_ref, wkv_ref, m_ref, l_ref, o_ref, kv_ref = refs[count:]
    width = query_ref.shape[1]
    rows = blocks[0].shape[0]
    for index, block_ref in enumerate(blocks):
        normed = scaled(block_ref[...], again_ref[...]).astype(jnp.bfloat16)
        kv_ref[index * rows : (index + 1) * rows, :] = jnp.dot(
            normed, wkv_ref[...], preferred_element_type=jnp.float32
        ).astype(jnp.bfloat16)
    both = kv_ref[...]
    scores = (
        lax.dot_general(
            query_ref[...], both[:, :width], (((1,), (1,)), ((), ())),
            preferred_element_type=jnp.float32,
        )
        * scale
    )
    me = me_ref[0]
    column = lax.broadcasted_iota(jnp.int32, scores.shape, 1)
    second = (column >= rows) & (column < 2 * rows)
    third = (column >= 2 * rows) & (column < 3 * rows)
    hidden = (second & (me < 1)) | (third & (me > parts - 2))
    scores = jnp.where(hidden, -1e30, scores)
    peak = jnp.max(scores, axis=1, keepdims=True)
    weights = jnp.exp(scores - peak)
    m_ref[...] = peak
    l_ref[...] = jnp.sum(weights, axis=1, keepdims=True)
    o_ref[...] = jnp.dot(
        weights.astype(jnp.bfloat16), both[:, width:], preferred_element_type=jnp.float32
    )


def split_kernels_b(
    scale, parts, me_ref, up_ref, down_ref, query_ref, again_ref, wkv_ref, m_ref, l_ref, o_ref,
    flat_ref, wo_ref, cgain_ref, resid_ref, act_ref,
):
    width = query_ref.shape[1]
    me = me_ref[0]
    block = jnp.where(me == parts - 1, up_ref[...], down_ref[...])
    normed = scaled(block, again_ref[...]).astype(jnp.bfloat16)
    both = jnp.dot(normed, wkv_ref[...], preferred_element_type=jnp.float32).astype(jnp.bfloat16)
    scores = (
        lax.dot_general(
            query_ref[...], both[:, :width], (((1,), (1,)), ((), ())),
            preferred_element_type=jnp.float32,
        )
        * scale
    )
    scores = jnp.where((me == 0) | (me == parts - 1), scores, -1e30)
    earlier = m_ref[...]
    peak = jnp.maximum(jnp.max(scores, axis=1, keepdims=True), earlier)
    alpha = jnp.exp(earlier - peak)
    weights = jnp.exp(scores - peak)
    total = l_ref[...] * alpha + jnp.sum(weights, axis=1, keepdims=True)
    summed = o_ref[...] * alpha + jnp.dot(
        weights.astype(jnp.bfloat16), both[:, width:], preferred_element_type=jnp.float32
    )
    attended = (summed / total).astype(jnp.bfloat16)
    resid = (
        flat_ref[...].astype(jnp.float32)
        + jnp.dot(attended, wo_ref[...], preferred_element_type=jnp.float32)
    ).astype(jnp.bfloat16)
    resid_ref[...] = resid
    shown = scaled(resid, cgain_ref[...])
    act_ref[...] = (shown / (1.0 + jnp.exp(-shown))).astype(jnp.bfloat16)


def whole_call(kernel, me, inputs, outputs, flops, transcendentals, scratch=()):
    return pl.pallas_call(
        kernel,
        out_shape=outputs,
        grid_spec=pltpu.PrefetchScalarGridSpec(
            num_scalar_prefetch=1,
            grid=(1,),
            in_specs=[pl.BlockSpec(x.shape, lambda i, me: (0, 0)) for x in inputs],
            out_specs=tuple(pl.BlockSpec(o.shape, lambda i, me: (0, 0)) for o in outputs),
            scratch_shapes=list(scratch),
        ),
        compiler_params=pltpu.CompilerParams(vmem_limit_bytes=24 * 1024 * 1024),
        cost_estimate=pl.CostEstimate(
            flops=flops,
            transcendentals=transcendentals,
            bytes_accessed=sum(x.size * x.dtype.itemsize for x in inputs),
        ),
    )(me, *inputs)


def split_attend(
    me, parts, blocks_a, up_b, down_b, flat, query, attn_gain, key_weight, value_weight,
    out_weight, conv_gain, scale,
):
    count, width = query.shape
    wkv = jnp.concatenate([key_weight, value_weight], axis=1)
    again = attn_gain.reshape(1, width)
    f32 = jnp.float32
    keys_a, keys_b = count * len(blocks_a), count
    m_a, l_a, o_a = whole_call(
        functools.partial(split_kernels_a, scale, len(blocks_a), parts),
        me,
        list(blocks_a) + [query, again, wkv],
        (
            jax.ShapeDtypeStruct((count, 1), f32),
            jax.ShapeDtypeStruct((count, 1), f32),
            jax.ShapeDtypeStruct((count, width), f32),
        ),
        4 * keys_a * width * width + 4 * count * keys_a * width,
        count * keys_a,
        [pltpu.VMEM((keys_a, 2 * width), jnp.bfloat16)],
    )
    return whole_call(
        functools.partial(split_kernels_b, scale, parts),
        me,
        [up_b, down_b, query, again, wkv, m_a, l_a, o_a, flat, out_weight,
         conv_gain.reshape(1, width)],
        (
            jax.ShapeDtypeStruct((count, width), jnp.bfloat16),
            jax.ShapeDtypeStruct((count, width), jnp.bfloat16),
        ),
        4 * keys_b * width * width + 4 * count * keys_b * width + 2 * count * width * width,
        count * keys_b + count * width,
    )


def shards(
    frames,
    cache_frames,
    attn_gain,
    query_weight,
    key_weight,
    value_weight,
    out_weight,
    conv_gain,
    conv_weight,
):
    rows = frames.shape[1]
    cols = frames.shape[2]
    width = frames.shape[3]
    flat = frames.reshape(-1, width)
    count = flat.shape[0]
    scale = float(np.float32(1.0) / np.sqrt(np.float32(width)))
    n = lax.axis_size("strip")
    split_path = n == 4
    if not split_path:
        whole = strip_gather(flat, "strip")
    normed = rms_scale(flat, attn_gain).astype(jnp.bfloat16)
    query = jnp.dot(normed, query_weight, preferred_element_type=jnp.float32).astype(jnp.bfloat16)
    if split_path:
        me = lax.axis_index("strip")
        ups, downs = relay(flat, "strip")
        far = jnp.where(me <= 1, downs[1], ups[1])
        resid, act = split_attend(
            me.astype(jnp.int32).reshape(1), n, [flat, ups[0], downs[0], far], ups[n - 2],
            downs[n - 2], flat, query, attn_gain, key_weight, value_weight, out_weight,
            conv_gain, scale,
        )
    else:
        resid, act = attend(
            whole, flat, query, attn_gain, key_weight, value_weight, out_weight, conv_gain, scale
        )
    act = act.reshape(rows, cols, width)
    frame_index = lax.axis_index("tm")
    prior = passed_along(act, "tm", 1)
    prior = jnp.where(frame_index == 0, cache_frames[1], prior)
    older = passed_along(prior, "tm", 1)
    older = jnp.where(frame_index == 0, cache_frames[0], older)
    kernel = [conv_weight[t].reshape(3, 3 * width, width) for t in range(3)]

    def widen(frame):
        padded = jnp.pad(frame, ((1, 1), (1, 1), (0, 0)))
        return jnp.concatenate(
            [padded[:, 0:cols], padded[:, 1 : cols + 1], padded[:, 2 : cols + 2]], axis=-1
        )

    def frame_terms(wide, step_t):
        main = None
        for step_r in range(3):
            window = wide[step_r : step_r + rows].reshape(-1, 3 * width)
            part = jnp.dot(window, kernel[step_t][step_r], preferred_element_type=jnp.float32)
            main = part if main is None else main + part
        first = jnp.dot(wide[1], kernel[step_t][2], preferred_element_type=jnp.float32)
        last = jnp.dot(wide[rows], kernel[step_t][0], preferred_element_type=jnp.float32)
        return main, first, last

    own_main, own_first, own_last = frame_terms(widen(act), 2)
    prior_main, prior_first, prior_last = frame_terms(widen(prior), 1)
    older_main, older_first, older_last = frame_terms(widen(older), 0)
    to_prev = own_first + prior_first + older_first
    to_next = own_last + prior_last + older_last
    n = lax.axis_size("strip")
    from_next = lax.ppermute(
        to_prev.astype(jnp.bfloat16), "strip", [(i + 1, i) for i in range(n - 1)]
    )
    from_prev = lax.ppermute(
        to_next.astype(jnp.bfloat16), "strip", [(i, i + 1) for i in range(n - 1)]
    )
    result = resid.astype(jnp.float32) + own_main + prior_main + older_main
    edges = jnp.concatenate(
        [
            from_prev[None].astype(jnp.float32),
            jnp.zeros((rows - 2, cols, width), jnp.float32),
            from_next[None].astype(jnp.float32),
        ],
        axis=0,
    )
    result = result + edges.reshape(-1, width)
    return result.astype(jnp.bfloat16).reshape(1, rows, cols, width)


def solution(mesh):
    return jax.shard_map(
        shards,
        mesh=mesh,
        in_specs=(
            P(("clip", "tm"), "strip", None, None),
            P("clip", "strip", None, None),
            P(),
            P(),
            P(),
            P(),
            P(),
            P(),
            P(),
        ),
        out_specs=P(("clip", "tm"), "strip", None, None),
        check_vma=False,
    )
```

```python
import functools

import jax
import jax.numpy as jnp
import numpy as np
from jax import lax
from jax.experimental import pallas as pl
from jax.experimental.pallas import tpu as pltpu
from jax.sharding import PartitionSpec as P


def passed_along(x, axis, by):
    size = lax.axis_size(axis)
    pairs = [(i, i + by) for i in range(size) if 0 <= i + by < size]
    return lax.ppermute(x, axis, pairs)


def relay(x, axis):
    n = lax.axis_size(axis)
    ups, downs = [], []
    up, down = x, x
    for step in range(1, n):
        up = lax.ppermute(up, axis, [(i, i + 1) for i in range(step - 1, n - 1)])
        down = lax.ppermute(down, axis, [(i + 1, i) for i in range(0, n - step)])
        ups.append(up)
        downs.append(down)
    return ups, downs


def strip_gather(x, axis):
    n = lax.axis_size(axis)
    if n == 1:
        return x
    m = x.shape[0]
    ups, downs = [], []
    up, down = x, x
    for step in range(1, n):
        up = lax.ppermute(up, axis, [(i, i + 1) for i in range(step - 1, n - 1)])
        down = lax.ppermute(down, axis, [(i + 1, i) for i in range(0, n - step)])
        ups.append(up)
        downs.append(down)
    stacked = jnp.concatenate(ups[::-1] + [x] + downs, axis=0)
    me = lax.axis_index(axis)
    return lax.dynamic_slice_in_dim(stacked, (n - 1 - me) * m, n * m, axis=0)


def rms_scale(values, gain):
    wide = values.astype(jnp.float32)
    return wide * lax.rsqrt(jnp.mean(wide * wide, axis=-1, keepdims=True) + 1e-06) * gain


def scaled(x, gain):
    wide = x.astype(jnp.float32)
    return wide * lax.rsqrt(jnp.mean(wide * wide, axis=-1, keepdims=True) + 1e-06) * gain


def attention_kernel(
    scale, whole_ref, flat_ref, query_ref, again_ref, wkv_ref, wo_ref, cgain_ref,
    resid_ref, act_ref, keys_ref, values_ref,
):
    @pl.when(pl.program_id(0) == 0)
    def _():
        normed_all = scaled(whole_ref[...], again_ref[...]).astype(jnp.bfloat16)
        both = jnp.dot(
            normed_all, wkv_ref[...], preferred_element_type=jnp.float32
        ).astype(jnp.bfloat16)
        width = keys_ref.shape[1]
        keys_ref[...] = both[:, :width]
        values_ref[...] = both[:, width:]

    scores = (
        lax.dot_general(
            query_ref[...], keys_ref[...], (((1,), (1,)), ((), ())),
            preferred_element_type=jnp.float32,
        )
        * scale
    )
    peak = jnp.max(scores, axis=1, keepdims=True)
    weights = jnp.exp(scores - peak)
    total = jnp.sum(weights, axis=1, keepdims=True)
    summed = jnp.dot(
        weights.astype(jnp.bfloat16), values_ref[...], preferred_element_type=jnp.float32
    )
    attended = (summed / total).astype(jnp.bfloat16)
    resid = (
        flat_ref[...].astype(jnp.float32)
        + jnp.dot(attended, wo_ref[...], preferred_element_type=jnp.float32)
    ).astype(jnp.bfloat16)
    resid_ref[...] = resid
    shown = scaled(resid, cgain_ref[...])
    act_ref[...] = (shown / (1.0 + jnp.exp(-shown))).astype(jnp.bfloat16)


def attend(whole, flat, query, attn_gain, key_weight, value_weight, out_weight, conv_gain, scale):
    count, width = query.shape
    total_keys = whole.shape[0]
    block = 160 if count % 160 == 0 and count * total_keys > 2 ** 21 else count
    full = lambda shape: pl.BlockSpec(shape, lambda i: (0, 0))
    rows_of = pl.BlockSpec((block, width), lambda i: (i, 0))
    flops = 4 * count * total_keys * width + 4 * total_keys * width * width
    flops += 2 * count * width * width
    return pl.pallas_call(
        functools.partial(attention_kernel, scale),
        out_shape=(
            jax.ShapeDtypeStruct((count, width), jnp.bfloat16),
            jax.ShapeDtypeStruct((count, width), jnp.bfloat16),
        ),
        grid=(count // block,),
        in_specs=[
            full((total_keys, width)),
            rows_of,
            rows_of,
            full((1, width)),
            full((width, 2 * width)),
            full((width, width)),
            full((1, width)),
        ],
        out_specs=(rows_of, rows_of),
        scratch_shapes=[
            pltpu.VMEM((total_keys, width), jnp.bfloat16),
            pltpu.VMEM((total_keys, width), jnp.bfloat16),
        ],
        compiler_params=pltpu.CompilerParams(vmem_limit_bytes=60 * 1024 * 1024),
        cost_estimate=pl.CostEstimate(
            flops=flops,
            transcendentals=count * total_keys + count * width,
            bytes_accessed=2 * width * (total_keys + 4 * count + 3 * width),
        ),
    )(
        whole, flat, query, attn_gain.reshape(1, width),
        jnp.concatenate([key_weight, value_weight], axis=1), out_weight,
        conv_gain.reshape(1, width),
    )


def split_kernels_a(scale, count, parts, me_ref, *refs):
    blocks = refs[:count]
    query_ref, again_ref, wkv_ref, m_ref, l_ref, o_ref, kv_ref = refs[count:]
    width = query_ref.shape[1]
    rows = blocks[0].shape[0]
    for index, block_ref in enumerate(blocks):
        normed = scaled(block_ref[...], again_ref[...]).astype(jnp.bfloat16)
        kv_ref[index * rows : (index + 1) * rows, :] = jnp.dot(
            normed, wkv_ref[...], preferred_element_type=jnp.float32
        ).astype(jnp.bfloat16)
    both = kv_ref[...]
    scores = (
        lax.dot_general(
            query_ref[...], both[:, :width], (((1,), (1,)), ((), ())),
            preferred_element_type=jnp.float32,
        )
        * scale
    )
    me = me_ref[0]
    column = lax.broadcasted_iota(jnp.int32, scores.shape, 1)
    second = (column >= rows) & (column < 2 * rows)
    third = (column >= 2 * rows) & (column < 3 * rows)
    hidden = (second & (me < 1)) | (third & (me > parts - 2))
    scores = jnp.where(hidden, -1e30, scores)
    peak = jnp.max(scores, axis=1, keepdims=True)
    weights = jnp.exp(scores - peak)
    m_ref[...] = peak
    l_ref[...] = jnp.sum(weights, axis=1, keepdims=True)
    o_ref[...] = jnp.dot(
        weights.astype(jnp.bfloat16), both[:, width:], preferred_element_type=jnp.float32
    )


def split_kernels_b(
    scale, parts, me_ref, up_ref, down_ref, query_ref, again_ref, wkv_ref, m_ref, l_ref, o_ref,
    flat_ref, wo_ref, cgain_ref, resid_ref, act_ref,
):
    width = query_ref.shape[1]
    me = me_ref[0]
    block = jnp.where(me == parts - 1, up_ref[...], down_ref[...])
    normed = scaled(block, again_ref[...]).astype(jnp.bfloat16)
    both = jnp.dot(normed, wkv_ref[...], preferred_element_type=jnp.float32).astype(jnp.bfloat16)
    scores = (
        lax.dot_general(
            query_ref[...], both[:, :width], (((1,), (1,)), ((), ())),
            preferred_element_type=jnp.float32,
        )
        * scale
    )
    scores = jnp.where((me == 0) | (me == parts - 1), scores, -1e30)
    earlier = m_ref[...]
    peak = jnp.maximum(jnp.max(scores, axis=1, keepdims=True), earlier)
    alpha = jnp.exp(earlier - peak)
    weights = jnp.exp(scores - peak)
    total = l_ref[...] * alpha + jnp.sum(weights, axis=1, keepdims=True)
    summed = o_ref[...] * alpha + jnp.dot(
        weights.astype(jnp.bfloat16), both[:, width:], preferred_element_type=jnp.float32
    )
    attended = (summed / total).astype(jnp.bfloat16)
    resid = (
        flat_ref[...].astype(jnp.float32)
        + jnp.dot(attended, wo_ref[...], preferred_element_type=jnp.float32)
    ).astype(jnp.bfloat16)
    resid_ref[...] = resid
    shown = scaled(resid, cgain_ref[...])
    act_ref[...] = (shown / (1.0 + jnp.exp(-shown))).astype(jnp.bfloat16)


def whole_call(kernel, me, inputs, outputs, flops, transcendentals, scratch=()):
    return pl.pallas_call(
        kernel,
        out_shape=outputs,
        grid_spec=pltpu.PrefetchScalarGridSpec(
            num_scalar_prefetch=1,
            grid=(1,),
            in_specs=[pl.BlockSpec(x.shape, lambda i, me: (0, 0)) for x in inputs],
            out_specs=tuple(pl.BlockSpec(o.shape, lambda i, me: (0, 0)) for o in outputs),
            scratch_shapes=list(scratch),
        ),
        compiler_params=pltpu.CompilerParams(vmem_limit_bytes=24 * 1024 * 1024),
        cost_estimate=pl.CostEstimate(
            flops=flops,
            transcendentals=transcendentals,
            bytes_accessed=sum(x.size * x.dtype.itemsize for x in inputs),
        ),
    )(me, *inputs)


def split_attend(
    me, parts, blocks_a, up_b, down_b, flat, query, attn_gain, key_weight, value_weight,
    out_weight, conv_gain, scale,
):
    count, width = query.shape
    wkv = jnp.concatenate([key_weight, value_weight], axis=1)
    again = attn_gain.reshape(1, width)
    f32 = jnp.float32
    keys_a, keys_b = count * len(blocks_a), count
    m_a, l_a, o_a = whole_call(
        functools.partial(split_kernels_a, scale, len(blocks_a), parts),
        me,
        list(blocks_a) + [query, again, wkv],
        (
            jax.ShapeDtypeStruct((count, 1), f32),
            jax.ShapeDtypeStruct((count, 1), f32),
            jax.ShapeDtypeStruct((count, width), f32),
        ),
        4 * keys_a * width * width + 4 * count * keys_a * width,
        count * keys_a,
        [pltpu.VMEM((keys_a, 2 * width), jnp.bfloat16)],
    )
    return whole_call(
        functools.partial(split_kernels_b, scale, parts),
        me,
        [up_b, down_b, query, again, wkv, m_a, l_a, o_a, flat, out_weight,
         conv_gain.reshape(1, width)],
        (
            jax.ShapeDtypeStruct((count, width), jnp.bfloat16),
            jax.ShapeDtypeStruct((count, width), jnp.bfloat16),
        ),
        4 * keys_b * width * width + 4 * count * keys_b * width + 2 * count * width * width,
        count * keys_b + count * width,
    )


def shards(
    frames,
    cache_frames,
    attn_gain,
    query_weight,
    key_weight,
    value_weight,
    out_weight,
    conv_gain,
    conv_weight,
):
    rows = frames.shape[1]
    cols = frames.shape[2]
    width = frames.shape[3]
    flat = frames.reshape(-1, width)
    count = flat.shape[0]
    scale = float(np.float32(1.0) / np.sqrt(np.float32(width)))
    n = lax.axis_size("strip")
    split_path = n == 4
    if not split_path:
        whole = strip_gather(flat, "strip")
    normed = rms_scale(flat, attn_gain).astype(jnp.bfloat16)
    query = jnp.dot(normed, query_weight, preferred_element_type=jnp.float32).astype(jnp.bfloat16)
    if split_path:
        me = lax.axis_index("strip")
        ups, downs = relay(flat, "strip")
        far = jnp.where(me <= 1, downs[1], ups[1])
        resid, act = split_attend(
            me.astype(jnp.int32).reshape(1), n, [flat, ups[0], downs[0], far], ups[n - 2],
            downs[n - 2], flat, query, attn_gain, key_weight, value_weight, out_weight,
            conv_gain, scale,
        )
    else:
        resid, act = attend(
            whole, flat, query, attn_gain, key_weight, value_weight, out_weight, conv_gain, scale
        )
    act = act.reshape(rows, cols, width)
    frame_index = lax.axis_index("tm")
    prior = passed_along(act, "tm", 1)
    prior = jnp.where(frame_index == 0, cache_frames[1], prior)
    older = passed_along(prior, "tm", 1)
    older = jnp.where(frame_index == 0, cache_frames[0], older)
    kernel = conv_weight.reshape(3, 3, 3 * width, width)

    def widen(frame):
        padded = jnp.pad(frame, ((1, 1), (1, 1), (0, 0)))
        return jnp.concatenate(
            [padded[:, 0:cols], padded[:, 1 : cols + 1], padded[:, 2 : cols + 2]], axis=-1
        )

    def frame_terms(wide, step_t):
        main = None
        for step_r in range(3):
            window = wide[step_r : step_r + rows].reshape(-1, 3 * width)
            part = jnp.dot(window, kernel[step_t, step_r], preferred_element_type=jnp.float32)
            main = part if main is None else main + part
        first = jnp.dot(wide[1], kernel[step_t, 2], preferred_element_type=jnp.float32)
        last = jnp.dot(wide[rows], kernel[step_t, 0], preferred_element_type=jnp.float32)
        return main, first, last

    own_main, own_first, own_last = frame_terms(widen(act), 2)
    prior_main, prior_first, prior_last = frame_terms(widen(prior), 1)
    older_main, older_first, older_last = frame_terms(widen(older), 0)
    to_prev = own_first + prior_first + older_first
    to_next = own_last + prior_last + older_last
    n = lax.axis_size("strip")
    from_next = lax.ppermute(
        to_prev.astype(jnp.bfloat16), "strip", [(i + 1, i) for i in range(n - 1)]
    )
    from_prev = lax.ppermute(
        to_next.astype(jnp.bfloat16), "strip", [(i, i + 1) for i in range(n - 1)]
    )
    result = resid.astype(jnp.float32) + own_main + prior_main + older_main
    result = result.reshape(rows, cols, width)
    result = result.at[0].add(from_prev.astype(jnp.float32))
    result = result.at[rows - 1].add(from_next.astype(jnp.float32))
    return result.astype(jnp.bfloat16).reshape(1, rows, cols, width)


def solution(mesh):
    return jax.shard_map(
        shards,
        mesh=mesh,
        in_specs=(
            P(("clip", "tm"), "strip", None, None),
            P("clip", "strip", None, None),
            P(),
            P(),
            P(),
            P(),
            P(),
            P(),
            P(),
        ),
        out_specs=P(("clip", "tm"), "strip", None, None),
        check_vma=False,
    )
```
